32 devices in a mesh: grp: 2 (over x), seg: 16 (over z, y, core).
Axes of the slice: x: 2, y: 2, z: 4, core: 2. Of those that a mesh axis runs over, the one named last changes fastest.
Arguments:
- strain: float32 [2097152], P(('grp', 'seg')), parts along dimension 0, may hold values from -6 to 6
- gate_mask: int32 [2097152], P(('grp', 'seg')), parts along dimension 0, may hold values 0 or 1
- template_bank: bfloat16 [32, 2, 32768], P('grp', None, 'seg'), parts along dimension 0, may hold values from -6 to 6
Outputs:
- peak_power: float32 [16, 8192], P(None, ('grp', 'seg')), parts along dimension 1
The draws below stay inside these ranges and needn't reach their ends.
There are 2 independent parts, one for each index of `grp`. The reference program is written for one: setup_inputs(seed, part) draws one part's arguments, and reference() takes and returns one part's arrays. A program takes and returns all parts, laid end to end along the dimension named above; each array names one. Nothing has to cross between parts.
All inputs are finite; a program needn't handle non-finite values. No bound on the sum of `gate_mask` on one device may be relied on, other than what follows from the above.
Results may differ from the reference program's by a relative error of at most 0.0003.
Values may be sent and summed in bfloat16 or wider, within the bound.
No kernel may reach another device: no remote copies, remote signals or barrier semaphores. Data moves between devices by JAX's collectives and lax.ppermute only.
A program may use at most 128 MiB of HBM per device.

```python
import jax
import jax.numpy as jnp
from jax import lax

RADIX = 256
NFFT = 65536
BLOCK = 32768
TEMPLATES = 16
SAMPLES = 1048576


def place_ends(result, rng, least, largest):
    shape = result.shape
    index_at = [jax.random.randint(jax.random.fold_in(rng, axis), (), 0, shape[axis]) for axis in range(len(shape))]
    result = result.at[tuple(index_at)].set(least)
    longest = shape.index(max(shape))
    index_at[longest] = (index_at[longest] + 1) % shape[longest]
    return result.at[tuple(index_at)].set(largest)


def block_scale(rng, extent, cuts, low, largest):
    gain, own = 1.0, jax.random.fold_in(rng, 6)
    for dim, blocks in cuts:
        draws = jnp.exp(jax.random.uniform(jax.random.fold_in(own, dim), (blocks,), jnp.float32, low / len(cuts), largest / len(cuts)))
        gain = gain * jnp.repeat(draws, extent[dim] // blocks).reshape([-1 if axis == dim else 1 for axis in range(len(extent))])
    return gain


def normal_values(rng, extent, width, bound, split=(), kind=jnp.bfloat16):
    level = block_scale(rng, extent, split, -0.22, 0.18) if split else 1.0
    result = jax.random.normal(rng, extent, jnp.float32) * width * level
    return jnp.minimum(jnp.maximum(result, -bound), bound).astype(kind)


def setup_inputs(seed: int = 0, part: int = 0) -> dict:
    streams_of = jax.random.split(jax.random.key(seed), 4)
    part_keys = jax.random.split(jax.random.fold_in(streams_of[3], part), 4)
    strain = normal_values(part_keys[0], (SAMPLES,), 1.0, 6.0, ((0, 16),), jnp.float32)
    gate_mask = place_ends((jax.random.randint(part_keys[1], (SAMPLES,), 0, 16) < 15).astype(jnp.int32), jax.random.fold_in(part_keys[1], 1), 0, 1)
    template_bank = normal_values(part_keys[2], (TEMPLATES, 2, BLOCK), 1.0, 6.0, ((2, 16),))
    return {"strain": strain, "gate_mask": gate_mask, "template_bank": template_bank}


EPSILON = 1e-06

def reference(strain, gate_mask, template_bank):
    gated = strain * gate_mask.astype(jnp.float32)
    blocks = gated.reshape(-1, BLOCK)
    spectra = jnp.fft.rfft(blocks, n=NFFT, axis=-1)[:, :BLOCK]
    waveform = template_bank.astype(jnp.float32)

    def one_template(row_pair):
        real_part = row_pair[0]
        imag_part = row_pair[1]
        power_sum = jnp.sum(real_part * real_part + imag_part * imag_part)
        norm_scale = 1.0 / jnp.sqrt(BLOCK * power_sum + EPSILON)
        product = spectra * (real_part - 1j * imag_part)[None, :]
        series = jnp.fft.ifft(product, n=NFFT, axis=-1) * NFFT * norm_scale
        carried = jnp.concatenate([jnp.zeros_like(series[:1, BLOCK:]), series[:-1, BLOCK:]], axis=0)
        summed = series[:, :BLOCK] + carried
        power_series = summed.real * summed.real + summed.imag * summed.imag
        return lax.optimization_barrier(jnp.max(power_series.reshape(-1, BLOCK // RADIX, RADIX), axis=-1)).reshape(-1)
    return lax.map(one_template, waveform)
```

```python
import math

import jax
import jax.numpy as jnp
from jax import lax
from jax.sharding import PartitionSpec as P

RADIX = 256
BLOCK = 32768
SUBBANK = 8


PRECISE = lax.Precision.HIGH
EPSILON = 1e-06


def passed_along(value, axis, by):
    count = lax.axis_size(axis)
    pairs = [(i, i + by) for i in range(count) if 0 <= i + by < count]
    return lax.ppermute(value, axis, pairs)


def angle_table(row_count, col_count, period):
    row_index = lax.broadcasted_iota(jnp.int32, (row_count, col_count), 0)
    col_index = lax.broadcasted_iota(jnp.int32, (row_count, col_count), 1)
    phase_step = row_index * col_index % period
    angle_value = phase_step.astype(jnp.float32) * (2.0 * math.pi / period)
    return (jnp.cos(angle_value), jnp.sin(angle_value))


def forward(windows):
    half_radix = RADIX // 2
    window_total = windows.shape[0]
    rows = windows.shape[1] // RADIX
    block_grid = windows.reshape(window_total, rows, RADIX)
    cos_first, sin_first = angle_table(rows, RADIX, RADIX)
    first_table = jnp.concatenate([cos_first, -sin_first], axis=1)
    first_section = jnp.einsum("bnm,nf->bmf", block_grid, first_table, precision=PRECISE)
    cos_twist, sin_twist = angle_table(RADIX, RADIX, RADIX * RADIX)
    real_part = first_section[..., :RADIX]
    imag_part = first_section[..., RADIX:]
    turned = jnp.concatenate(
        [
            real_part * cos_twist + imag_part * sin_twist,
            imag_part * cos_twist - real_part * sin_twist,
        ],
        axis=-1,
    )
    cos_second, sin_second = angle_table(RADIX, half_radix, RADIX)
    cosine_part = jnp.einsum("bnf,nk->bkf", turned, cos_second, precision=PRECISE)
    sine_part = jnp.einsum("bnf,nk->bkf", turned, sin_second, precision=PRECISE)
    return jnp.concatenate(
        [
            cosine_part[..., :RADIX] + sine_part[..., RADIX:],
            cosine_part[..., RADIX:] - sine_part[..., :RADIX],
        ],
        axis=-1,
    )


def output_table():
    half_radix = RADIX // 2
    cos_out, sin_out = angle_table(RADIX, RADIX, RADIX)
    real_cols = jnp.concatenate([cos_out, -sin_out], axis=0)
    imag_cols = jnp.concatenate([sin_out, cos_out], axis=0)
    return jnp.concatenate([real_cols[:, half_radix:], imag_cols[:, half_radix:]], axis=1)


def inverse_peaks(flat_rows, out_table):
    half_radix = RADIX // 2
    k_rows = flat_rows.shape[1]
    cos_first, sin_first = angle_table(k_rows, RADIX, RADIX)
    cosine_part = jnp.einsum("rkf,kt->rtf", flat_rows, cos_first, precision=PRECISE)
    sine_part = jnp.einsum("rkf,kt->rtf", flat_rows, sin_first, precision=PRECISE)
    real_part = cosine_part[..., :RADIX] - sine_part[..., RADIX:]
    imag_part = sine_part[..., :RADIX] + cosine_part[..., RADIX:]
    cos_twist, sin_twist = angle_table(RADIX, RADIX, RADIX * RADIX)
    turned = jnp.concatenate(
        [
            real_part * cos_twist - imag_part * sin_twist,
            real_part * sin_twist + imag_part * cos_twist,
        ],
        axis=-1,
    )
    series = jnp.einsum("rtf,fu->rtu", turned, out_table, precision=PRECISE)
    power_series = (
        series[..., :half_radix] * series[..., :half_radix]
        + series[..., half_radix:] * series[..., half_radix:]
    )
    return jnp.max(power_series, axis=1)


def gathered_bank(bank_rows):
    seg_total = lax.axis_size("seg")
    rows, parts, local_bins = bank_rows.shape
    flat = bank_rows.reshape(1, rows * parts * local_bins)
    every = lax.all_gather(flat, "seg", axis=0, tiled=True)
    every = every.reshape(seg_total, rows, parts, local_bins // RADIX, RADIX)
    every = jnp.transpose(every, (1, 2, 0, 3, 4))
    return every.reshape(rows, parts, seg_total * local_bins // RADIX, RADIX)


def local(strain, gate_mask, template_bank):
    gated = strain * gate_mask.astype(jnp.float32)
    local_blocks = gated.reshape(-1, BLOCK)
    block_total = local_blocks.shape[0]
    earlier = passed_along(local_blocks[block_total - 1], "seg", 1)
    before = jnp.concatenate([earlier[None], local_blocks[:-1]], axis=0)
    windows = jnp.concatenate([before, local_blocks], axis=1)
    spectra = forward(windows)
    spec_real = spectra[..., :RADIX]
    spec_imag = spectra[..., RADIX:]
    out_table = output_table()
    template_total = template_bank.shape[0]
    results = []
    for start in range(0, template_total, SUBBANK):
        wave = gathered_bank(template_bank[start : start + SUBBANK]).astype(jnp.float32)
        wave_real = wave[:, 0][:, None]
        wave_imag = wave[:, 1][:, None]
        power_sum = jnp.sum(wave_real * wave_real + wave_imag * wave_imag, axis=(1, 2, 3))
        norm_scale = (1.0 / jnp.sqrt(BLOCK * power_sum + EPSILON))[:, None, None, None]
        prod_real = (spec_real[None] * wave_real + spec_imag[None] * wave_imag) * norm_scale
        prod_imag = (spec_imag[None] * wave_real - spec_real[None] * wave_imag) * norm_scale
        flat_rows = jnp.concatenate([prod_real, prod_imag], axis=-1)
        sub_total = flat_rows.shape[0]
        flat_rows = flat_rows.reshape(sub_total * block_total, flat_rows.shape[2], 2 * RADIX)
        peaks = inverse_peaks(flat_rows, out_table)
        results.append(peaks.reshape(sub_total, block_total * (RADIX // 2)))
    return jnp.concatenate(results, axis=0)


def solution(mesh):
    in_specs = (P(("grp", "seg")), P(("grp", "seg")), P("grp", None, "seg"))
    out_specs = P(None, ("grp", "seg"))
    return jax.shard_map(local, mesh=mesh, in_specs=in_specs, out_specs=out_specs, check_vma=False)
```

```python
import math

import jax
import jax.numpy as jnp
from jax import lax
from jax.experimental import pallas as pl
from jax.experimental.pallas import tpu as pltpu
from jax.sharding import PartitionSpec as P

RADIX = 256
BLOCK = 32768
SUBBANK = 16


PRECISE = lax.Precision.HIGH
EPSILON = 1e-06


def passed_along(value, axis, by):
    count = lax.axis_size(axis)
    pairs = [(i, i + by) for i in range(count) if 0 <= i + by < count]
    return lax.ppermute(value, axis, pairs)


def angle_table(row_count, col_count, period):
    row_index = lax.broadcasted_iota(jnp.int32, (row_count, col_count), 0)
    col_index = lax.broadcasted_iota(jnp.int32, (row_count, col_count), 1)
    phase_step = row_index * col_index % period
    angle_value = phase_step.astype(jnp.float32) * (2.0 * math.pi / period)
    return (jnp.cos(angle_value), jnp.sin(angle_value))


def forward(windows):
    half_radix = RADIX // 2
    window_total = windows.shape[0]
    rows = windows.shape[1] // RADIX
    block_grid = windows.reshape(window_total, rows, RADIX)
    cos_first, sin_first = angle_table(rows, RADIX, RADIX)
    first_table = jnp.concatenate([cos_first, -sin_first], axis=1)
    first_section = jnp.einsum("bnm,nf->bmf", block_grid, first_table, precision=PRECISE)
    cos_twist, sin_twist = angle_table(RADIX, RADIX, RADIX * RADIX)
    real_part = first_section[..., :RADIX]
    imag_part = first_section[..., RADIX:]
    turned = jnp.concatenate(
        [
            real_part * cos_twist + imag_part * sin_twist,
            imag_part * cos_twist - real_part * sin_twist,
        ],
        axis=-1,
    )
    cos_second, sin_second = angle_table(RADIX, half_radix, RADIX)
    cosine_part = jnp.einsum("bnf,nk->bkf", turned, cos_second, precision=PRECISE)
    sine_part = jnp.einsum("bnf,nk->bkf", turned, sin_second, precision=PRECISE)
    return jnp.concatenate(
        [
            cosine_part[..., :RADIX] + sine_part[..., RADIX:],
            cosine_part[..., RADIX:] - sine_part[..., :RADIX],
        ],
        axis=-1,
    )


def split_pair(value):
    high = value.astype(jnp.bfloat16)
    low = (value - high.astype(jnp.float32)).astype(jnp.bfloat16)
    return high, low


def table_pair(value):
    high = lax.reduce_precision(value, exponent_bits=8, mantissa_bits=7)
    return high.astype(jnp.bfloat16), (value - high).astype(jnp.bfloat16)


def triple_dot(left_high, left_low, right_high, right_low):
    total = jnp.dot(left_high, right_high, preferred_element_type=jnp.float32)
    total = total + jnp.dot(left_high, right_low, preferred_element_type=jnp.float32)
    return total + jnp.dot(left_low, right_high, preferred_element_type=jnp.float32)


def inverse_tables(k_rows):
    half_radix = RADIX // 2
    cos_first, sin_first = angle_table(RADIX, k_rows, RADIX)
    first = jnp.concatenate(
        [
            jnp.concatenate([cos_first, -sin_first], axis=1),
            jnp.concatenate([sin_first, cos_first], axis=1),
        ],
        axis=0,
    )
    cos_twist, sin_twist = angle_table(RADIX, RADIX, RADIX * RADIX)
    cos_out, sin_out = angle_table(RADIX, RADIX, RADIX)
    real_cols = jnp.concatenate([cos_out, -sin_out], axis=0)
    imag_cols = jnp.concatenate([sin_out, cos_out], axis=0)
    second = jnp.concatenate([real_cols[:, half_radix:], imag_cols[:, half_radix:]], axis=1)
    first_high, first_low = table_pair(first)
    second_high, second_low = table_pair(second)
    return first_high, first_low, cos_twist, sin_twist, second_high, second_low


def peaks_kernel(spec_ref, bank_ref, fh_ref, fl_ref, tc_ref, ts_ref, sh_ref, sl_ref, out_ref):
    half_radix = RADIX // 2
    wave_real = bank_ref[0, 0].astype(jnp.float32)
    wave_imag = bank_ref[0, 1].astype(jnp.float32)
    for block in range(spec_ref.shape[0]):
        spec_real = spec_ref[block, :, :RADIX]
        spec_imag = spec_ref[block, :, RADIX:]
        prod_real = spec_real * wave_real + spec_imag * wave_imag
        prod_imag = spec_imag * wave_real - spec_real * wave_imag
        stacked = jnp.concatenate([prod_real, prod_imag], axis=0)
        stacked_high, stacked_low = split_pair(stacked)
        first = triple_dot(fh_ref[...], fl_ref[...], stacked_high, stacked_low)
        real_part = first[:RADIX]
        imag_part = first[RADIX:]
        cos_twist = tc_ref[...]
        sin_twist = ts_ref[...]
        turned = jnp.concatenate(
            [
                real_part * cos_twist - imag_part * sin_twist,
                real_part * sin_twist + imag_part * cos_twist,
            ],
            axis=1,
        )
        turned_high, turned_low = split_pair(turned)
        series = triple_dot(turned_high, turned_low, sh_ref[...], sl_ref[...])
        power_series = (
            series[:, :half_radix] * series[:, :half_radix]
            + series[:, half_radix:] * series[:, half_radix:]
        )
        out_ref[0, block : block + 1, :] = jnp.max(power_series, axis=0, keepdims=True)


def window_peaks(spectra, bank, tables):
    block_total, k_rows, _ = spectra.shape
    template_total = bank.shape[0]
    fixed = lambda k: (0, 0)
    pair_flops = 6 * (2 * RADIX) * (2 * k_rows) * RADIX + 6 * RADIX * (2 * RADIX) * RADIX
    return pl.pallas_call(
        peaks_kernel,
        out_shape=jax.ShapeDtypeStruct((template_total, block_total, RADIX // 2), jnp.float32),
        grid=(template_total,),
        in_specs=[
            pl.BlockSpec((block_total, k_rows, 2 * RADIX), lambda k: (0, 0, 0)),
            pl.BlockSpec((1, 2, k_rows, RADIX), lambda k: (k, 0, 0, 0)),
            pl.BlockSpec((2 * RADIX, 2 * k_rows), fixed),
            pl.BlockSpec((2 * RADIX, 2 * k_rows), fixed),
            pl.BlockSpec((RADIX, RADIX), fixed),
            pl.BlockSpec((RADIX, RADIX), fixed),
            pl.BlockSpec((2 * RADIX, RADIX), fixed),
            pl.BlockSpec((2 * RADIX, RADIX), fixed),
        ],
        out_specs=pl.BlockSpec((1, block_total, RADIX // 2), lambda k: (k, 0, 0)),
        compiler_params=pltpu.CompilerParams(dimension_semantics=("arbitrary",)),
        cost_estimate=pl.CostEstimate(
            flops=pair_flops * template_total * block_total,
            transcendentals=0,
            bytes_accessed=spectra.size * 4 + bank.size * 2 + template_total * block_total * RADIX * 2,
        ),
    )(spectra, bank, *tables)


def gathered_bank(bank_rows):
    seg_total = lax.axis_size("seg")
    me = lax.axis_index("seg")
    rows, parts, local_bins = bank_rows.shape
    held = bank_rows[None]
    distance = seg_total // 2
    steps = 0
    while distance >= 1:
        pairs = [(i, i ^ distance) for i in range(seg_total)]
        arrived = lax.ppermute(held, "seg", pairs)
        upper = (me & distance) != 0
        held = jnp.stack([jnp.where(upper, arrived, held), jnp.where(upper, held, arrived)], axis=0)
        distance //= 2
        steps += 1
    held = held.reshape((2,) * steps + (rows, parts, local_bins // RADIX, RADIX))
    order = tuple(reversed(range(steps)))
    held = jnp.transpose(held, (steps, steps + 1) + order + (steps + 2, steps + 3))
    return held.reshape(rows, parts, seg_total * local_bins // RADIX, RADIX)


def local(strain, gate_mask, template_bank):
    gated = strain * gate_mask.astype(jnp.float32)
    local_blocks = gated.reshape(-1, BLOCK)
    block_total = local_blocks.shape[0]
    earlier = passed_along(local_blocks[block_total - 1], "seg", 1)
    before = jnp.concatenate([earlier[None], local_blocks[:-1]], axis=0)
    windows = jnp.concatenate([before, local_blocks], axis=1)
    spectra = forward(windows)
    wide_bank = template_bank.astype(jnp.float32)
    power_sum = lax.psum(jnp.sum(wide_bank * wide_bank, axis=(1, 2)), "seg")
    norm_scale = 1.0 / jnp.sqrt(BLOCK * power_sum + EPSILON)
    tables = inverse_tables(spectra.shape[1])
    template_total = template_bank.shape[0]
    results = []
    for start in range(0, template_total, SUBBANK):
        bank = gathered_bank(template_bank[start : start + SUBBANK])
        peaks = window_peaks(spectra, bank, tables)
        results.append(peaks.reshape(bank.shape[0], block_total * (RADIX // 2)))
    peaks = jnp.concatenate(results, axis=0)
    return peaks * (norm_scale * norm_scale)[:, None]


def solution(mesh):
    in_specs = (P(("grp", "seg")), P(("grp", "seg")), P("grp", None, "seg"))
    out_specs = P(None, ("grp", "seg"))
    return jax.shard_map(local, mesh=mesh, in_specs=in_specs, out_specs=out_specs, check_vma=False)
```

```python
import math

import jax
import jax.numpy as jnp
from jax import lax
from jax.experimental import pallas as pl
from jax.experimental.pallas import tpu as pltpu
from jax.sharding import PartitionSpec as P

RADIX = 256
BLOCK = 32768
SUBBANK = 16


PRECISE = lax.Precision.HIGH
EPSILON = 1e-06


def passed_along(value, axis, by):
    count = lax.axis_size(axis)
    pairs = [(i, i + by) for i in range(count) if 0 <= i + by < count]
    return lax.ppermute(value, axis, pairs)


def angle_table(row_count, col_count, period):
    row_index = lax.broadcasted_iota(jnp.int32, (row_count, col_count), 0)
    col_index = lax.broadcasted_iota(jnp.int32, (row_count, col_count), 1)
    phase_step = row_index * col_index % period
    angle_value = phase_step.astype(jnp.float32) * (2.0 * math.pi / period)
    return (jnp.cos(angle_value), jnp.sin(angle_value))


def forward(windows):
    half_radix = RADIX // 2
    window_total = windows.shape[0]
    rows = windows.shape[1] // RADIX
    block_grid = windows.reshape(window_total, rows, RADIX)
    cos_first, sin_first = angle_table(rows, RADIX, RADIX)
    first_table = jnp.concatenate([cos_first, -sin_first], axis=1)
    first_section = jnp.einsum("bnm,nf->bmf", block_grid, first_table, precision=PRECISE)
    cos_twist, sin_twist = angle_table(RADIX, RADIX, RADIX * RADIX)
    real_part = first_section[..., :RADIX]
    imag_part = first_section[..., RADIX:]
    turned = jnp.concatenate(
        [
            real_part * cos_twist + imag_part * sin_twist,
            imag_part * cos_twist - real_part * sin_twist,
        ],
        axis=-1,
    )
    cos_second, sin_second = angle_table(RADIX, half_radix, RADIX)
    cosine_part = jnp.einsum("bnf,nk->bkf", turned, cos_second, precision=PRECISE)
    sine_part = jnp.einsum("bnf,nk->bkf", turned, sin_second, precision=PRECISE)
    return jnp.concatenate(
        [
            cosine_part[..., :RADIX] + sine_part[..., RADIX:],
            cosine_part[..., RADIX:] - sine_part[..., :RADIX],
        ],
        axis=-1,
    )


def split_pair(value):
    high = value.astype(jnp.bfloat16)
    low = (value - high.astype(jnp.float32)).astype(jnp.bfloat16)
    return high, low


def table_pair(value):
    high = lax.reduce_precision(value, exponent_bits=8, mantissa_bits=7)
    return high.astype(jnp.bfloat16), (value - high).astype(jnp.bfloat16)


def triple_dot(left_high, left_low, right_high, right_low):
    total = jnp.dot(left_high, right_high, preferred_element_type=jnp.float32)
    total = total + jnp.dot(left_high, right_low, preferred_element_type=jnp.float32)
    return total + jnp.dot(left_low, right_high, preferred_element_type=jnp.float32)


def inverse_tables(k_rows):
    half_radix = RADIX // 2
    cos_first, sin_first = angle_table(RADIX, k_rows, RADIX)
    first = jnp.concatenate(
        [
            jnp.concatenate([cos_first, -sin_first], axis=1),
            jnp.concatenate([sin_first, cos_first], axis=1),
        ],
        axis=0,
    )
    cos_twist, sin_twist = angle_table(RADIX, RADIX, RADIX * RADIX)
    cos_out, sin_out = angle_table(RADIX, RADIX, RADIX)
    real_cols = jnp.concatenate([cos_out, -sin_out], axis=0)
    imag_cols = jnp.concatenate([sin_out, cos_out], axis=0)
    second = jnp.concatenate([real_cols[:, half_radix:], imag_cols[:, half_radix:]], axis=1)
    first_high, first_low = table_pair(first)
    second_high, second_low = table_pair(second)
    return first_high, first_low, cos_twist, sin_twist, second_high, second_low


def peaks_kernel(spec_ref, bank_ref, fh_ref, fl_ref, tc_ref, ts_ref, sh_ref, sl_ref, out_ref):
    half_radix = RADIX // 2
    wave_real = bank_ref[0, 0].astype(jnp.float32)
    wave_imag = bank_ref[0, 1].astype(jnp.float32)
    power_sum = jnp.sum(wave_real * wave_real + wave_imag * wave_imag, keepdims=True)
    norm_scale = 1.0 / jnp.sqrt(BLOCK * power_sum + EPSILON)
    for block in range(spec_ref.shape[0]):
        spec_real = spec_ref[block, :, :RADIX]
        spec_imag = spec_ref[block, :, RADIX:]
        prod_real = spec_real * wave_real + spec_imag * wave_imag
        prod_imag = spec_imag * wave_real - spec_real * wave_imag
        stacked = jnp.concatenate([prod_real, prod_imag], axis=0)
        stacked_high, stacked_low = split_pair(stacked)
        first = triple_dot(fh_ref[...], fl_ref[...], stacked_high, stacked_low)
        real_part = first[:RADIX]
        imag_part = first[RADIX:]
        cos_twist = tc_ref[...]
        sin_twist = ts_ref[...]
        turned = jnp.concatenate(
            [
                real_part * cos_twist - imag_part * sin_twist,
                real_part * sin_twist + imag_part * cos_twist,
            ],
            axis=1,
        )
        turned_high, turned_low = split_pair(turned)
        series = triple_dot(turned_high, turned_low, sh_ref[...], sl_ref[...])
        power_series = (
            series[:, :half_radix] * series[:, :half_radix]
            + series[:, half_radix:] * series[:, half_radix:]
        )
        peak = jnp.max(power_series, axis=0, keepdims=True)
        out_ref[0, block : block + 1, :] = peak * (norm_scale * norm_scale)


def window_peaks(spectra, bank, tables):
    block_total, k_rows, _ = spectra.shape
    template_total = bank.shape[0]
    fixed = lambda k: (0, 0)
    pair_flops = 6 * (2 * RADIX) * (2 * k_rows) * RADIX + 6 * RADIX * (2 * RADIX) * RADIX
    return pl.pallas_call(
        peaks_kernel,
        out_shape=jax.ShapeDtypeStruct((template_total, block_total, RADIX // 2), jnp.float32),
        grid=(template_total,),
        in_specs=[
            pl.BlockSpec((block_total, k_rows, 2 * RADIX), lambda k: (0, 0, 0)),
            pl.BlockSpec((1, 2, k_rows, RADIX), lambda k: (k, 0, 0, 0)),
            pl.BlockSpec((2 * RADIX, 2 * k_rows), fixed),
            pl.BlockSpec((2 * RADIX, 2 * k_rows), fixed),
            pl.BlockSpec((RADIX, RADIX), fixed),
            pl.BlockSpec((RADIX, RADIX), fixed),
            pl.BlockSpec((2 * RADIX, RADIX), fixed),
            pl.BlockSpec((2 * RADIX, RADIX), fixed),
        ],
        out_specs=pl.BlockSpec((1, block_total, RADIX // 2), lambda k: (k, 0, 0)),
        compiler_params=pltpu.CompilerParams(dimension_semantics=("arbitrary",)),
        cost_estimate=pl.CostEstimate(
            flops=pair_flops * template_total * block_total,
            transcendentals=0,
            bytes_accessed=spectra.size * 4 + bank.size * 2 + template_total * block_total * RADIX * 2,
        ),
    )(spectra, bank, *tables)


def gathered_bank(bank_rows):
    seg_total = lax.axis_size("seg")
    me = lax.axis_index("seg")
    rows, parts, local_bins = bank_rows.shape
    held = bank_rows[None]
    distance = seg_total // 2
    steps = 0
    while distance >= 1:
        pairs = [(i, i ^ distance) for i in range(seg_total)]
        arrived = lax.ppermute(held, "seg", pairs)
        upper = (me & distance) != 0
        held = jnp.stack([jnp.where(upper, arrived, held), jnp.where(upper, held, arrived)], axis=0)
        distance //= 2
        steps += 1
    held = held.reshape((2,) * steps + (rows, parts, local_bins // RADIX, RADIX))
    order = tuple(reversed(range(steps)))
    held = jnp.transpose(held, (steps, steps + 1) + order + (steps + 2, steps + 3))
    return held.reshape(rows, parts, seg_total * local_bins // RADIX, RADIX)


def local(strain, gate_mask, template_bank):
    gated = strain * gate_mask.astype(jnp.float32)
    local_blocks = gated.reshape(-1, BLOCK)
    block_total = local_blocks.shape[0]
    earlier = passed_along(local_blocks[block_total - 1], "seg", 1)
    before = jnp.concatenate([earlier[None], local_blocks[:-1]], axis=0)
    windows = jnp.concatenate([before, local_blocks], axis=1)
    spectra = forward(windows)
    tables = inverse_tables(spectra.shape[1])
    template_total = template_bank.shape[0]
    results = []
    for start in range(0, template_total, SUBBANK):
        bank = gathered_bank(template_bank[start : start + SUBBANK])
        peaks = window_peaks(spectra, bank, tables)
        results.append(peaks.reshape(bank.shape[0], block_total * (RADIX // 2)))
    return jnp.concatenate(results, axis=0)


def solution(mesh):
    in_specs = (P(("grp", "seg")), P(("grp", "seg")), P("grp", None, "seg"))
    out_specs = P(None, ("grp", "seg"))
    return jax.shard_map(local, mesh=mesh, in_specs=in_specs, out_specs=out_specs, check_vma=False)
```

```python
import math

import jax
import jax.numpy as jnp
from jax import lax
from jax.experimental import pallas as pl
from jax.experimental.pallas import tpu as pltpu
from jax.sharding import PartitionSpec as P

RADIX = 256
BLOCK = 32768
SUBBANK = 16


PRECISE = lax.Precision.HIGH
EPSILON = 1e-06


def passed_along(value, axis, by):
    count = lax.axis_size(axis)
    pairs = [(i, i + by) for i in range(count) if 0 <= i + by < count]
    return lax.ppermute(value, axis, pairs)


def angle_table(row_count, col_count, period):
    row_index = lax.broadcasted_iota(jnp.int32, (row_count, col_count), 0)
    col_index = lax.broadcasted_iota(jnp.int32, (row_count, col_count), 1)
    phase_step = row_index * col_index % period
    angle_value = phase_step.astype(jnp.float32) * (2.0 * math.pi / period)
    return (jnp.cos(angle_value), jnp.sin(angle_value))


def forward(windows):
    half_radix = RADIX // 2
    window_total = windows.shape[0]
    rows = windows.shape[1] // RADIX
    block_grid = windows.reshape(window_total, rows, RADIX)
    cos_first, sin_first = angle_table(rows, RADIX, RADIX)
    first_table = jnp.concatenate([cos_first, -sin_first], axis=1)
    first_section = jnp.einsum("bnm,nf->bmf", block_grid, first_table, precision=PRECISE)
    cos_twist, sin_twist = angle_table(RADIX, RADIX, RADIX * RADIX)
    real_part = first_section[..., :RADIX]
    imag_part = first_section[..., RADIX:]
    turned = jnp.concatenate(
        [
            real_part * cos_twist + imag_part * sin_twist,
            imag_part * cos_twist - real_part * sin_twist,
        ],
        axis=-1,
    )
    cos_second, sin_second = angle_table(RADIX, half_radix, RADIX)
    cosine_part = jnp.einsum("bnf,nk->bkf", turned, cos_second, precision=PRECISE)
    sine_part = jnp.einsum("bnf,nk->bkf", turned, sin_second, precision=PRECISE)
    return jnp.concatenate(
        [
            cosine_part[..., :RADIX] + sine_part[..., RADIX:],
            cosine_part[..., RADIX:] - sine_part[..., :RADIX],
        ],
        axis=-1,
    )


def split_pair(value):
    high = value.astype(jnp.bfloat16)
    low = (value - high.astype(jnp.float32)).astype(jnp.bfloat16)
    return high, low


def table_pair(value):
    high = lax.reduce_precision(value, exponent_bits=8, mantissa_bits=7)
    return high.astype(jnp.bfloat16), (value - high).astype(jnp.bfloat16)


def triple_dot(left_high, left_low, right_high, right_low):
    total = jnp.dot(left_high, right_high, preferred_element_type=jnp.float32)
    total = total + jnp.dot(left_high, right_low, preferred_element_type=jnp.float32)
    return total + jnp.dot(left_low, right_high, preferred_element_type=jnp.float32)


def inverse_tables(k_rows):
    half_radix = RADIX // 2
    cos_first, sin_first = angle_table(RADIX, k_rows, RADIX)
    first = jnp.concatenate(
        [
            jnp.concatenate([cos_first, -sin_first], axis=1),
            jnp.concatenate([sin_first, cos_first], axis=1),
        ],
        axis=0,
    )
    cos_twist, sin_twist = angle_table(RADIX, RADIX, RADIX * RADIX)
    cos_out, sin_out = angle_table(RADIX, RADIX, RADIX)
    real_cols = jnp.concatenate([cos_out, -sin_out], axis=0)
    imag_cols = jnp.concatenate([sin_out, cos_out], axis=0)
    second = jnp.concatenate([real_cols[:, half_radix:], imag_cols[:, half_radix:]], axis=1)
    first_high, first_low = table_pair(first)
    second_high, second_low = table_pair(second)
    return first_high, first_low, cos_twist, sin_twist, second_high, second_low


def peaks_kernel(spec_ref, bank_ref, fh_ref, fl_ref, tc_ref, ts_ref, sh_ref, sl_ref, out_ref):
    half_radix = RADIX // 2
    wave_real = bank_ref[0, 0].astype(jnp.float32)
    wave_imag = bank_ref[0, 1].astype(jnp.float32)
    power_sum = jnp.sum(wave_real * wave_real + wave_imag * wave_imag, keepdims=True)
    norm_scale = 1.0 / jnp.sqrt(BLOCK * power_sum + EPSILON)
    for block in range(spec_ref.shape[0]):
        spec_real = spec_ref[block, :, :RADIX]
        spec_imag = spec_ref[block, :, RADIX:]
        prod_real = spec_real * wave_real + spec_imag * wave_imag
        prod_imag = spec_imag * wave_real - spec_real * wave_imag
        stacked = jnp.concatenate([prod_real, prod_imag], axis=0)
        stacked_high, stacked_low = split_pair(stacked)
        first = triple_dot(fh_ref[...], fl_ref[...], stacked_high, stacked_low)
        real_part = first[:RADIX]
        imag_part = first[RADIX:]
        cos_twist = tc_ref[...]
        sin_twist = ts_ref[...]
        turned = jnp.concatenate(
            [
                real_part * cos_twist - imag_part * sin_twist,
                real_part * sin_twist + imag_part * cos_twist,
            ],
            axis=1,
        )
        turned_high, turned_low = split_pair(turned)
        series = triple_dot(turned_high, turned_low, sh_ref[...], sl_ref[...])
        power_series = (
            series[:, :half_radix] * series[:, :half_radix]
            + series[:, half_radix:] * series[:, half_radix:]
        )
        peak = jnp.max(power_series, axis=0, keepdims=True)
        out_ref[0, block : block + 1, :] = peak * (norm_scale * norm_scale)


def window_peaks(spectra, bank, tables):
    block_total, k_rows, _ = spectra.shape
    template_total = bank.shape[0]
    fixed = lambda k: (0, 0)
    pair_flops = 6 * (2 * RADIX) * (2 * k_rows) * RADIX + 6 * RADIX * (2 * RADIX) * RADIX
    return pl.pallas_call(
        peaks_kernel,
        out_shape=jax.ShapeDtypeStruct((template_total, block_total, RADIX // 2), jnp.float32),
        grid=(template_total,),
        in_specs=[
            pl.BlockSpec((block_total, k_rows, 2 * RADIX), lambda k: (0, 0, 0)),
            pl.BlockSpec((1, 2, k_rows, RADIX), lambda k: (k, 0, 0, 0)),
            pl.BlockSpec((2 * RADIX, 2 * k_rows), fixed),
            pl.BlockSpec((2 * RADIX, 2 * k_rows), fixed),
            pl.BlockSpec((RADIX, RADIX), fixed),
            pl.BlockSpec((RADIX, RADIX), fixed),
            pl.BlockSpec((2 * RADIX, RADIX), fixed),
            pl.BlockSpec((2 * RADIX, RADIX), fixed),
        ],
        out_specs=pl.BlockSpec((1, block_total, RADIX // 2), lambda k: (k, 0, 0)),
        compiler_params=pltpu.CompilerParams(dimension_semantics=("arbitrary",)),
        cost_estimate=pl.CostEstimate(
            flops=pair_flops * template_total * block_total,
            transcendentals=0,
            bytes_accessed=spectra.size * 4 + bank.size * 2 + template_total * block_total * RADIX * 2,
        ),
    )(spectra, bank, *tables)


def gathered_bank(bank_rows):
    seg_total = lax.axis_size("seg")
    rows, parts, local_bins = bank_rows.shape
    copies = jnp.broadcast_to(bank_rows[None], (seg_total, rows, parts, local_bins))
    every = lax.all_to_all(copies, "seg", 0, 0, tiled=True)
    every = every.reshape(seg_total, rows, parts, local_bins // RADIX, RADIX)
    every = jnp.transpose(every, (1, 2, 0, 3, 4))
    return every.reshape(rows, parts, seg_total * local_bins // RADIX, RADIX)


def local(strain, gate_mask, template_bank):
    gated = strain * gate_mask.astype(jnp.float32)
    local_blocks = gated.reshape(-1, BLOCK)
    block_total = local_blocks.shape[0]
    earlier = passed_along(local_blocks[block_total - 1], "seg", 1)
    before = jnp.concatenate([earlier[None], local_blocks[:-1]], axis=0)
    windows = jnp.concatenate([before, local_blocks], axis=1)
    spectra = forward(windows)
    tables = inverse_tables(spectra.shape[1])
    template_total = template_bank.shape[0]
    results = []
    for start in range(0, template_total, SUBBANK):
        bank = gathered_bank(template_bank[start : start + SUBBANK])
        peaks = window_peaks(spectra, bank, tables)
        results.append(peaks.reshape(bank.shape[0], block_total * (RADIX // 2)))
    return jnp.concatenate(results, axis=0)


def solution(mesh):
    in_specs = (P(("grp", "seg")), P(("grp", "seg")), P("grp", None, "seg"))
    out_specs = P(None, ("grp", "seg"))
    return jax.shard_map(local, mesh=mesh, in_specs=in_specs, out_specs=out_specs, check_vma=False)
```

```python
import math

import jax
import jax.numpy as jnp
from jax import lax
from jax.experimental import pallas as pl
from jax.experimental.pallas import tpu as pltpu
from jax.sharding import PartitionSpec as P

RADIX = 256
BLOCK = 32768
SUBBANK = 8


PRECISE = lax.Precision.HIGH
EPSILON = 1e-06


def passed_along(value, axis, by):
    count = lax.axis_size(axis)
    pairs = [(i, i + by) for i in range(count) if 0 <= i + by < count]
    return lax.ppermute(value, axis, pairs)


def angle_table(row_count, col_count, period):
    row_index = lax.broadcasted_iota(jnp.int32, (row_count, col_count), 0)
    col_index = lax.broadcasted_iota(jnp.int32, (row_count, col_count), 1)
    phase_step = row_index * col_index % period
    angle_value = phase_step.astype(jnp.float32) * (2.0 * math.pi / period)
    return (jnp.cos(angle_value), jnp.sin(angle_value))


def forward(windows):
    half_radix = RADIX // 2
    window_total = windows.shape[0]
    rows = windows.shape[1] // RADIX
    block_grid = windows.reshape(window_total, rows, RADIX)
    cos_first, sin_first = angle_table(rows, RADIX, RADIX)
    first_table = jnp.concatenate([cos_first, -sin_first], axis=1)
    first_section = jnp.einsum("bnm,nf->bmf", block_grid, first_table, precision=PRECISE)
    cos_twist, sin_twist = angle_table(RADIX, RADIX, RADIX * RADIX)
    real_part = first_section[..., :RADIX]
    imag_part = first_section[..., RADIX:]
    turned = jnp.concatenate(
        [
            real_part * cos_twist + imag_part * sin_twist,
            imag_part * cos_twist - real_part * sin_twist,
        ],
        axis=-1,
    )
    cos_second, sin_second = angle_table(RADIX, half_radix, RADIX)
    cosine_part = jnp.einsum("bnf,nk->bkf", turned, cos_second, precision=PRECISE)
    sine_part = jnp.einsum("bnf,nk->bkf", turned, sin_second, precision=PRECISE)
    return jnp.concatenate(
        [
            cosine_part[..., :RADIX] + sine_part[..., RADIX:],
            cosine_part[..., RADIX:] - sine_part[..., :RADIX],
        ],
        axis=-1,
    )


def split_pair(value):
    high = value.astype(jnp.bfloat16)
    low = (value - high.astype(jnp.float32)).astype(jnp.bfloat16)
    return high, low


def table_pair(value):
    high = lax.reduce_precision(value, exponent_bits=8, mantissa_bits=7)
    return high.astype(jnp.bfloat16), (value - high).astype(jnp.bfloat16)


def triple_dot(left_high, left_low, right_high, right_low):
    total = jnp.dot(left_high, right_high, preferred_element_type=jnp.float32)
    total = total + jnp.dot(left_high, right_low, preferred_element_type=jnp.float32)
    return total + jnp.dot(left_low, right_high, preferred_element_type=jnp.float32)


def inverse_tables(k_rows):
    half_radix = RADIX // 2
    cos_first, sin_first = angle_table(RADIX, k_rows, RADIX)
    first = jnp.concatenate(
        [
            jnp.concatenate([cos_first, -sin_first], axis=1),
            jnp.concatenate([sin_first, cos_first], axis=1),
        ],
        axis=0,
    )
    cos_twist, sin_twist = angle_table(RADIX, RADIX, RADIX * RADIX)
    cos_out, sin_out = angle_table(RADIX, RADIX, RADIX)
    real_cols = jnp.concatenate([cos_out, -sin_out], axis=0)
    imag_cols = jnp.concatenate([sin_out, cos_out], axis=0)
    second = jnp.concatenate([real_cols[:, half_radix:], imag_cols[:, half_radix:]], axis=1)
    first_high, first_low = table_pair(first)
    second_high, second_low = table_pair(second)
    return first_high, first_low, cos_twist, sin_twist, second_high, second_low


def peaks_kernel(spec_ref, bank_ref, fh_ref, fl_ref, tc_ref, ts_ref, sh_ref, sl_ref, out_ref):
    half_radix = RADIX // 2
    wave_real = bank_ref[0, 0].astype(jnp.float32)
    wave_imag = bank_ref[0, 1].astype(jnp.float32)
    power_sum = jnp.sum(wave_real * wave_real + wave_imag * wave_imag, keepdims=True)
    norm_scale = 1.0 / jnp.sqrt(BLOCK * power_sum + EPSILON)
    for block in range(spec_ref.shape[0]):
        spec_real = spec_ref[block, :, :RADIX]
        spec_imag = spec_ref[block, :, RADIX:]
        prod_real = spec_real * wave_real + spec_imag * wave_imag
        prod_imag = spec_imag * wave_real - spec_real * wave_imag
        stacked = jnp.concatenate([prod_real, prod_imag], axis=0)
        stacked_high, stacked_low = split_pair(stacked)
        first = triple_dot(fh_ref[...], fl_ref[...], stacked_high, stacked_low)
        real_part = first[:RADIX]
        imag_part = first[RADIX:]
        cos_twist = tc_ref[...]
        sin_twist = ts_ref[...]
        turned = jnp.concatenate(
            [
                real_part * cos_twist - imag_part * sin_twist,
                real_part * sin_twist + imag_part * cos_twist,
            ],
            axis=1,
        )
        turned_high, turned_low = split_pair(turned)
        series = triple_dot(turned_high, turned_low, sh_ref[...], sl_ref[...])
        power_series = (
            series[:, :half_radix] * series[:, :half_radix]
            + series[:, half_radix:] * series[:, half_radix:]
        )
        peak = jnp.max(power_series, axis=0, keepdims=True)
        out_ref[0, block : block + 1, :] = peak * (norm_scale * norm_scale)


def window_peaks(spectra, bank, tables):
    block_total, k_rows, _ = spectra.shape
    template_total = bank.shape[0]
    fixed = lambda k: (0, 0)
    pair_flops = 6 * (2 * RADIX) * (2 * k_rows) * RADIX + 6 * RADIX * (2 * RADIX) * RADIX
    return pl.pallas_call(
        peaks_kernel,
        out_shape=jax.ShapeDtypeStruct((template_total, block_total, RADIX // 2), jnp.float32),
        grid=(template_total,),
        in_specs=[
            pl.BlockSpec((block_total, k_rows, 2 * RADIX), lambda k: (0, 0, 0)),
            pl.BlockSpec((1, 2, k_rows, RADIX), lambda k: (k, 0, 0, 0)),
            pl.BlockSpec((2 * RADIX, 2 * k_rows), fixed),
            pl.BlockSpec((2 * RADIX, 2 * k_rows), fixed),
            pl.BlockSpec((RADIX, RADIX), fixed),
            pl.BlockSpec((RADIX, RADIX), fixed),
            pl.BlockSpec((2 * RADIX, RADIX), fixed),
            pl.BlockSpec((2 * RADIX, RADIX), fixed),
        ],
        out_specs=pl.BlockSpec((1, block_total, RADIX // 2), lambda k: (k, 0, 0)),
        compiler_params=pltpu.CompilerParams(dimension_semantics=("arbitrary",)),
        cost_estimate=pl.CostEstimate(
            flops=pair_flops * template_total * block_total,
            transcendentals=0,
            bytes_accessed=spectra.size * 4 + bank.size * 2 + template_total * block_total * RADIX * 2,
        ),
    )(spectra, bank, *tables)


def gathered_bank(bank_rows):
    seg_total = lax.axis_size("seg")
    me = lax.axis_index("seg")
    rows, parts, local_bins = bank_rows.shape
    held = bank_rows[None]
    distance = seg_total // 2
    steps = 0
    while distance >= 1:
        pairs = [(i, i ^ distance) for i in range(seg_total)]
        arrived = lax.ppermute(held, "seg", pairs)
        upper = (me & distance) != 0
        held = jnp.stack([jnp.where(upper, arrived, held), jnp.where(upper, held, arrived)], axis=0)
        distance //= 2
        steps += 1
    held = held.reshape((2,) * steps + (rows, parts, local_bins // RADIX, RADIX))
    order = tuple(reversed(range(steps)))
    held = jnp.transpose(held, (steps, steps + 1) + order + (steps + 2, steps + 3))
    return held.reshape(rows, parts, seg_total * local_bins // RADIX, RADIX)


def local(strain, gate_mask, template_bank):
    gated = strain * gate_mask.astype(jnp.float32)
    local_blocks = gated.reshape(-1, BLOCK)
    block_total = local_blocks.shape[0]
    earlier = passed_along(local_blocks[block_total - 1], "seg", 1)
    before = jnp.concatenate([earlier[None], local_blocks[:-1]], axis=0)
    windows = jnp.concatenate([before, local_blocks], axis=1)
    spectra = forward(windows)
    tables = inverse_tables(spectra.shape[1])
    template_total = template_bank.shape[0]
    results = []
    for start in range(0, template_total, SUBBANK):
        bank = gathered_bank(template_bank[start : start + SUBBANK])
        peaks = window_peaks(spectra, bank, tables)
        results.append(peaks.reshape(bank.shape[0], block_total * (RADIX // 2)))
    return jnp.concatenate(results, axis=0)


def solution(mesh):
    in_specs = (P(("grp", "seg")), P(("grp", "seg")), P("grp", None, "seg"))
    out_specs = P(None, ("grp", "seg"))
    return jax.shard_map(local, mesh=mesh, in_specs=in_specs, out_specs=out_specs, check_vma=False)
```

```python
import math

import jax
import jax.numpy as jnp
from jax import lax
from jax.experimental import pallas as pl
from jax.experimental.pallas import tpu as pltpu
from jax.sharding import PartitionSpec as P

RADIX = 256
BLOCK = 32768
SUBBANK = 4


PRECISE = lax.Precision.HIGH
EPSILON = 1e-06


def passed_along(value, axis, by):
    count = lax.axis_size(axis)
    pairs = [(i, i + by) for i in range(count) if 0 <= i + by < count]
    return lax.ppermute(value, axis, pairs)


def angle_table(row_count, col_count, period):
    row_index = lax.broadcasted_iota(jnp.int32, (row_count, col_count), 0)
    col_index = lax.broadcasted_iota(jnp.int32, (row_count, col_count), 1)
    phase_step = row_index * col_index % period
    angle_value = phase_step.astype(jnp.float32) * (2.0 * math.pi / period)
    return (jnp.cos(angle_value), jnp.sin(angle_value))


def forward(windows):
    half_radix = RADIX // 2
    window_total = windows.shape[0]
    rows = windows.shape[1] // RADIX
    block_grid = windows.reshape(window_total, rows, RADIX)
    cos_first, sin_first = angle_table(rows, RADIX, RADIX)
    first_table = jnp.concatenate([cos_first, -sin_first], axis=1)
    first_section = jnp.einsum("bnm,nf->bmf", block_grid, first_table, precision=PRECISE)
    cos_twist, sin_twist = angle_table(RADIX, RADIX, RADIX * RADIX)
    real_part = first_section[..., :RADIX]
    imag_part = first_section[..., RADIX:]
    turned = jnp.concatenate(
        [
            real_part * cos_twist + imag_part * sin_twist,
            imag_part * cos_twist - real_part * sin_twist,
        ],
        axis=-1,
    )
    cos_second, sin_second = angle_table(RADIX, half_radix, RADIX)
    cosine_part = jnp.einsum("bnf,nk->bkf", turned, cos_second, precision=PRECISE)
    sine_part = jnp.einsum("bnf,nk->bkf", turned, sin_second, precision=PRECISE)
    return jnp.concatenate(
        [
            cosine_part[..., :RADIX] + sine_part[..., RADIX:],
            cosine_part[..., RADIX:] - sine_part[..., :RADIX],
        ],
        axis=-1,
    )


def split_pair(value):
    high = value.astype(jnp.bfloat16)
    low = (value - high.astype(jnp.float32)).astype(jnp.bfloat16)
    return high, low


def table_pair(value):
    high = lax.reduce_precision(value, exponent_bits=8, mantissa_bits=7)
    return high.astype(jnp.bfloat16), (value - high).astype(jnp.bfloat16)


def triple_dot(left_high, left_low, right_high, right_low):
    total = jnp.dot(left_high, right_high, preferred_element_type=jnp.float32)
    total = total + jnp.dot(left_high, right_low, preferred_element_type=jnp.float32)
    return total + jnp.dot(left_low, right_high, preferred_element_type=jnp.float32)


def inverse_tables(k_rows):
    half_radix = RADIX // 2
    cos_first, sin_first = angle_table(RADIX, k_rows, RADIX)
    first = jnp.concatenate(
        [
            jnp.concatenate([cos_first, -sin_first], axis=1),
            jnp.concatenate([sin_first, cos_first], axis=1),
        ],
        axis=0,
    )
    cos_twist, sin_twist = angle_table(RADIX, RADIX, RADIX * RADIX)
    cos_out, sin_out = angle_table(RADIX, RADIX, RADIX)
    real_cols = jnp.concatenate([cos_out, -sin_out], axis=0)
    imag_cols = jnp.concatenate([sin_out, cos_out], axis=0)
    second = jnp.concatenate([real_cols[:, half_radix:], imag_cols[:, half_radix:]], axis=1)
    first_high, first_low = table_pair(first)
    second_high, second_low = table_pair(second)
    return first_high, first_low, cos_twist, sin_twist, second_high, second_low


def peaks_kernel(spec_ref, bank_ref, fh_ref, fl_ref, tc_ref, ts_ref, sh_ref, sl_ref, out_ref):
    half_radix = RADIX // 2
    wave_real = bank_ref[0, 0].astype(jnp.float32)
    wave_imag = bank_ref[0, 1].astype(jnp.float32)
    power_sum = jnp.sum(wave_real * wave_real + wave_imag * wave_imag, keepdims=True)
    norm_scale = 1.0 / jnp.sqrt(BLOCK * power_sum + EPSILON)
    for block in range(spec_ref.shape[0]):
        spec_real = spec_ref[block, :, :RADIX]
        spec_imag = spec_ref[block, :, RADIX:]
        prod_real = spec_real * wave_real + spec_imag * wave_imag
        prod_imag = spec_imag * wave_real - spec_real * wave_imag
        stacked = jnp.concatenate([prod_real, prod_imag], axis=0)
        stacked_high, stacked_low = split_pair(stacked)
        first = triple_dot(fh_ref[...], fl_ref[...], stacked_high, stacked_low)
        real_part = first[:RADIX]
        imag_part = first[RADIX:]
        cos_twist = tc_ref[...]
        sin_twist = ts_ref[...]
        turned = jnp.concatenate(
            [
                real_part * cos_twist - imag_part * sin_twist,
                real_part * sin_twist + imag_part * cos_twist,
            ],
            axis=1,
        )
        turned_high, turned_low = split_pair(turned)
        series = triple_dot(turned_high, turned_low, sh_ref[...], sl_ref[...])
        power_series = (
            series[:, :half_radix] * series[:, :half_radix]
            + series[:, half_radix:] * series[:, half_radix:]
        )
        peak = jnp.max(power_series, axis=0, keepdims=True)
        out_ref[0, block : block + 1, :] = peak * (norm_scale * norm_scale)


def window_peaks(spectra, bank, tables):
    block_total, k_rows, _ = spectra.shape
    template_total = bank.shape[0]
    fixed = lambda k: (0, 0)
    pair_flops = 6 * (2 * RADIX) * (2 * k_rows) * RADIX + 6 * RADIX * (2 * RADIX) * RADIX
    return pl.pallas_call(
        peaks_kernel,
        out_shape=jax.ShapeDtypeStruct((template_total, block_total, RADIX // 2), jnp.float32),
        grid=(template_total,),
        in_specs=[
            pl.BlockSpec((block_total, k_rows, 2 * RADIX), lambda k: (0, 0, 0)),
            pl.BlockSpec((1, 2, k_rows, RADIX), lambda k: (k, 0, 0, 0)),
            pl.BlockSpec((2 * RADIX, 2 * k_rows), fixed),
            pl.BlockSpec((2 * RADIX, 2 * k_rows), fixed),
            pl.BlockSpec((RADIX, RADIX), fixed),
            pl.BlockSpec((RADIX, RADIX), fixed),
            pl.BlockSpec((2 * RADIX, RADIX), fixed),
            pl.BlockSpec((2 * RADIX, RADIX), fixed),
        ],
        out_specs=pl.BlockSpec((1, block_total, RADIX // 2), lambda k: (k, 0, 0)),
        compiler_params=pltpu.CompilerParams(dimension_semantics=("arbitrary",)),
        cost_estimate=pl.CostEstimate(
            flops=pair_flops * template_total * block_total,
            transcendentals=0,
            bytes_accessed=spectra.size * 4 + bank.size * 2 + template_total * block_total * RADIX * 2,
        ),
    )(spectra, bank, *tables)


def gathered_bank(bank_rows):
    seg_total = lax.axis_size("seg")
    me = lax.axis_index("seg")
    rows, parts, local_bins = bank_rows.shape
    held = bank_rows[None]
    distance = seg_total // 2
    steps = 0
    while distance >= 1:
        pairs = [(i, i ^ distance) for i in range(seg_total)]
        arrived = lax.ppermute(held, "seg", pairs)
        upper = (me & distance) != 0
        held = jnp.stack([jnp.where(upper, arrived, held), jnp.where(upper, held, arrived)], axis=0)
        distance //= 2
        steps += 1
    held = held.reshape((2,) * steps + (rows, parts, local_bins // RADIX, RADIX))
    order = tuple(reversed(range(steps)))
    held = jnp.transpose(held, (steps, steps + 1) + order + (steps + 2, steps + 3))
    return held.reshape(rows, parts, seg_total * local_bins // RADIX, RADIX)


def local(strain, gate_mask, template_bank):
    gated = strain * gate_mask.astype(jnp.float32)
    local_blocks = gated.reshape(-1, BLOCK)
    block_total = local_blocks.shape[0]
    earlier = passed_along(local_blocks[block_total - 1], "seg", 1)
    before = jnp.concatenate([earlier[None], local_blocks[:-1]], axis=0)
    windows = jnp.concatenate([before, local_blocks], axis=1)
    spectra = forward(windows)
    tables = inverse_tables(spectra.shape[1])
    template_total = template_bank.shape[0]
    results = []
    for start in range(0, template_total, SUBBANK):
        bank = gathered_bank(template_bank[start : start + SUBBANK])
        peaks = window_peaks(spectra, bank, tables)
        results.append(peaks.reshape(bank.shape[0], block_total * (RADIX // 2)))
    return jnp.concatenate(results, axis=0)


def solution(mesh):
    in_specs = (P(("grp", "seg")), P(("grp", "seg")), P("grp", None, "seg"))
    out_specs = P(None, ("grp", "seg"))
    return jax.shard_map(local, mesh=mesh, in_specs=in_specs, out_specs=out_specs, check_vma=False)
```

```python
import math

import jax
import jax.numpy as jnp
from jax import lax
from jax.experimental import pallas as pl
from jax.experimental.pallas import tpu as pltpu
from jax.sharding import PartitionSpec as P

RADIX = 256
BLOCK = 32768
SUBBANK = 8
STEP_TEMPLATES = 2


PRECISE = lax.Precision.HIGH
EPSILON = 1e-06


def passed_along(value, axis, by):
    count = lax.axis_size(axis)
    pairs = [(i, i + by) for i in range(count) if 0 <= i + by < count]
    return lax.ppermute(value, axis, pairs)


def angle_table(row_count, col_count, period):
    row_index = lax.broadcasted_iota(jnp.int32, (row_count, col_count), 0)
    col_index = lax.broadcasted_iota(jnp.int32, (row_count, col_count), 1)
    phase_step = row_index * col_index % period
    angle_value = phase_step.astype(jnp.float32) * (2.0 * math.pi / period)
    return (jnp.cos(angle_value), jnp.sin(angle_value))


def forward(windows):
    half_radix = RADIX // 2
    window_total = windows.shape[0]
    rows = windows.shape[1] // RADIX
    block_grid = windows.reshape(window_total, rows, RADIX)
    cos_first, sin_first = angle_table(rows, RADIX, RADIX)
    first_table = jnp.concatenate([cos_first, -sin_first], axis=1)
    first_section = jnp.einsum("bnm,nf->bmf", block_grid, first_table, precision=PRECISE)
    cos_twist, sin_twist = angle_table(RADIX, RADIX, RADIX * RADIX)
    real_part = first_section[..., :RADIX]
    imag_part = first_section[..., RADIX:]
    turned = jnp.concatenate(
        [
            real_part * cos_twist + imag_part * sin_twist,
            imag_part * cos_twist - real_part * sin_twist,
        ],
        axis=-1,
    )
    cos_second, sin_second = angle_table(RADIX, half_radix, RADIX)
    cosine_part = jnp.einsum("bnf,nk->bkf", turned, cos_second, precision=PRECISE)
    sine_part = jnp.einsum("bnf,nk->bkf", turned, sin_second, precision=PRECISE)
    return jnp.concatenate(
        [
            cosine_part[..., :RADIX] + sine_part[..., RADIX:],
            cosine_part[..., RADIX:] - sine_part[..., :RADIX],
        ],
        axis=-1,
    )


def split_pair(value):
    high = value.astype(jnp.bfloat16)
    low = (value - high.astype(jnp.float32)).astype(jnp.bfloat16)
    return high, low


def table_pair(value):
    high = lax.reduce_precision(value, exponent_bits=8, mantissa_bits=7)
    return high.astype(jnp.bfloat16), (value - high).astype(jnp.bfloat16)


def triple_dot(left_high, left_low, right_high, right_low):
    total = jnp.dot(left_high, right_high, preferred_element_type=jnp.float32)
    total = total + jnp.dot(left_high, right_low, preferred_element_type=jnp.float32)
    return total + jnp.dot(left_low, right_high, preferred_element_type=jnp.float32)


def inverse_tables(k_rows):
    half_radix = RADIX // 2
    cos_first, sin_first = angle_table(RADIX, k_rows, RADIX)
    first = jnp.concatenate(
        [
            jnp.concatenate([cos_first, -sin_first], axis=1),
            jnp.concatenate([sin_first, cos_first], axis=1),
        ],
        axis=0,
    )
    cos_twist, sin_twist = angle_table(RADIX, RADIX, RADIX * RADIX)
    cos_out, sin_out = angle_table(RADIX, RADIX, RADIX)
    real_cols = jnp.concatenate([cos_out, -sin_out], axis=0)
    imag_cols = jnp.concatenate([sin_out, cos_out], axis=0)
    second = jnp.concatenate([real_cols[:, half_radix:], imag_cols[:, half_radix:]], axis=1)
    first_high, first_low = table_pair(first)
    second_high, second_low = table_pair(second)
    return first_high, first_low, cos_twist, sin_twist, second_high, second_low


def peaks_kernel(spec_ref, bank_ref, fh_ref, fl_ref, tc_ref, ts_ref, sh_ref, sl_ref, out_ref):
    half_radix = RADIX // 2
    block_total = spec_ref.shape[0]
    step_templates = bank_ref.shape[0]
    pair_total = step_templates * block_total
    products = []
    scales = []
    for template in range(step_templates):
        wave_real = bank_ref[template, 0].astype(jnp.float32)
        wave_imag = bank_ref[template, 1].astype(jnp.float32)
        power_sum = jnp.sum(wave_real * wave_real + wave_imag * wave_imag, keepdims=True)
        norm_scale = 1.0 / jnp.sqrt(BLOCK * power_sum + EPSILON)
        scales.append(norm_scale * norm_scale)
        for block in range(block_total):
            spec_real = spec_ref[block, :, :RADIX]
            spec_imag = spec_ref[block, :, RADIX:]
            prod_real = spec_real * wave_real + spec_imag * wave_imag
            prod_imag = spec_imag * wave_real - spec_real * wave_imag
            products.append(jnp.concatenate([prod_real, prod_imag], axis=0))
    stacked = jnp.concatenate(products, axis=1)
    stacked_high, stacked_low = split_pair(stacked)
    first = triple_dot(fh_ref[...], fl_ref[...], stacked_high, stacked_low)
    cos_twist = tc_ref[...]
    sin_twist = ts_ref[...]
    turned_rows = []
    for pair in range(pair_total):
        real_part = first[:RADIX, pair * RADIX : (pair + 1) * RADIX]
        imag_part = first[RADIX:, pair * RADIX : (pair + 1) * RADIX]
        turned_rows.append(
            jnp.concatenate(
                [
                    real_part * cos_twist - imag_part * sin_twist,
                    real_part * sin_twist + imag_part * cos_twist,
                ],
                axis=1,
            )
        )
    turned = jnp.concatenate(turned_rows, axis=0)
    turned_high, turned_low = split_pair(turned)
    series = triple_dot(turned_high, turned_low, sh_ref[...], sl_ref[...])
    power_series = (
        series[:, :half_radix] * series[:, :half_radix]
        + series[:, half_radix:] * series[:, half_radix:]
    )
    peaks = jnp.max(power_series.reshape(pair_total, RADIX, half_radix), axis=1)
    for template in range(step_templates):
        rows = peaks[template * block_total : (template + 1) * block_total]
        out_ref[template] = rows * scales[template]


def window_peaks(spectra, bank, tables):
    block_total, k_rows, _ = spectra.shape
    template_total = bank.shape[0]
    step_templates = STEP_TEMPLATES if template_total % STEP_TEMPLATES == 0 else 1
    fixed = lambda k: (0, 0)
    pair_flops = 6 * (2 * RADIX) * (2 * k_rows) * RADIX + 6 * RADIX * (2 * RADIX) * RADIX
    return pl.pallas_call(
        peaks_kernel,
        out_shape=jax.ShapeDtypeStruct((template_total, block_total, RADIX // 2), jnp.float32),
        grid=(template_total // step_templates,),
        in_specs=[
            pl.BlockSpec((block_total, k_rows, 2 * RADIX), lambda k: (0, 0, 0)),
            pl.BlockSpec((step_templates, 2, k_rows, RADIX), lambda k: (k, 0, 0, 0)),
            pl.BlockSpec((2 * RADIX, 2 * k_rows), fixed),
            pl.BlockSpec((2 * RADIX, 2 * k_rows), fixed),
            pl.BlockSpec((RADIX, RADIX), fixed),
            pl.BlockSpec((RADIX, RADIX), fixed),
            pl.BlockSpec((2 * RADIX, RADIX), fixed),
            pl.BlockSpec((2 * RADIX, RADIX), fixed),
        ],
        out_specs=pl.BlockSpec((step_templates, block_total, RADIX // 2), lambda k: (k, 0, 0)),
        compiler_params=pltpu.CompilerParams(dimension_semantics=("arbitrary",)),
        cost_estimate=pl.CostEstimate(
            flops=pair_flops * template_total * block_total,
            transcendentals=0,
            bytes_accessed=spectra.size * 4 + bank.size * 2 + template_total * block_total * RADIX * 2,
        ),
    )(spectra, bank, *tables)


def gathered_bank(bank_rows):
    seg_total = lax.axis_size("seg")
    me = lax.axis_index("seg")
    rows, parts, local_bins = bank_rows.shape
    held = bank_rows[None]
    distance = seg_total // 2
    steps = 0
    while distance >= 1:
        pairs = [(i, i ^ distance) for i in range(seg_total)]
        arrived = lax.ppermute(held, "seg", pairs)
        upper = (me & distance) != 0
        held = jnp.stack([jnp.where(upper, arrived, held), jnp.where(upper, held, arrived)], axis=0)
        distance //= 2
        steps += 1
    held = held.reshape((2,) * steps + (rows, parts, local_bins // RADIX, RADIX))
    order = tuple(reversed(range(steps)))
    held = jnp.transpose(held, (steps, steps + 1) + order + (steps + 2, steps + 3))
    return held.reshape(rows, parts, seg_total * local_bins // RADIX, RADIX)


def local(strain, gate_mask, template_bank):
    gated = strain * gate_mask.astype(jnp.float32)
    local_blocks = gated.reshape(-1, BLOCK)
    block_total = local_blocks.shape[0]
    earlier = passed_along(local_blocks[block_total - 1], "seg", 1)
    before = jnp.concatenate([earlier[None], local_blocks[:-1]], axis=0)
    windows = jnp.concatenate([before, local_blocks], axis=1)
    spectra = forward(windows)
    tables = inverse_tables(spectra.shape[1])
    template_total = template_bank.shape[0]
    results = []
    for start in range(0, template_total, SUBBANK):
        bank = gathered_bank(template_bank[start : start + SUBBANK])
        peaks = window_peaks(spectra, bank, tables)
        results.append(peaks.reshape(bank.shape[0], block_total * (RADIX // 2)))
    return jnp.concatenate(results, axis=0)


def solution(mesh):
    in_specs = (P(("grp", "seg")), P(("grp", "seg")), P("grp", None, "seg"))
    out_specs = P(None, ("grp", "seg"))
    return jax.shard_map(local, mesh=mesh, in_specs=in_specs, out_specs=out_specs, check_vma=False)
```

```python
import math

import jax
import jax.numpy as jnp
from jax import lax
from jax.experimental import pallas as pl
from jax.experimental.pallas import tpu as pltpu
from jax.sharding import PartitionSpec as P

RADIX = 256
BLOCK = 32768
SUBBANK = 8
STEP_TEMPLATES = 4


PRECISE = lax.Precision.HIGH
EPSILON = 1e-06


def passed_along(value, axis, by):
    count = lax.axis_size(axis)
    pairs = [(i, i + by) for i in range(count) if 0 <= i + by < count]
    return lax.ppermute(value, axis, pairs)


def angle_table(row_count, col_count, period):
    row_index = lax.broadcasted_iota(jnp.int32, (row_count, col_count), 0)
    col_index = lax.broadcasted_iota(jnp.int32, (row_count, col_count), 1)
    phase_step = row_index * col_index % period
    angle_value = phase_step.astype(jnp.float32) * (2.0 * math.pi / period)
    return (jnp.cos(angle_value), jnp.sin(angle_value))


def forward(windows):
    half_radix = RADIX // 2
    window_total = windows.shape[0]
    rows = windows.shape[1] // RADIX
    block_grid = windows.reshape(window_total, rows, RADIX)
    cos_first, sin_first = angle_table(rows, RADIX, RADIX)
    first_table = jnp.concatenate([cos_first, -sin_first], axis=1)
    first_section = jnp.einsum("bnm,nf->bmf", block_grid, first_table, precision=PRECISE)
    cos_twist, sin_twist = angle_table(RADIX, RADIX, RADIX * RADIX)
    real_part = first_section[..., :RADIX]
    imag_part = first_section[..., RADIX:]
    turned = jnp.concatenate(
        [
            real_part * cos_twist + imag_part * sin_twist,
            imag_part * cos_twist - real_part * sin_twist,
        ],
        axis=-1,
    )
    cos_second, sin_second = angle_table(RADIX, half_radix, RADIX)
    cosine_part = jnp.einsum("bnf,nk->bkf", turned, cos_second, precision=PRECISE)
    sine_part = jnp.einsum("bnf,nk->bkf", turned, sin_second, precision=PRECISE)
    return jnp.concatenate(
        [
            cosine_part[..., :RADIX] + sine_part[..., RADIX:],
            cosine_part[..., RADIX:] - sine_part[..., :RADIX],
        ],
        axis=-1,
    )


def split_pair(value):
    high = value.astype(jnp.bfloat16)
    low = (value - high.astype(jnp.float32)).astype(jnp.bfloat16)
    return high, low


def table_pair(value):
    high = lax.reduce_precision(value, exponent_bits=8, mantissa_bits=7)
    return high.astype(jnp.bfloat16), (value - high).astype(jnp.bfloat16)


def triple_dot(left_high, left_low, right_high, right_low):
    total = jnp.dot(left_high, right_high, preferred_element_type=jnp.float32)
    total = total + jnp.dot(left_high, right_low, preferred_element_type=jnp.float32)
    return total + jnp.dot(left_low, right_high, preferred_element_type=jnp.float32)


def inverse_tables(k_rows):
    half_radix = RADIX // 2
    cos_first, sin_first = angle_table(RADIX, k_rows, RADIX)
    first = jnp.concatenate(
        [
            jnp.concatenate([cos_first, -sin_first], axis=1),
            jnp.concatenate([sin_first, cos_first], axis=1),
        ],
        axis=0,
    )
    cos_twist, sin_twist = angle_table(RADIX, RADIX, RADIX * RADIX)
    cos_out, sin_out = angle_table(RADIX, RADIX, RADIX)
    real_cols = jnp.concatenate([cos_out, -sin_out], axis=0)
    imag_cols = jnp.concatenate([sin_out, cos_out], axis=0)
    second = jnp.concatenate([real_cols[:, half_radix:], imag_cols[:, half_radix:]], axis=1)
    first_high, first_low = table_pair(first)
    second_high, second_low = table_pair(second)
    return first_high, first_low, cos_twist, sin_twist, second_high, second_low


def peaks_kernel(spec_ref, bank_ref, fh_ref, fl_ref, tc_ref, ts_ref, sh_ref, sl_ref, out_ref):
    half_radix = RADIX // 2
    block_total = spec_ref.shape[0]
    step_templates = bank_ref.shape[0]
    pair_total = step_templates * block_total
    products = []
    scales = []
    for template in range(step_templates):
        wave_real = bank_ref[template, 0].astype(jnp.float32)
        wave_imag = bank_ref[template, 1].astype(jnp.float32)
        power_sum = jnp.sum(wave_real * wave_real + wave_imag * wave_imag, keepdims=True)
        norm_scale = 1.0 / jnp.sqrt(BLOCK * power_sum + EPSILON)
        scales.append(norm_scale * norm_scale)
        for block in range(block_total):
            spec_real = spec_ref[block, :, :RADIX]
            spec_imag = spec_ref[block, :, RADIX:]
            prod_real = spec_real * wave_real + spec_imag * wave_imag
            prod_imag = spec_imag * wave_real - spec_real * wave_imag
            products.append(jnp.concatenate([prod_real, prod_imag], axis=0))
    stacked = jnp.concatenate(products, axis=1)
    stacked_high, stacked_low = split_pair(stacked)
    first = triple_dot(fh_ref[...], fl_ref[...], stacked_high, stacked_low)
    cos_twist = tc_ref[...]
    sin_twist = ts_ref[...]
    turned_rows = []
    for pair in range(pair_total):
        real_part = first[:RADIX, pair * RADIX : (pair + 1) * RADIX]
        imag_part = first[RADIX:, pair * RADIX : (pair + 1) * RADIX]
        turned_rows.append(
            jnp.concatenate(
                [
                    real_part * cos_twist - imag_part * sin_twist,
                    real_part * sin_twist + imag_part * cos_twist,
                ],
                axis=1,
            )
        )
    turned = jnp.concatenate(turned_rows, axis=0)
    turned_high, turned_low = split_pair(turned)
    series = triple_dot(turned_high, turned_low, sh_ref[...], sl_ref[...])
    power_series = (
        series[:, :half_radix] * series[:, :half_radix]
        + series[:, half_radix:] * series[:, half_radix:]
    )
    peaks = jnp.max(power_series.reshape(pair_total, RADIX, half_radix), axis=1)
    for template in range(step_templates):
        rows = peaks[template * block_total : (template + 1) * block_total]
        out_ref[template] = rows * scales[template]


def window_peaks(spectra, bank, tables):
    block_total, k_rows, _ = spectra.shape
    template_total = bank.shape[0]
    step_templates = STEP_TEMPLATES if template_total % STEP_TEMPLATES == 0 else 1
    fixed = lambda k: (0, 0)
    pair_flops = 6 * (2 * RADIX) * (2 * k_rows) * RADIX + 6 * RADIX * (2 * RADIX) * RADIX
    return pl.pallas_call(
        peaks_kernel,
        out_shape=jax.ShapeDtypeStruct((template_total, block_total, RADIX // 2), jnp.float32),
        grid=(template_total // step_templates,),
        in_specs=[
            pl.BlockSpec((block_total, k_rows, 2 * RADIX), lambda k: (0, 0, 0)),
            pl.BlockSpec((step_templates, 2, k_rows, RADIX), lambda k: (k, 0, 0, 0)),
            pl.BlockSpec((2 * RADIX, 2 * k_rows), fixed),
            pl.BlockSpec((2 * RADIX, 2 * k_rows), fixed),
            pl.BlockSpec((RADIX, RADIX), fixed),
            pl.BlockSpec((RADIX, RADIX), fixed),
            pl.BlockSpec((2 * RADIX, RADIX), fixed),
            pl.BlockSpec((2 * RADIX, RADIX), fixed),
        ],
        out_specs=pl.BlockSpec((step_templates, block_total, RADIX // 2), lambda k: (k, 0, 0)),
        compiler_params=pltpu.CompilerParams(dimension_semantics=("arbitrary",)),
        cost_estimate=pl.CostEstimate(
            flops=pair_flops * template_total * block_total,
            transcendentals=0,
            bytes_accessed=spectra.size * 4 + bank.size * 2 + template_total * block_total * RADIX * 2,
        ),
    )(spectra, bank, *tables)


def gathered_bank(bank_rows):
    seg_total = lax.axis_size("seg")
    me = lax.axis_index("seg")
    rows, parts, local_bins = bank_rows.shape
    held = bank_rows[None]
    distance = seg_total // 2
    steps = 0
    while distance >= 1:
        pairs = [(i, i ^ distance) for i in range(seg_total)]
        arrived = lax.ppermute(held, "seg", pairs)
        upper = (me & distance) != 0
        held = jnp.stack([jnp.where(upper, arrived, held), jnp.where(upper, held, arrived)], axis=0)
        distance //= 2
        steps += 1
    held = held.reshape((2,) * steps + (rows, parts, local_bins // RADIX, RADIX))
    order = tuple(reversed(range(steps)))
    held = jnp.transpose(held, (steps, steps + 1) + order + (steps + 2, steps + 3))
    return held.reshape(rows, parts, seg_total * local_bins // RADIX, RADIX)


def local(strain, gate_mask, template_bank):
    gated = strain * gate_mask.astype(jnp.float32)
    local_blocks = gated.reshape(-1, BLOCK)
    block_total = local_blocks.shape[0]
    earlier = passed_along(local_blocks[block_total - 1], "seg", 1)
    before = jnp.concatenate([earlier[None], local_blocks[:-1]], axis=0)
    windows = jnp.concatenate([before, local_blocks], axis=1)
    spectra = forward(windows)
    tables = inverse_tables(spectra.shape[1])
    template_total = template_bank.shape[0]
    results = []
    for start in range(0, template_total, SUBBANK):
        bank = gathered_bank(template_bank[start : start + SUBBANK])
        peaks = window_peaks(spectra, bank, tables)
        results.append(peaks.reshape(bank.shape[0], block_total * (RADIX // 2)))
    return jnp.concatenate(results, axis=0)


def solution(mesh):
    in_specs = (P(("grp", "seg")), P(("grp", "seg")), P("grp", None, "seg"))
    out_specs = P(None, ("grp", "seg"))
    return jax.shard_map(local, mesh=mesh, in_specs=in_specs, out_specs=out_specs, check_vma=False)
```

```python
import math

import jax
import numpy as np
import jax.numpy as jnp
from jax import lax
from jax.experimental import pallas as pl
from jax.experimental.pallas import tpu as pltpu
from jax.sharding import PartitionSpec as P

RADIX = 256
BLOCK = 32768
SUBBANK = 8
STEP_TEMPLATES = 2


PRECISE = lax.Precision.HIGH
EPSILON = 1e-06


def passed_along(value, axis, by):
    count = lax.axis_size(axis)
    pairs = [(i, i + by) for i in range(count) if 0 <= i + by < count]
    return lax.ppermute(value, axis, pairs)


def angle_table(row_count, col_count, period):
    row_index = lax.broadcasted_iota(jnp.int32, (row_count, col_count), 0)
    col_index = lax.broadcasted_iota(jnp.int32, (row_count, col_count), 1)
    phase_step = row_index * col_index % period
    angle_value = phase_step.astype(jnp.float32) * (2.0 * math.pi / period)
    return (jnp.cos(angle_value), jnp.sin(angle_value))


def forward(windows):
    half_radix = RADIX // 2
    window_total = windows.shape[0]
    rows = windows.shape[1] // RADIX
    block_grid = windows.reshape(window_total, rows, RADIX)
    cos_first, sin_first = angle_table(rows, RADIX, RADIX)
    first_table = jnp.concatenate([cos_first, -sin_first], axis=1)
    first_section = jnp.einsum("bnm,nf->bmf", block_grid, first_table, precision=PRECISE)
    cos_twist, sin_twist = angle_table(RADIX, RADIX, RADIX * RADIX)
    real_part = first_section[..., :RADIX]
    imag_part = first_section[..., RADIX:]
    turned = jnp.concatenate(
        [
            real_part * cos_twist + imag_part * sin_twist,
            imag_part * cos_twist - real_part * sin_twist,
        ],
        axis=-1,
    )
    cos_second, sin_second = angle_table(RADIX, half_radix, RADIX)
    cosine_part = jnp.einsum("bnf,nk->bkf", turned, cos_second, precision=PRECISE)
    sine_part = jnp.einsum("bnf,nk->bkf", turned, sin_second, precision=PRECISE)
    return jnp.concatenate(
        [
            cosine_part[..., :RADIX] + sine_part[..., RADIX:],
            cosine_part[..., RADIX:] - sine_part[..., :RADIX],
        ],
        axis=-1,
    )


def split_pair(value):
    high = value.astype(jnp.bfloat16)
    low = (value - high.astype(jnp.float32)).astype(jnp.bfloat16)
    return high, low


def table_pair(value):
    high = lax.reduce_precision(value, exponent_bits=8, mantissa_bits=7)
    return high.astype(jnp.bfloat16), (value - high).astype(jnp.bfloat16)


def triple_dot(left_high, left_low, right_high, right_low):
    total = jnp.dot(left_high, right_high, preferred_element_type=jnp.float32)
    total = total + jnp.dot(left_high, right_low, preferred_element_type=jnp.float32)
    return total + jnp.dot(left_low, right_high, preferred_element_type=jnp.float32)


def inverse_tables(k_order):
    half_radix = RADIX // 2
    t_index = lax.broadcasted_iota(jnp.int32, (RADIX, k_order.shape[0]), 0)
    first_angle = (t_index * k_order[None, :] % RADIX).astype(jnp.float32) * (2.0 * math.pi / RADIX)
    cos_first, sin_first = jnp.cos(first_angle), jnp.sin(first_angle)
    first = jnp.concatenate(
        [
            jnp.concatenate([cos_first, -sin_first], axis=1),
            jnp.concatenate([sin_first, cos_first], axis=1),
        ],
        axis=0,
    )
    cos_twist, sin_twist = angle_table(RADIX, RADIX, RADIX * RADIX)
    cos_out, sin_out = angle_table(RADIX, RADIX, RADIX)
    real_cols = jnp.concatenate([cos_out, -sin_out], axis=0)
    imag_cols = jnp.concatenate([sin_out, cos_out], axis=0)
    second = jnp.concatenate([real_cols[:, half_radix:], imag_cols[:, half_radix:]], axis=1)
    first_high, first_low = table_pair(first)
    second_high, second_low = table_pair(second)
    return first_high, first_low, cos_twist, sin_twist, second_high, second_low


def peaks_kernel(spec_ref, bank_ref, fh_ref, fl_ref, tc_ref, ts_ref, sh_ref, sl_ref, out_ref):
    half_radix = RADIX // 2
    block_total = spec_ref.shape[0]
    step_templates = bank_ref.shape[1]
    pair_total = step_templates * block_total
    products = []
    scales = []
    for template in range(step_templates):
        wave_real = bank_ref[:, template, 0].astype(jnp.float32).reshape(-1, RADIX)
        wave_imag = bank_ref[:, template, 1].astype(jnp.float32).reshape(-1, RADIX)
        power_sum = jnp.sum(wave_real * wave_real + wave_imag * wave_imag, keepdims=True)
        norm_scale = 1.0 / jnp.sqrt(BLOCK * power_sum + EPSILON)
        scales.append(norm_scale * norm_scale)
        for block in range(block_total):
            spec_real = spec_ref[block, :, :RADIX]
            spec_imag = spec_ref[block, :, RADIX:]
            prod_real = spec_real * wave_real + spec_imag * wave_imag
            prod_imag = spec_imag * wave_real - spec_real * wave_imag
            products.append(jnp.concatenate([prod_real, prod_imag], axis=0))
    stacked = jnp.concatenate(products, axis=1)
    stacked_high, stacked_low = split_pair(stacked)
    first = triple_dot(fh_ref[...], fl_ref[...], stacked_high, stacked_low)
    cos_twist = tc_ref[...]
    sin_twist = ts_ref[...]
    turned_rows = []
    for pair in range(pair_total):
        real_part = first[:RADIX, pair * RADIX : (pair + 1) * RADIX]
        imag_part = first[RADIX:, pair * RADIX : (pair + 1) * RADIX]
        turned_rows.append(
            jnp.concatenate(
                [
                    real_part * cos_twist - imag_part * sin_twist,
                    real_part * sin_twist + imag_part * cos_twist,
                ],
                axis=1,
            )
        )
    turned = jnp.concatenate(turned_rows, axis=0)
    turned_high, turned_low = split_pair(turned)
    series = triple_dot(turned_high, turned_low, sh_ref[...], sl_ref[...])
    power_series = (
        series[:, :half_radix] * series[:, :half_radix]
        + series[:, half_radix:] * series[:, half_radix:]
    )
    peaks = jnp.max(power_series.reshape(pair_total, RADIX, half_radix), axis=1)
    for template in range(step_templates):
        rows = peaks[template * block_total : (template + 1) * block_total]
        out_ref[template] = rows * scales[template]


def window_peaks(spectra, bank, tables):
    block_total, k_rows, _ = spectra.shape
    template_total = bank.shape[1]
    bank_block = (bank.shape[0], STEP_TEMPLATES) + bank.shape[2:]
    bank_map = lambda k: (0, k) + (0,) * (bank.ndim - 2)
    step_templates = STEP_TEMPLATES
    fixed = lambda k: (0, 0)
    pair_flops = 6 * (2 * RADIX) * (2 * k_rows) * RADIX + 6 * RADIX * (2 * RADIX) * RADIX
    return pl.pallas_call(
        peaks_kernel,
        out_shape=jax.ShapeDtypeStruct((template_total, block_total, RADIX // 2), jnp.float32),
        grid=(template_total // step_templates,),
        in_specs=[
            pl.BlockSpec((block_total, k_rows, 2 * RADIX), lambda k: (0, 0, 0)),
            pl.BlockSpec(bank_block, bank_map),
            pl.BlockSpec((2 * RADIX, 2 * k_rows), fixed),
            pl.BlockSpec((2 * RADIX, 2 * k_rows), fixed),
            pl.BlockSpec((RADIX, RADIX), fixed),
            pl.BlockSpec((RADIX, RADIX), fixed),
            pl.BlockSpec((2 * RADIX, RADIX), fixed),
            pl.BlockSpec((2 * RADIX, RADIX), fixed),
        ],
        out_specs=pl.BlockSpec((step_templates, block_total, RADIX // 2), lambda k: (k, 0, 0)),
        compiler_params=pltpu.CompilerParams(dimension_semantics=("arbitrary",)),
        cost_estimate=pl.CostEstimate(
            flops=pair_flops * template_total * block_total,
            transcendentals=0,
            bytes_accessed=spectra.size * 4 + bank.size * 2 + template_total * block_total * RADIX * 2,
        ),
    )(spectra, bank, *tables)


def chain_groups(seg_total):
    distances = []
    distance = seg_total // 2
    while distance >= 1:
        distances.append(distance)
        distance //= 2
    inter = distances[:-1]
    return [tuple(inter[i : i + 2]) for i in range(0, len(inter), 2)] + [tuple(distances[-1:])]


def group_offsets(group):
    offsets = []
    for position in range(2 ** len(group)):
        bits = [(position >> (len(group) - 1 - j)) & 1 for j in range(len(group))]
        offsets.append(sum(bit * distance for bit, distance in zip(bits, group)))
    return offsets


def piece_offsets(seg_total):
    offsets = np.zeros((1,), np.int32)
    for group in chain_groups(seg_total):
        offsets = (np.array(group_offsets(group), np.int32)[:, None] ^ offsets[None, :]).reshape(-1)
    return offsets


def gathered_bank(bank_rows):
    seg_total = lax.axis_size("seg")
    rows, parts, local_bins = bank_rows.shape
    held = bank_rows
    for group in chain_groups(seg_total):
        arrived = [held]
        for offset in group_offsets(group)[1:]:
            pairs = [(i, i ^ offset) for i in range(seg_total)]
            arrived.append(lax.ppermute(held, "seg", pairs))
        held = jnp.stack(arrived, axis=0)
    piece_rows = local_bins // RADIX
    if piece_rows == 1:
        return held.reshape(seg_total, rows, parts, RADIX)
    return held.reshape(seg_total, rows, parts, piece_rows, RADIX)


def local(strain, gate_mask, template_bank):
    gated = strain * gate_mask.astype(jnp.float32)
    local_blocks = gated.reshape(-1, BLOCK)
    block_total = local_blocks.shape[0]
    earlier = passed_along(local_blocks[block_total - 1], "seg", 1)
    before = jnp.concatenate([earlier[None], local_blocks[:-1]], axis=0)
    windows = jnp.concatenate([before, local_blocks], axis=1)
    spectra = forward(windows)
    seg_total = lax.axis_size("seg")
    source = lax.axis_index("seg") ^ jnp.asarray(piece_offsets(seg_total))
    piece_rows = spectra.shape[1] // seg_total
    k_order = (source[:, None] * piece_rows + jnp.arange(piece_rows, dtype=jnp.int32)[None, :]).reshape(-1)
    spectra = jnp.take(spectra, k_order, axis=1)
    tables = inverse_tables(k_order)
    template_total = template_bank.shape[0]
    results = []
    for start in range(0, template_total, SUBBANK):
        bank = gathered_bank(template_bank[start : start + SUBBANK])
        peaks = window_peaks(spectra, bank, tables)
        results.append(peaks.reshape(bank.shape[1], block_total * (RADIX // 2)))
    return jnp.concatenate(results, axis=0)


def solution(mesh):
    in_specs = (P(("grp", "seg")), P(("grp", "seg")), P("grp", None, "seg"))
    out_specs = P(None, ("grp", "seg"))
    return jax.shard_map(local, mesh=mesh, in_specs=in_specs, out_specs=out_specs, check_vma=False)
```

```python
import math

import jax
import jax.numpy as jnp
from jax import lax
from jax.experimental import pallas as pl
from jax.experimental.pallas import tpu as pltpu
from jax.sharding import PartitionSpec as P

RADIX = 256
BLOCK = 32768
SUBBANK = 8
STEP_TEMPLATES = 2


PRECISE = lax.Precision.HIGH
EPSILON = 1e-06


def passed_along(value, axis, by):
    count = lax.axis_size(axis)
    pairs = [(i, i + by) for i in range(count) if 0 <= i + by < count]
    return lax.ppermute(value, axis, pairs)


def angle_table(row_count, col_count, period):
    row_index = lax.broadcasted_iota(jnp.int32, (row_count, col_count), 0)
    col_index = lax.broadcasted_iota(jnp.int32, (row_count, col_count), 1)
    phase_step = row_index * col_index % period
    angle_value = phase_step.astype(jnp.float32) * (2.0 * math.pi / period)
    return (jnp.cos(angle_value), jnp.sin(angle_value))


def forward(windows):
    half_radix = RADIX // 2
    window_total = windows.shape[0]
    rows = windows.shape[1] // RADIX
    block_grid = windows.reshape(window_total, rows, RADIX)
    cos_first, sin_first = angle_table(rows, RADIX, RADIX)
    first_table = jnp.concatenate([cos_first, -sin_first], axis=1)
    first_section = jnp.einsum("bnm,nf->bmf", block_grid, first_table, precision=PRECISE)
    cos_twist, sin_twist = angle_table(RADIX, RADIX, RADIX * RADIX)
    real_part = first_section[..., :RADIX]
    imag_part = first_section[..., RADIX:]
    turned = jnp.concatenate(
        [
            real_part * cos_twist + imag_part * sin_twist,
            imag_part * cos_twist - real_part * sin_twist,
        ],
        axis=-1,
    )
    cos_second, sin_second = angle_table(RADIX, half_radix, RADIX)
    cosine_part = jnp.einsum("bnf,nk->bkf", turned, cos_second, precision=PRECISE)
    sine_part = jnp.einsum("bnf,nk->bkf", turned, sin_second, precision=PRECISE)
    return jnp.concatenate(
        [
            cosine_part[..., :RADIX] + sine_part[..., RADIX:],
            cosine_part[..., RADIX:] - sine_part[..., :RADIX],
        ],
        axis=-1,
    )


def split_pair(value):
    high = value.astype(jnp.bfloat16)
    low = (value - high.astype(jnp.float32)).astype(jnp.bfloat16)
    return high, low


def table_pair(value):
    high = lax.reduce_precision(value, exponent_bits=8, mantissa_bits=7)
    return high.astype(jnp.bfloat16), (value - high).astype(jnp.bfloat16)


def triple_dot(left_high, left_low, right_high, right_low):
    total = jnp.dot(left_high, right_high, preferred_element_type=jnp.float32)
    total = total + jnp.dot(left_high, right_low, preferred_element_type=jnp.float32)
    return total + jnp.dot(left_low, right_high, preferred_element_type=jnp.float32)


def inverse_tables(k_rows):
    half_radix = RADIX // 2
    cos_first, sin_first = angle_table(RADIX, k_rows, RADIX)
    first = jnp.concatenate(
        [
            jnp.concatenate([cos_first, -sin_first], axis=1),
            jnp.concatenate([sin_first, cos_first], axis=1),
        ],
        axis=0,
    )
    cos_twist, sin_twist = angle_table(RADIX, RADIX, RADIX * RADIX)
    cos_out, sin_out = angle_table(RADIX, RADIX, RADIX)
    real_cols = jnp.concatenate([cos_out, -sin_out], axis=0)
    imag_cols = jnp.concatenate([sin_out, cos_out], axis=0)
    second = jnp.concatenate([real_cols[:, half_radix:], imag_cols[:, half_radix:]], axis=1)
    first_high, first_low = table_pair(first)
    second_high, second_low = table_pair(second)
    return first_high, first_low, cos_twist, sin_twist, second_high, second_low


def peaks_kernel(spec_ref, bank_ref, fh_ref, fl_ref, tc_ref, ts_ref, sh_ref, sl_ref, out_ref):
    half_radix = RADIX // 2
    block_total = spec_ref.shape[0]
    step_templates = bank_ref.shape[0]
    pair_total = step_templates * block_total
    products = []
    scales = []
    for template in range(step_templates):
        wave_real = bank_ref[template, 0].astype(jnp.float32)
        wave_imag = bank_ref[template, 1].astype(jnp.float32)
        power_sum = jnp.sum(wave_real * wave_real + wave_imag * wave_imag, keepdims=True)
        norm_scale = 1.0 / jnp.sqrt(BLOCK * power_sum + EPSILON)
        scales.append(norm_scale * norm_scale)
        for block in range(block_total):
            spec_real = spec_ref[block, :, :RADIX]
            spec_imag = spec_ref[block, :, RADIX:]
            prod_real = spec_real * wave_real + spec_imag * wave_imag
            prod_imag = spec_imag * wave_real - spec_real * wave_imag
            products.append(jnp.concatenate([prod_real, prod_imag], axis=0))
    stacked = jnp.concatenate(products, axis=1)
    stacked_high, stacked_low = split_pair(stacked)
    first = triple_dot(fh_ref[...], fl_ref[...], stacked_high, stacked_low)
    cos_twist = tc_ref[...]
    sin_twist = ts_ref[...]
    turned_rows = []
    for pair in range(pair_total):
        real_part = first[:RADIX, pair * RADIX : (pair + 1) * RADIX]
        imag_part = first[RADIX:, pair * RADIX : (pair + 1) * RADIX]
        turned_rows.append(
            jnp.concatenate(
                [
                    real_part * cos_twist - imag_part * sin_twist,
                    real_part * sin_twist + imag_part * cos_twist,
                ],
                axis=1,
            )
        )
    turned = jnp.concatenate(turned_rows, axis=0)
    turned_high, turned_low = split_pair(turned)
    series = triple_dot(turned_high, turned_low, sh_ref[...], sl_ref[...])
    power_series = (
        series[:, :half_radix] * series[:, :half_radix]
        + series[:, half_radix:] * series[:, half_radix:]
    )
    peaks = jnp.max(power_series.reshape(pair_total, RADIX, half_radix), axis=1)
    for template in range(step_templates):
        rows = peaks[template * block_total : (template + 1) * block_total]
        out_ref[template] = rows * scales[template]


def window_peaks(spectra, bank, tables):
    block_total, k_rows, _ = spectra.shape
    template_total = bank.shape[0]
    step_templates = STEP_TEMPLATES if template_total % STEP_TEMPLATES == 0 else 1
    fixed = lambda k: (0, 0)
    pair_flops = 6 * (2 * RADIX) * (2 * k_rows) * RADIX + 6 * RADIX * (2 * RADIX) * RADIX
    return pl.pallas_call(
        peaks_kernel,
        out_shape=jax.ShapeDtypeStruct((template_total, block_total, RADIX // 2), jnp.float32),
        grid=(template_total // step_templates,),
        in_specs=[
            pl.BlockSpec((block_total, k_rows, 2 * RADIX), lambda k: (0, 0, 0)),
            pl.BlockSpec((step_templates, 2, k_rows, RADIX), lambda k: (k, 0, 0, 0)),
            pl.BlockSpec((2 * RADIX, 2 * k_rows), fixed),
            pl.BlockSpec((2 * RADIX, 2 * k_rows), fixed),
            pl.BlockSpec((RADIX, RADIX), fixed),
            pl.BlockSpec((RADIX, RADIX), fixed),
            pl.BlockSpec((2 * RADIX, RADIX), fixed),
            pl.BlockSpec((2 * RADIX, RADIX), fixed),
        ],
        out_specs=pl.BlockSpec((step_templates, block_total, RADIX // 2), lambda k: (k, 0, 0)),
        compiler_params=pltpu.CompilerParams(dimension_semantics=("arbitrary",)),
        cost_estimate=pl.CostEstimate(
            flops=pair_flops * template_total * block_total,
            transcendentals=0,
            bytes_accessed=spectra.size * 4 + bank.size * 2 + template_total * block_total * RADIX * 2,
        ),
    )(spectra, bank, *tables)


def gathered_bank(bank_rows):
    seg_total = lax.axis_size("seg")
    me = lax.axis_index("seg")
    rows, parts, local_bins = bank_rows.shape
    held = bank_rows[None]
    distance = seg_total // 2
    steps = 0
    while distance >= 1:
        pairs = [(i, i ^ distance) for i in range(seg_total)]
        arrived = lax.ppermute(held, "seg", pairs)
        upper = (me & distance) != 0
        held = jnp.stack([jnp.where(upper, arrived, held), jnp.where(upper, held, arrived)], axis=0)
        distance //= 2
        steps += 1
    held = held.reshape((2,) * steps + (rows, parts, local_bins // RADIX, RADIX))
    order = tuple(reversed(range(steps)))
    held = jnp.transpose(held, (steps, steps + 1) + order + (steps + 2, steps + 3))
    return held.reshape(rows, parts, seg_total * local_bins // RADIX, RADIX)


def offloaded_bank(bank_rows):
    seg_total = lax.axis_size("seg")
    rows, parts, local_bins = bank_rows.shape
    flat = bank_rows.reshape(1, rows * parts * local_bins)
    every = lax.all_gather(flat, "seg", axis=0, tiled=True)
    every = every.reshape(seg_total, rows, parts, local_bins // RADIX, RADIX)
    every = jnp.transpose(every, (1, 2, 0, 3, 4))
    return every.reshape(rows, parts, seg_total * local_bins // RADIX, RADIX)


def local(strain, gate_mask, template_bank):
    gated = strain * gate_mask.astype(jnp.float32)
    local_blocks = gated.reshape(-1, BLOCK)
    block_total = local_blocks.shape[0]
    earlier = passed_along(local_blocks[block_total - 1], "seg", 1)
    before = jnp.concatenate([earlier[None], local_blocks[:-1]], axis=0)
    windows = jnp.concatenate([before, local_blocks], axis=1)
    spectra = forward(windows)
    tables = inverse_tables(spectra.shape[1])
    template_total = template_bank.shape[0]
    results = []
    for start in range(0, template_total, SUBBANK):
        rows = template_bank[start : start + SUBBANK]
        bank = offloaded_bank(rows) if start == 0 else gathered_bank(rows)
        peaks = window_peaks(spectra, bank, tables)
        results.append(peaks.reshape(bank.shape[0], block_total * (RADIX // 2)))
    return jnp.concatenate(results, axis=0)


def solution(mesh):
    in_specs = (P(("grp", "seg")), P(("grp", "seg")), P("grp", None, "seg"))
    out_specs = P(None, ("grp", "seg"))
    return jax.shard_map(local, mesh=mesh, in_specs=in_specs, out_specs=out_specs, check_vma=False)
```

```python
import math

import jax
import numpy as np
import jax.numpy as jnp
from jax import lax
from jax.experimental import pallas as pl
from jax.experimental.pallas import tpu as pltpu
from jax.sharding import PartitionSpec as P

RADIX = 256
BLOCK = 32768
SUBBANK = 8
STEP_TEMPLATES = 2


PRECISE = lax.Precision.HIGH
EPSILON = 1e-06


def passed_along(value, axis, by):
    count = lax.axis_size(axis)
    pairs = [(i, i + by) for i in range(count) if 0 <= i + by < count]
    return lax.ppermute(value, axis, pairs)


def angle_table(row_count, col_count, period):
    row_index = lax.broadcasted_iota(jnp.int32, (row_count, col_count), 0)
    col_index = lax.broadcasted_iota(jnp.int32, (row_count, col_count), 1)
    phase_step = row_index * col_index % period
    angle_value = phase_step.astype(jnp.float32) * (2.0 * math.pi / period)
    return (jnp.cos(angle_value), jnp.sin(angle_value))


def forward(windows):
    half_radix = RADIX // 2
    window_total = windows.shape[0]
    rows = windows.shape[1] // RADIX
    block_grid = windows.reshape(window_total, rows, RADIX)
    cos_first, sin_first = angle_table(rows, RADIX, RADIX)
    first_table = jnp.concatenate([cos_first, -sin_first], axis=1)
    first_section = jnp.einsum("bnm,nf->bmf", block_grid, first_table, precision=PRECISE)
    cos_twist, sin_twist = angle_table(RADIX, RADIX, RADIX * RADIX)
    real_part = first_section[..., :RADIX]
    imag_part = first_section[..., RADIX:]
    turned = jnp.concatenate(
        [
            real_part * cos_twist + imag_part * sin_twist,
            imag_part * cos_twist - real_part * sin_twist,
        ],
        axis=-1,
    )
    cos_second, sin_second = angle_table(RADIX, half_radix, RADIX)
    cosine_part = jnp.einsum("bnf,nk->bkf", turned, cos_second, precision=PRECISE)
    sine_part = jnp.einsum("bnf,nk->bkf", turned, sin_second, precision=PRECISE)
    return jnp.concatenate(
        [
            cosine_part[..., :RADIX] + sine_part[..., RADIX:],
            cosine_part[..., RADIX:] - sine_part[..., :RADIX],
        ],
        axis=-1,
    )


def split_pair(value):
    high = value.astype(jnp.bfloat16)
    low = (value - high.astype(jnp.float32)).astype(jnp.bfloat16)
    return high, low


def table_pair(value):
    high = lax.reduce_precision(value, exponent_bits=8, mantissa_bits=7)
    return high.astype(jnp.bfloat16), (value - high).astype(jnp.bfloat16)


def triple_dot(left_high, left_low, right_high, right_low):
    total = jnp.dot(left_high, right_high, preferred_element_type=jnp.float32)
    total = total + jnp.dot(left_high, right_low, preferred_element_type=jnp.float32)
    return total + jnp.dot(left_low, right_high, preferred_element_type=jnp.float32)


def inverse_tables(k_order):
    half_radix = RADIX // 2
    t_index = lax.broadcasted_iota(jnp.int32, (RADIX, k_order.shape[0]), 0)
    first_angle = (t_index * k_order[None, :] % RADIX).astype(jnp.float32) * (2.0 * math.pi / RADIX)
    cos_first, sin_first = jnp.cos(first_angle), jnp.sin(first_angle)
    first = jnp.concatenate(
        [
            jnp.concatenate([cos_first, -sin_first], axis=1),
            jnp.concatenate([sin_first, cos_first], axis=1),
        ],
        axis=0,
    )
    cos_twist, sin_twist = angle_table(RADIX, RADIX, RADIX * RADIX)
    cos_out, sin_out = angle_table(RADIX, RADIX, RADIX)
    real_cols = jnp.concatenate([cos_out, -sin_out], axis=0)
    imag_cols = jnp.concatenate([sin_out, cos_out], axis=0)
    second = jnp.concatenate([real_cols[:, half_radix:], imag_cols[:, half_radix:]], axis=1)
    first_high, first_low = table_pair(first)
    second_high, second_low = table_pair(second)
    return first_high, first_low, cos_twist, sin_twist, second_high, second_low


def peaks_kernel(spec_ref, bank_ref, fh_ref, fl_ref, tc_ref, ts_ref, sh_ref, sl_ref, out_ref):
    half_radix = RADIX // 2
    block_total = spec_ref.shape[0]
    step_templates = bank_ref.shape[0]
    pair_total = step_templates * block_total
    products = []
    scales = []
    for template in range(step_templates):
        wave_real = bank_ref[template, 0].astype(jnp.float32)
        wave_imag = bank_ref[template, 1].astype(jnp.float32)
        power_sum = jnp.sum(wave_real * wave_real + wave_imag * wave_imag, keepdims=True)
        norm_scale = 1.0 / jnp.sqrt(BLOCK * power_sum + EPSILON)
        scales.append(norm_scale * norm_scale)
        for block in range(block_total):
            spec_real = spec_ref[block, :, :RADIX]
            spec_imag = spec_ref[block, :, RADIX:]
            prod_real = spec_real * wave_real + spec_imag * wave_imag
            prod_imag = spec_imag * wave_real - spec_real * wave_imag
            products.append(jnp.concatenate([prod_real, prod_imag], axis=0))
    stacked = jnp.concatenate(products, axis=1)
    stacked_high, stacked_low = split_pair(stacked)
    first = triple_dot(fh_ref[...], fl_ref[...], stacked_high, stacked_low)
    cos_twist = tc_ref[...]
    sin_twist = ts_ref[...]
    turned_rows = []
    for pair in range(pair_total):
        real_part = first[:RADIX, pair * RADIX : (pair + 1) * RADIX]
        imag_part = first[RADIX:, pair * RADIX : (pair + 1) * RADIX]
        turned_rows.append(
            jnp.concatenate(
                [
                    real_part * cos_twist - imag_part * sin_twist,
                    real_part * sin_twist + imag_part * cos_twist,
                ],
                axis=1,
            )
        )
    turned = jnp.concatenate(turned_rows, axis=0)
    turned_high, turned_low = split_pair(turned)
    series = triple_dot(turned_high, turned_low, sh_ref[...], sl_ref[...])
    power_series = (
        series[:, :half_radix] * series[:, :half_radix]
        + series[:, half_radix:] * series[:, half_radix:]
    )
    peaks = jnp.max(power_series.reshape(pair_total, RADIX, half_radix), axis=1)
    for template in range(step_templates):
        rows = peaks[template * block_total : (template + 1) * block_total]
        out_ref[template] = rows * scales[template]


def window_peaks(spectra, bank, tables):
    block_total, k_rows, _ = spectra.shape
    template_total = bank.shape[0]
    bank_block = (STEP_TEMPLATES, 2, k_rows, RADIX)
    bank_map = lambda k: (k, 0, 0, 0)
    step_templates = STEP_TEMPLATES
    fixed = lambda k: (0, 0)
    pair_flops = 6 * (2 * RADIX) * (2 * k_rows) * RADIX + 6 * RADIX * (2 * RADIX) * RADIX
    return pl.pallas_call(
        peaks_kernel,
        out_shape=jax.ShapeDtypeStruct((template_total, block_total, RADIX // 2), jnp.float32),
        grid=(template_total // step_templates,),
        in_specs=[
            pl.BlockSpec((block_total, k_rows, 2 * RADIX), lambda k: (0, 0, 0)),
            pl.BlockSpec(bank_block, bank_map),
            pl.BlockSpec((2 * RADIX, 2 * k_rows), fixed),
            pl.BlockSpec((2 * RADIX, 2 * k_rows), fixed),
            pl.BlockSpec((RADIX, RADIX), fixed),
            pl.BlockSpec((RADIX, RADIX), fixed),
            pl.BlockSpec((2 * RADIX, RADIX), fixed),
            pl.BlockSpec((2 * RADIX, RADIX), fixed),
        ],
        out_specs=pl.BlockSpec((step_templates, block_total, RADIX // 2), lambda k: (k, 0, 0)),
        compiler_params=pltpu.CompilerParams(dimension_semantics=("arbitrary",)),
        cost_estimate=pl.CostEstimate(
            flops=pair_flops * template_total * block_total,
            transcendentals=0,
            bytes_accessed=spectra.size * 4 + bank.size * 2 + template_total * block_total * RADIX * 2,
        ),
    )(spectra, bank, *tables)


def chain_groups(seg_total):
    distances = []
    distance = seg_total // 2
    while distance >= 1:
        distances.append(distance)
        distance //= 2
    return [(distance,) for distance in distances]


def group_offsets(group):
    offsets = []
    for position in range(2 ** len(group)):
        bits = [(position >> (len(group) - 1 - j)) & 1 for j in range(len(group))]
        offsets.append(sum(bit * distance for bit, distance in zip(bits, group)))
    return offsets


def piece_offsets(seg_total):
    offsets = np.zeros((1,), np.int32)
    for group in chain_groups(seg_total):
        offsets = (np.array(group_offsets(group), np.int32)[:, None] ^ offsets[None, :]).reshape(-1)
    return offsets


def gathered_bank(bank_rows):
    seg_total = lax.axis_size("seg")
    rows, parts, local_bins = bank_rows.shape
    held = bank_rows
    for group in chain_groups(seg_total):
        arrived = [held]
        for offset in group_offsets(group)[1:]:
            pairs = [(i, i ^ offset) for i in range(seg_total)]
            arrived.append(lax.ppermute(held, "seg", pairs))
        held = jnp.stack(arrived, axis=0)
    held = held.reshape(seg_total, rows, parts, local_bins)
    return jnp.transpose(held, (1, 2, 0, 3)).reshape(rows, parts, seg_total * local_bins // RADIX, RADIX)


def local(strain, gate_mask, template_bank):
    gated = strain * gate_mask.astype(jnp.float32)
    local_blocks = gated.reshape(-1, BLOCK)
    block_total = local_blocks.shape[0]
    earlier = passed_along(local_blocks[block_total - 1], "seg", 1)
    before = jnp.concatenate([earlier[None], local_blocks[:-1]], axis=0)
    windows = jnp.concatenate([before, local_blocks], axis=1)
    spectra = forward(windows)
    seg_total = lax.axis_size("seg")
    source = lax.axis_index("seg") ^ jnp.asarray(piece_offsets(seg_total))
    piece_rows = spectra.shape[1] // seg_total
    k_order = (source[:, None] * piece_rows + jnp.arange(piece_rows, dtype=jnp.int32)[None, :]).reshape(-1)
    spectra = jnp.take(spectra, k_order, axis=1)
    tables = inverse_tables(k_order)
    template_total = template_bank.shape[0]
    results = []
    for start in range(0, template_total, SUBBANK):
        bank = gathered_bank(template_bank[start : start + SUBBANK])
        peaks = window_peaks(spectra, bank, tables)
        results.append(peaks.reshape(bank.shape[0], block_total * (RADIX // 2)))
    return jnp.concatenate(results, axis=0)


def solution(mesh):
    in_specs = (P(("grp", "seg")), P(("grp", "seg")), P("grp", None, "seg"))
    out_specs = P(None, ("grp", "seg"))
    return jax.shard_map(local, mesh=mesh, in_specs=in_specs, out_specs=out_specs, check_vma=False)
```

```python
import math

import jax
import jax.numpy as jnp
from jax import lax
from jax.experimental import pallas as pl
from jax.experimental.pallas import tpu as pltpu
from jax.sharding import PartitionSpec as P

RADIX = 256
BLOCK = 32768
SUBBANK = 8
STEP_TEMPLATES = 2


PRECISE = lax.Precision.HIGH
EPSILON = 1e-06


def passed_along(value, axis, by):
    count = lax.axis_size(axis)
    pairs = [(i, i + by) for i in range(count) if 0 <= i + by < count]
    return lax.ppermute(value, axis, pairs)


def angle_table(row_count, col_count, period):
    row_index = lax.broadcasted_iota(jnp.int32, (row_count, col_count), 0)
    col_index = lax.broadcasted_iota(jnp.int32, (row_count, col_count), 1)
    phase_step = row_index * col_index % period
    angle_value = phase_step.astype(jnp.float32) * (2.0 * math.pi / period)
    return (jnp.cos(angle_value), jnp.sin(angle_value))


def forward(windows):
    half_radix = RADIX // 2
    window_total = windows.shape[0]
    rows = windows.shape[1] // RADIX
    block_grid = windows.reshape(window_total, rows, RADIX)
    cos_first, sin_first = angle_table(rows, RADIX, RADIX)
    first_table = jnp.concatenate([cos_first, -sin_first], axis=1)
    first_section = jnp.einsum("bnm,nf->bmf", block_grid, first_table, precision=PRECISE)
    cos_twist, sin_twist = angle_table(RADIX, RADIX, RADIX * RADIX)
    real_part = first_section[..., :RADIX]
    imag_part = first_section[..., RADIX:]
    turned = jnp.concatenate(
        [
            real_part * cos_twist + imag_part * sin_twist,
            imag_part * cos_twist - real_part * sin_twist,
        ],
        axis=-1,
    )
    cos_second, sin_second = angle_table(RADIX, half_radix, RADIX)
    cosine_part = jnp.einsum("bnf,nk->bkf", turned, cos_second, precision=PRECISE)
    sine_part = jnp.einsum("bnf,nk->bkf", turned, sin_second, precision=PRECISE)
    return jnp.concatenate(
        [
            cosine_part[..., :RADIX] + sine_part[..., RADIX:],
            cosine_part[..., RADIX:] - sine_part[..., :RADIX],
        ],
        axis=-1,
    )


def split_pair(value):
    high = value.astype(jnp.bfloat16)
    low = (value - high.astype(jnp.float32)).astype(jnp.bfloat16)
    return high, low


def table_pair(value):
    high = lax.reduce_precision(value, exponent_bits=8, mantissa_bits=7)
    return high.astype(jnp.bfloat16), (value - high).astype(jnp.bfloat16)


def triple_dot(left_high, left_low, right_high, right_low):
    total = jnp.dot(left_high, right_high, preferred_element_type=jnp.float32)
    total = total + jnp.dot(left_high, right_low, preferred_element_type=jnp.float32)
    return total + jnp.dot(left_low, right_high, preferred_element_type=jnp.float32)


def inverse_tables(k_rows):
    half_radix = RADIX // 2
    cos_first, sin_first = angle_table(RADIX, k_rows, RADIX)
    first = jnp.concatenate(
        [
            jnp.concatenate([cos_first, -sin_first], axis=1),
            jnp.concatenate([sin_first, cos_first], axis=1),
        ],
        axis=0,
    )
    cos_twist, sin_twist = angle_table(RADIX, RADIX, RADIX * RADIX)
    cos_out, sin_out = angle_table(RADIX, RADIX, RADIX)
    real_cols = jnp.concatenate([cos_out, -sin_out], axis=0)
    imag_cols = jnp.concatenate([sin_out, cos_out], axis=0)
    second = jnp.concatenate([real_cols[:, half_radix:], imag_cols[:, half_radix:]], axis=1)
    first_high, first_low = table_pair(first)
    second_high, second_low = table_pair(second)
    return first_high, first_low, cos_twist, sin_twist, second_high, second_low


def peaks_kernel(spec_ref, bank_ref, fh_ref, fl_ref, tc_ref, ts_ref, sh_ref, sl_ref, out_ref):
    half_radix = RADIX // 2
    block_total = spec_ref.shape[0]
    step_templates = bank_ref.shape[0]
    pair_total = step_templates * block_total
    products = []
    scales = []
    for template in range(step_templates):
        wave_real = bank_ref[template, 0].astype(jnp.float32)
        wave_imag = bank_ref[template, 1].astype(jnp.float32)
        power_sum = jnp.sum(wave_real * wave_real + wave_imag * wave_imag, keepdims=True)
        norm_scale = 1.0 / jnp.sqrt(BLOCK * power_sum + EPSILON)
        scales.append(norm_scale * norm_scale)
        for block in range(block_total):
            spec_real = spec_ref[block, :, :RADIX]
            spec_imag = spec_ref[block, :, RADIX:]
            prod_real = spec_real * wave_real + spec_imag * wave_imag
            prod_imag = spec_imag * wave_real - spec_real * wave_imag
            products.append(jnp.concatenate([prod_real, prod_imag], axis=0))
    stacked = jnp.concatenate(products, axis=1)
    stacked_high, stacked_low = split_pair(stacked)
    first = triple_dot(fh_ref[...], fl_ref[...], stacked_high, stacked_low)
    cos_twist = tc_ref[...]
    sin_twist = ts_ref[...]
    turned_rows = []
    for pair in range(pair_total):
        real_part = first[:RADIX, pair * RADIX : (pair + 1) * RADIX]
        imag_part = first[RADIX:, pair * RADIX : (pair + 1) * RADIX]
        turned_rows.append(
            jnp.concatenate(
                [
                    real_part * cos_twist - imag_part * sin_twist,
                    real_part * sin_twist + imag_part * cos_twist,
                ],
                axis=1,
            )
        )
    turned = jnp.concatenate(turned_rows, axis=0)
    turned_high, turned_low = split_pair(turned)
    series = triple_dot(turned_high, turned_low, sh_ref[...], sl_ref[...])
    power_series = (
        series[:, :half_radix] * series[:, :half_radix]
        + series[:, half_radix:] * series[:, half_radix:]
    )
    peaks = jnp.max(power_series.reshape(pair_total, RADIX, half_radix), axis=1)
    for template in range(step_templates):
        rows = peaks[template * block_total : (template + 1) * block_total]
        out_ref[template] = rows * scales[template]


def window_peaks(spectra, bank, tables):
    block_total, k_rows, _ = spectra.shape
    template_total = bank.shape[0]
    step_templates = STEP_TEMPLATES if template_total % STEP_TEMPLATES == 0 else 1
    fixed = lambda k: (0, 0)
    pair_flops = 6 * (2 * RADIX) * (2 * k_rows) * RADIX + 6 * RADIX * (2 * RADIX) * RADIX
    return pl.pallas_call(
        peaks_kernel,
        out_shape=jax.ShapeDtypeStruct((template_total, block_total, RADIX // 2), jnp.float32),
        grid=(template_total // step_templates,),
        in_specs=[
            pl.BlockSpec((block_total, k_rows, 2 * RADIX), lambda k: (0, 0, 0)),
            pl.BlockSpec((step_templates, 2, k_rows, RADIX), lambda k: (k, 0, 0, 0)),
            pl.BlockSpec((2 * RADIX, 2 * k_rows), fixed),
            pl.BlockSpec((2 * RADIX, 2 * k_rows), fixed),
            pl.BlockSpec((RADIX, RADIX), fixed),
            pl.BlockSpec((RADIX, RADIX), fixed),
            pl.BlockSpec((2 * RADIX, RADIX), fixed),
            pl.BlockSpec((2 * RADIX, RADIX), fixed),
        ],
        out_specs=pl.BlockSpec((step_templates, block_total, RADIX // 2), lambda k: (k, 0, 0)),
        compiler_params=pltpu.CompilerParams(dimension_semantics=("arbitrary",)),
        cost_estimate=pl.CostEstimate(
            flops=pair_flops * template_total * block_total,
            transcendentals=0,
            bytes_accessed=spectra.size * 4 + bank.size * 2 + template_total * block_total * RADIX * 2,
        ),
    )(spectra, bank, *tables)


def chain_order(seg_total, chunk):
    distances = []
    distance = seg_total // 2
    while distance >= 1:
        distances.append(distance)
        distance //= 2
    if chunk % 2 == 1 and len(distances) > 2:
        distances = distances[-2:-1] + distances[:-2] + distances[-1:]
    return distances


def gathered_bank(bank_rows, chunk):
    seg_total = lax.axis_size("seg")
    me = lax.axis_index("seg")
    rows, parts, local_bins = bank_rows.shape
    held = bank_rows[None]
    order = chain_order(seg_total, chunk)
    for distance in order:
        pairs = [(i, i ^ distance) for i in range(seg_total)]
        arrived = lax.ppermute(held, "seg", pairs)
        upper = (me & distance) != 0
        held = jnp.stack([jnp.where(upper, arrived, held), jnp.where(upper, held, arrived)], axis=0)
    steps = len(order)
    held = held.reshape((2,) * steps + (rows, parts, local_bins // RADIX, RADIX))
    axis_distance = list(reversed(order))
    bit_axes = tuple(sorted(range(steps), key=lambda axis: -axis_distance[axis]))
    held = jnp.transpose(held, (steps, steps + 1) + bit_axes + (steps + 2, steps + 3))
    return held.reshape(rows, parts, seg_total * local_bins // RADIX, RADIX)


def local(strain, gate_mask, template_bank):
    gated = strain * gate_mask.astype(jnp.float32)
    local_blocks = gated.reshape(-1, BLOCK)
    block_total = local_blocks.shape[0]
    earlier = passed_along(local_blocks[block_total - 1], "seg", 1)
    before = jnp.concatenate([earlier[None], local_blocks[:-1]], axis=0)
    windows = jnp.concatenate([before, local_blocks], axis=1)
    spectra = forward(windows)
    tables = inverse_tables(spectra.shape[1])
    template_total = template_bank.shape[0]
    results = []
    for start in range(0, template_total, SUBBANK):
        bank = gathered_bank(template_bank[start : start + SUBBANK], start // SUBBANK)
        peaks = window_peaks(spectra, bank, tables)
        results.append(peaks.reshape(bank.shape[0], block_total * (RADIX // 2)))
    return jnp.concatenate(results, axis=0)


def solution(mesh):
    in_specs = (P(("grp", "seg")), P(("grp", "seg")), P("grp", None, "seg"))
    out_specs = P(None, ("grp", "seg"))
    return jax.shard_map(local, mesh=mesh, in_specs=in_specs, out_specs=out_specs, check_vma=False)
```

```python
import math

import jax
import jax.numpy as jnp
from jax import lax
from jax.experimental import pallas as pl
from jax.experimental.pallas import tpu as pltpu
from jax.sharding import PartitionSpec as P

RADIX = 256
BLOCK = 32768
SUBBANK = 8
STEP_TEMPLATES = 2


PRECISE = lax.Precision.HIGH
EPSILON = 1e-06


def passed_along(value, axis, by):
    count = lax.axis_size(axis)
    pairs = [(i, i + by) for i in range(count) if 0 <= i + by < count]
    return lax.ppermute(value, axis, pairs)


def angle_table(row_count, col_count, period):
    row_index = lax.broadcasted_iota(jnp.int32, (row_count, col_count), 0)
    col_index = lax.broadcasted_iota(jnp.int32, (row_count, col_count), 1)
    phase_step = row_index * col_index % period
    angle_value = phase_step.astype(jnp.float32) * (2.0 * math.pi / period)
    return (jnp.cos(angle_value), jnp.sin(angle_value))


def forward(windows):
    half_radix = RADIX // 2
    window_total = windows.shape[0]
    rows = windows.shape[1] // RADIX
    block_grid = windows.reshape(window_total, rows, RADIX)
    cos_first, sin_first = angle_table(rows, RADIX, RADIX)
    first_table = jnp.concatenate([cos_first, -sin_first], axis=1)
    first_section = jnp.einsum("bnm,nf->bmf", block_grid, first_table, precision=PRECISE)
    cos_twist, sin_twist = angle_table(RADIX, RADIX, RADIX * RADIX)
    real_part = first_section[..., :RADIX]
    imag_part = first_section[..., RADIX:]
    turned = jnp.concatenate(
        [
            real_part * cos_twist + imag_part * sin_twist,
            imag_part * cos_twist - real_part * sin_twist,
        ],
        axis=-1,
    )
    cos_second, sin_second = angle_table(RADIX, half_radix, RADIX)
    cosine_part = jnp.einsum("bnf,nk->bkf", turned, cos_second, precision=PRECISE)
    sine_part = jnp.einsum("bnf,nk->bkf", turned, sin_second, precision=PRECISE)
    return jnp.concatenate(
        [
            cosine_part[..., :RADIX] + sine_part[..., RADIX:],
            cosine_part[..., RADIX:] - sine_part[..., :RADIX],
        ],
        axis=-1,
    )


def split_pair(value):
    high = value.astype(jnp.bfloat16)
    low = (value - high.astype(jnp.float32)).astype(jnp.bfloat16)
    return high, low


def table_pair(value):
    high = lax.reduce_precision(value, exponent_bits=8, mantissa_bits=7)
    return high.astype(jnp.bfloat16), (value - high).astype(jnp.bfloat16)


def triple_dot(left_high, left_low, right_high, right_low):
    total = jnp.dot(left_high, right_high, preferred_element_type=jnp.float32)
    total = total + jnp.dot(left_high, right_low, preferred_element_type=jnp.float32)
    return total + jnp.dot(left_low, right_high, preferred_element_type=jnp.float32)


def inverse_tables(k_rows):
    half_radix = RADIX // 2
    cos_first, sin_first = angle_table(RADIX, k_rows, RADIX)
    first = jnp.concatenate(
        [
            jnp.concatenate([cos_first, -sin_first], axis=1),
            jnp.concatenate([sin_first, cos_first], axis=1),
        ],
        axis=0,
    )
    cos_twist, sin_twist = angle_table(RADIX, RADIX, RADIX * RADIX)
    cos_out, sin_out = angle_table(RADIX, RADIX, RADIX)
    real_cols = jnp.concatenate([cos_out, -sin_out], axis=0)
    imag_cols = jnp.concatenate([sin_out, cos_out], axis=0)
    second = jnp.concatenate([real_cols[:, half_radix:], imag_cols[:, half_radix:]], axis=1)
    first_high, first_low = table_pair(first)
    second_high, second_low = table_pair(second)
    return first_high, first_low, cos_twist, sin_twist, second_high, second_low


def peaks_kernel(spec_ref, bank_ref, fh_ref, fl_ref, tc_ref, ts_ref, sh_ref, sl_ref, out_ref):
    half_radix = RADIX // 2
    block_total = spec_ref.shape[0]
    step_templates = bank_ref.shape[0]
    pair_total = step_templates * block_total
    products = []
    scales = []
    for template in range(step_templates):
        wave_real = bank_ref[template, 0].astype(jnp.float32)
        wave_imag = bank_ref[template, 1].astype(jnp.float32)
        power_sum = jnp.sum(wave_real * wave_real + wave_imag * wave_imag, keepdims=True)
        norm_scale = 1.0 / jnp.sqrt(BLOCK * power_sum + EPSILON)
        scales.append(norm_scale * norm_scale)
        for block in range(block_total):
            spec_real = spec_ref[block, :, :RADIX]
            spec_imag = spec_ref[block, :, RADIX:]
            prod_real = spec_real * wave_real + spec_imag * wave_imag
            prod_imag = spec_imag * wave_real - spec_real * wave_imag
            products.append(jnp.concatenate([prod_real, prod_imag], axis=0))
    stacked = jnp.concatenate(products, axis=1)
    stacked_high, stacked_low = split_pair(stacked)
    first = triple_dot(fh_ref[...], fl_ref[...], stacked_high, stacked_low)
    cos_twist = tc_ref[...]
    sin_twist = ts_ref[...]
    turned_rows = []
    for pair in range(pair_total):
        real_part = first[:RADIX, pair * RADIX : (pair + 1) * RADIX]
        imag_part = first[RADIX:, pair * RADIX : (pair + 1) * RADIX]
        turned_rows.append(
            jnp.concatenate(
                [
                    real_part * cos_twist - imag_part * sin_twist,
                    real_part * sin_twist + imag_part * cos_twist,
                ],
                axis=1,
            )
        )
    turned = jnp.concatenate(turned_rows, axis=0)
    turned_high, turned_low = split_pair(turned)
    series = triple_dot(turned_high, turned_low, sh_ref[...], sl_ref[...])
    power_series = (
        series[:, :half_radix] * series[:, :half_radix]
        + series[:, half_radix:] * series[:, half_radix:]
    )
    peaks = jnp.max(power_series.reshape(pair_total, RADIX, half_radix), axis=1)
    for template in range(step_templates):
        rows = peaks[template * block_total : (template + 1) * block_total]
        out_ref[template] = rows * scales[template]


def window_peaks(spectra, bank, tables):
    block_total, k_rows, _ = spectra.shape
    template_total = bank.shape[0]
    step_templates = STEP_TEMPLATES if template_total % STEP_TEMPLATES == 0 else 1
    fixed = lambda k: (0, 0)
    pair_flops = 6 * (2 * RADIX) * (2 * k_rows) * RADIX + 6 * RADIX * (2 * RADIX) * RADIX
    return pl.pallas_call(
        peaks_kernel,
        out_shape=jax.ShapeDtypeStruct((template_total, block_total, RADIX // 2), jnp.float32),
        grid=(template_total // step_templates,),
        in_specs=[
            pl.BlockSpec((block_total, k_rows, 2 * RADIX), lambda k: (0, 0, 0)),
            pl.BlockSpec((step_templates, 2, k_rows, RADIX), lambda k: (k, 0, 0, 0)),
            pl.BlockSpec((2 * RADIX, 2 * k_rows), fixed),
            pl.BlockSpec((2 * RADIX, 2 * k_rows), fixed),
            pl.BlockSpec((RADIX, RADIX), fixed),
            pl.BlockSpec((RADIX, RADIX), fixed),
            pl.BlockSpec((2 * RADIX, RADIX), fixed),
            pl.BlockSpec((2 * RADIX, RADIX), fixed),
        ],
        out_specs=pl.BlockSpec((step_templates, block_total, RADIX // 2), lambda k: (k, 0, 0)),
        compiler_params=pltpu.CompilerParams(dimension_semantics=("arbitrary",)),
        cost_estimate=pl.CostEstimate(
            flops=pair_flops * template_total * block_total,
            transcendentals=0,
            bytes_accessed=spectra.size * 4 + bank.size * 2 + template_total * block_total * RADIX * 2,
        ),
    )(spectra, bank, *tables)


def gathered_bank(bank_rows):
    seg_total = lax.axis_size("seg")
    me = lax.axis_index("seg")
    rows, parts, local_bins = bank_rows.shape
    held = bank_rows[None]
    distance = seg_total // 2
    steps = 0
    first_arrived = None
    while distance >= 1:
        pairs = [(i, i ^ distance) for i in range(seg_total)]
        arrived = lax.ppermute(held, "seg", pairs)
        if first_arrived is None:
            first_arrived = arrived
        upper = (me & distance) != 0
        held = jnp.stack([jnp.where(upper, arrived, held), jnp.where(upper, held, arrived)], axis=0)
        distance //= 2
        steps += 1
    held = held.reshape((2,) * steps + (rows, parts, local_bins // RADIX, RADIX))
    order = tuple(reversed(range(steps)))
    held = jnp.transpose(held, (steps, steps + 1) + order + (steps + 2, steps + 3))
    return held.reshape(rows, parts, seg_total * local_bins // RADIX, RADIX), first_arrived


def local(strain, gate_mask, template_bank):
    template_total = template_bank.shape[0]
    banks = []
    first_pieces = []
    for start in range(0, template_total, SUBBANK):
        bank, first_arrived = gathered_bank(template_bank[start : start + SUBBANK])
        banks.append(bank)
        first_pieces.append(first_arrived)
    gated = strain * gate_mask.astype(jnp.float32)
    local_blocks = gated.reshape(-1, BLOCK)
    block_total = local_blocks.shape[0]
    last_block, _ = lax.optimization_barrier((local_blocks[block_total - 1], first_pieces))
    earlier = passed_along(last_block, "seg", 1)
    before = jnp.concatenate([earlier[None], local_blocks[:-1]], axis=0)
    windows = jnp.concatenate([before, local_blocks], axis=1)
    spectra = forward(windows)
    tables = inverse_tables(spectra.shape[1])
    results = []
    for bank in banks:
        peaks = window_peaks(spectra, bank, tables)
        results.append(peaks.reshape(bank.shape[0], block_total * (RADIX // 2)))
    return jnp.concatenate(results, axis=0)


def solution(mesh):
    in_specs = (P(("grp", "seg")), P(("grp", "seg")), P("grp", None, "seg"))
    out_specs = P(None, ("grp", "seg"))
    return jax.shard_map(local, mesh=mesh, in_specs=in_specs, out_specs=out_specs, check_vma=False)
```

```python
import math

import jax
import jax.numpy as jnp
from jax import lax
from jax.experimental import pallas as pl
from jax.experimental.pallas import tpu as pltpu
from jax.sharding import PartitionSpec as P

RADIX = 256
BLOCK = 32768
SUBBANK = 8
STEP_TEMPLATES = 2


PRECISE = lax.Precision.HIGH
EPSILON = 1e-06


def passed_along(value, axis, by):
    count = lax.axis_size(axis)
    pairs = [(i, i + by) for i in range(count) if 0 <= i + by < count]
    return lax.ppermute(value, axis, pairs)


def angle_table(row_count, col_count, period):
    row_index = lax.broadcasted_iota(jnp.int32, (row_count, col_count), 0)
    col_index = lax.broadcasted_iota(jnp.int32, (row_count, col_count), 1)
    phase_step = row_index * col_index % period
    angle_value = phase_step.astype(jnp.float32) * (2.0 * math.pi / period)
    return (jnp.cos(angle_value), jnp.sin(angle_value))


def forward(windows):
    half_radix = RADIX // 2
    window_total = windows.shape[0]
    rows = windows.shape[1] // RADIX
    block_grid = windows.reshape(window_total, rows, RADIX)
    cos_first, sin_first = angle_table(rows, RADIX, RADIX)
    first_table = jnp.concatenate([cos_first, -sin_first], axis=1)
    first_section = jnp.einsum("bnm,nf->bmf", block_grid, first_table, precision=PRECISE)
    cos_twist, sin_twist = angle_table(RADIX, RADIX, RADIX * RADIX)
    real_part = first_section[..., :RADIX]
    imag_part = first_section[..., RADIX:]
    turned = jnp.concatenate(
        [
            real_part * cos_twist + imag_part * sin_twist,
            imag_part * cos_twist - real_part * sin_twist,
        ],
        axis=-1,
    )
    cos_second, sin_second = angle_table(RADIX, half_radix, RADIX)
    cosine_part = jnp.einsum("bnf,nk->bkf", turned, cos_second, precision=PRECISE)
    sine_part = jnp.einsum("bnf,nk->bkf", turned, sin_second, precision=PRECISE)
    return jnp.concatenate(
        [
            cosine_part[..., :RADIX] + sine_part[..., RADIX:],
            cosine_part[..., RADIX:] - sine_part[..., :RADIX],
        ],
        axis=-1,
    )


def split_pair(value):
    high = value.astype(jnp.bfloat16)
    low = (value - high.astype(jnp.float32)).astype(jnp.bfloat16)
    return high, low


def table_pair(value):
    high = lax.reduce_precision(value, exponent_bits=8, mantissa_bits=7)
    return high.astype(jnp.bfloat16), (value - high).astype(jnp.bfloat16)


def triple_dot(left_high, left_low, right_high, right_low):
    total = jnp.dot(left_high, right_high, preferred_element_type=jnp.float32)
    total = total + jnp.dot(left_high, right_low, preferred_element_type=jnp.float32)
    return total + jnp.dot(left_low, right_high, preferred_element_type=jnp.float32)


def inverse_tables(k_rows):
    half_radix = RADIX // 2
    cos_first, sin_first = angle_table(RADIX, k_rows, RADIX)
    first = jnp.concatenate(
        [
            jnp.concatenate([cos_first, -sin_first], axis=1),
            jnp.concatenate([sin_first, cos_first], axis=1),
        ],
        axis=0,
    )
    cos_twist, sin_twist = angle_table(RADIX, RADIX, RADIX * RADIX)
    cos_out, sin_out = angle_table(RADIX, RADIX, RADIX)
    real_cols = jnp.concatenate([cos_out, -sin_out], axis=0)
    imag_cols = jnp.concatenate([sin_out, cos_out], axis=0)
    second = jnp.concatenate([real_cols[:, half_radix:], imag_cols[:, half_radix:]], axis=1)
    first_high, first_low = table_pair(first)
    second_high, second_low = table_pair(second)
    return first_high, first_low, cos_twist, sin_twist, second_high, second_low


def peaks_kernel(spec_ref, bank_ref, fh_ref, fl_ref, tc_ref, ts_ref, sh_ref, sl_ref, out_ref):
    half_radix = RADIX // 2
    block_total = spec_ref.shape[0]
    step_templates = bank_ref.shape[0]
    pair_total = step_templates * block_total
    products = []
    scales = []
    for template in range(step_templates):
        wave_real = bank_ref[template, 0].astype(jnp.float32)
        wave_imag = bank_ref[template, 1].astype(jnp.float32)
        power_sum = jnp.sum(wave_real * wave_real + wave_imag * wave_imag, keepdims=True)
        norm_scale = 1.0 / jnp.sqrt(BLOCK * power_sum + EPSILON)
        scales.append(norm_scale * norm_scale)
        for block in range(block_total):
            spec_real = spec_ref[block, :, :RADIX]
            spec_imag = spec_ref[block, :, RADIX:]
            prod_real = spec_real * wave_real + spec_imag * wave_imag
            prod_imag = spec_imag * wave_real - spec_real * wave_imag
            products.append(jnp.concatenate([prod_real, prod_imag], axis=0))
    stacked = jnp.concatenate(products, axis=1)
    stacked_high, stacked_low = split_pair(stacked)
    first = triple_dot(fh_ref[...], fl_ref[...], stacked_high, stacked_low)
    cos_twist = tc_ref[...]
    sin_twist = ts_ref[...]
    turned_rows = []
    for pair in range(pair_total):
        real_part = first[:RADIX, pair * RADIX : (pair + 1) * RADIX]
        imag_part = first[RADIX:, pair * RADIX : (pair + 1) * RADIX]
        turned_rows.append(
            jnp.concatenate(
                [
                    real_part * cos_twist - imag_part * sin_twist,
                    real_part * sin_twist + imag_part * cos_twist,
                ],
                axis=1,
            )
        )
    turned = jnp.concatenate(turned_rows, axis=0)
    turned_high, turned_low = split_pair(turned)
    series = triple_dot(turned_high, turned_low, sh_ref[...], sl_ref[...])
    power_series = (
        series[:, :half_radix] * series[:, :half_radix]
        + series[:, half_radix:] * series[:, half_radix:]
    )
    peaks = jnp.max(power_series.reshape(pair_total, RADIX, half_radix), axis=1)
    for template in range(step_templates):
        rows = peaks[template * block_total : (template + 1) * block_total]
        out_ref[template] = rows * scales[template]


def window_peaks(spectra, bank, tables):
    block_total, k_rows, _ = spectra.shape
    template_total = bank.shape[0]
    step_templates = STEP_TEMPLATES if template_total % STEP_TEMPLATES == 0 else 1
    fixed = lambda k: (0, 0)
    pair_flops = 6 * (2 * RADIX) * (2 * k_rows) * RADIX + 6 * RADIX * (2 * RADIX) * RADIX
    return pl.pallas_call(
        peaks_kernel,
        out_shape=jax.ShapeDtypeStruct((template_total, block_total, RADIX // 2), jnp.float32),
        grid=(template_total // step_templates,),
        in_specs=[
            pl.BlockSpec((block_total, k_rows, 2 * RADIX), lambda k: (0, 0, 0)),
            pl.BlockSpec((step_templates, 2, k_rows, RADIX), lambda k: (k, 0, 0, 0)),
            pl.BlockSpec((2 * RADIX, 2 * k_rows), fixed),
            pl.BlockSpec((2 * RADIX, 2 * k_rows), fixed),
            pl.BlockSpec((RADIX, RADIX), fixed),
            pl.BlockSpec((RADIX, RADIX), fixed),
            pl.BlockSpec((2 * RADIX, RADIX), fixed),
            pl.BlockSpec((2 * RADIX, RADIX), fixed),
        ],
        out_specs=pl.BlockSpec((step_templates, block_total, RADIX // 2), lambda k: (k, 0, 0)),
        compiler_params=pltpu.CompilerParams(dimension_semantics=("arbitrary",)),
        cost_estimate=pl.CostEstimate(
            flops=pair_flops * template_total * block_total,
            transcendentals=0,
            bytes_accessed=spectra.size * 4 + bank.size * 2 + template_total * block_total * RADIX * 2,
        ),
    )(spectra, bank, *tables)


def gathered_bank(bank_rows):
    seg_total = lax.axis_size("seg")
    me = lax.axis_index("seg")
    rows, parts, local_bins = bank_rows.shape
    piece_rows = local_bins // RADIX
    held = bank_rows[None]
    distance = seg_total // 2
    steps = 0
    while distance > 1:
        pairs = [(i, i ^ distance) for i in range(seg_total)]
        arrived = lax.ppermute(held, "seg", pairs)
        slot = lax.broadcasted_iota(jnp.int32, (2,) + (1,) * held.ndim, 0)
        held = jnp.where(slot == (me // distance) % 2, held[None], arrived[None])
        distance //= 2
        steps += 1
    arrived = lax.ppermute(held, "seg", [(i, i ^ 1) for i in range(seg_total)])

    def by_template(value):
        value = value.reshape((2,) * steps + (rows, parts, piece_rows, RADIX))
        value = jnp.transpose(value, (steps, steps + 1) + tuple(reversed(range(steps))) + (steps + 2, steps + 3))
        return value.reshape(rows, parts, seg_total // 2, 1, piece_rows, RADIX)

    slot = lax.broadcasted_iota(jnp.int32, (1, 1, 1, 2, 1, 1), 3)
    every = jnp.where(slot == me % 2, by_template(held), by_template(arrived))
    return every.reshape(rows, parts, seg_total * piece_rows, RADIX)


def local(strain, gate_mask, template_bank):
    gated = strain * gate_mask.astype(jnp.float32)
    local_blocks = gated.reshape(-1, BLOCK)
    block_total = local_blocks.shape[0]
    earlier = passed_along(local_blocks[block_total - 1], "seg", 1)
    before = jnp.concatenate([earlier[None], local_blocks[:-1]], axis=0)
    windows = jnp.concatenate([before, local_blocks], axis=1)
    spectra = forward(windows)
    tables = inverse_tables(spectra.shape[1])
    template_total = template_bank.shape[0]
    results = []
    for start in range(0, template_total, SUBBANK):
        bank = gathered_bank(template_bank[start : start + SUBBANK])
        peaks = window_peaks(spectra, bank, tables)
        results.append(peaks.reshape(bank.shape[0], block_total * (RADIX // 2)))
    return jnp.concatenate(results, axis=0)


def solution(mesh):
    in_specs = (P(("grp", "seg")), P(("grp", "seg")), P("grp", None, "seg"))
    out_specs = P(None, ("grp", "seg"))
    return jax.shard_map(local, mesh=mesh, in_specs=in_specs, out_specs=out_specs, check_vma=False)
```

```python
import math

import jax
import jax.numpy as jnp
from jax import lax
from jax.experimental import pallas as pl
from jax.experimental.pallas import tpu as pltpu
from jax.sharding import PartitionSpec as P

RADIX = 256
BLOCK = 32768
SUBBANK = 8
STEP_TEMPLATES = 2


PRECISE = lax.Precision.HIGH
EPSILON = 1e-06


def passed_along(value, axis, by):
    count = lax.axis_size(axis)
    pairs = [(i, i + by) for i in range(count) if 0 <= i + by < count]
    return lax.ppermute(value, axis, pairs)


def angle_table(row_count, col_count, period):
    row_index = lax.broadcasted_iota(jnp.int32, (row_count, col_count), 0)
    col_index = lax.broadcasted_iota(jnp.int32, (row_count, col_count), 1)
    phase_step = row_index * col_index % period
    angle_value = phase_step.astype(jnp.float32) * (2.0 * math.pi / period)
    return (jnp.cos(angle_value), jnp.sin(angle_value))


def forward(windows):
    half_radix = RADIX // 2
    window_total = windows.shape[0]
    rows = windows.shape[1] // RADIX
    block_grid = windows.reshape(window_total, rows, RADIX)
    cos_first, sin_first = angle_table(rows, RADIX, RADIX)
    first_table = jnp.concatenate([cos_first, -sin_first], axis=1)
    first_section = jnp.einsum("bnm,nf->bmf", block_grid, first_table, precision=PRECISE)
    cos_twist, sin_twist = angle_table(RADIX, RADIX, RADIX * RADIX)
    real_part = first_section[..., :RADIX]
    imag_part = first_section[..., RADIX:]
    turned = jnp.concatenate(
        [
            real_part * cos_twist + imag_part * sin_twist,
            imag_part * cos_twist - real_part * sin_twist,
        ],
        axis=-1,
    )
    cos_second, sin_second = angle_table(RADIX, half_radix, RADIX)
    cosine_part = jnp.einsum("bnf,nk->bkf", turned, cos_second, precision=PRECISE)
    sine_part = jnp.einsum("bnf,nk->bkf", turned, sin_second, precision=PRECISE)
    return jnp.concatenate(
        [
            cosine_part[..., :RADIX] + sine_part[..., RADIX:],
            cosine_part[..., RADIX:] - sine_part[..., :RADIX],
        ],
        axis=-1,
    )


def split_pair(value):
    high = value.astype(jnp.bfloat16)
    low = (value - high.astype(jnp.float32)).astype(jnp.bfloat16)
    return high, low


def table_pair(value):
    high = lax.reduce_precision(value, exponent_bits=8, mantissa_bits=7)
    return high.astype(jnp.bfloat16), (value - high).astype(jnp.bfloat16)


def triple_dot(left_high, left_low, right_high, right_low):
    total = jnp.dot(left_high, right_high, preferred_element_type=jnp.float32)
    total = total + jnp.dot(left_high, right_low, preferred_element_type=jnp.float32)
    return total + jnp.dot(left_low, right_high, preferred_element_type=jnp.float32)


def inverse_tables(k_rows):
    half_radix = RADIX // 2
    cos_first, sin_first = angle_table(RADIX, k_rows, RADIX)
    first = jnp.concatenate(
        [
            jnp.concatenate([cos_first, -sin_first], axis=1),
            jnp.concatenate([sin_first, cos_first], axis=1),
        ],
        axis=0,
    )
    cos_twist, sin_twist = angle_table(RADIX, RADIX, RADIX * RADIX)
    cos_out, sin_out = angle_table(RADIX, RADIX, RADIX)
    real_cols = jnp.concatenate([cos_out, -sin_out], axis=0)
    imag_cols = jnp.concatenate([sin_out, cos_out], axis=0)
    second = jnp.concatenate([real_cols[:, half_radix:], imag_cols[:, half_radix:]], axis=1)
    first_high, first_low = table_pair(first)
    second_high, second_low = table_pair(second)
    return first_high, first_low, cos_twist, sin_twist, second_high, second_low


def peaks_kernel(spec_ref, bank_ref, fh_ref, fl_ref, tc_ref, ts_ref, sh_ref, sl_ref, out_ref):
    half_radix = RADIX // 2
    block_total = spec_ref.shape[0]
    step_templates = bank_ref.shape[0]
    pair_total = step_templates * block_total
    products = []
    scales = []
    for template in range(step_templates):
        wave_real = bank_ref[template, 0].astype(jnp.float32)
        wave_imag = bank_ref[template, 1].astype(jnp.float32)
        power_sum = jnp.sum(wave_real * wave_real + wave_imag * wave_imag, keepdims=True)
        norm_scale = 1.0 / jnp.sqrt(BLOCK * power_sum + EPSILON)
        scales.append(norm_scale * norm_scale)
        for block in range(block_total):
            spec_real = spec_ref[block, :, :RADIX]
            spec_imag = spec_ref[block, :, RADIX:]
            prod_real = spec_real * wave_real + spec_imag * wave_imag
            prod_imag = spec_imag * wave_real - spec_real * wave_imag
            products.append(jnp.concatenate([prod_real, prod_imag], axis=0))
    stacked = jnp.concatenate(products, axis=1)
    stacked_high, stacked_low = split_pair(stacked)
    first = triple_dot(fh_ref[...], fl_ref[...], stacked_high, stacked_low)
    cos_twist = tc_ref[...]
    sin_twist = ts_ref[...]
    turned_rows = []
    for pair in range(pair_total):
        real_part = first[:RADIX, pair * RADIX : (pair + 1) * RADIX]
        imag_part = first[RADIX:, pair * RADIX : (pair + 1) * RADIX]
        turned_rows.append(
            jnp.concatenate(
                [
                    real_part * cos_twist - imag_part * sin_twist,
                    real_part * sin_twist + imag_part * cos_twist,
                ],
                axis=1,
            )
        )
    turned = jnp.concatenate(turned_rows, axis=0)
    turned_high, turned_low = split_pair(turned)
    series = triple_dot(turned_high, turned_low, sh_ref[...], sl_ref[...])
    power_series = (
        series[:, :half_radix] * series[:, :half_radix]
        + series[:, half_radix:] * series[:, half_radix:]
    )
    peaks = jnp.max(power_series.reshape(pair_total, RADIX, half_radix), axis=1)
    for template in range(step_templates):
        rows = peaks[template * block_total : (template + 1) * block_total]
        out_ref[template] = rows * scales[template]


def window_peaks(spectra, bank, tables):
    block_total, k_rows, _ = spectra.shape
    template_total = bank.shape[0]
    step_templates = STEP_TEMPLATES if template_total % STEP_TEMPLATES == 0 else 1
    fixed = lambda k: (0, 0)
    pair_flops = 6 * (2 * RADIX) * (2 * k_rows) * RADIX + 6 * RADIX * (2 * RADIX) * RADIX
    return pl.pallas_call(
        peaks_kernel,
        out_shape=jax.ShapeDtypeStruct((template_total, block_total, RADIX // 2), jnp.float32),
        grid=(template_total // step_templates,),
        in_specs=[
            pl.BlockSpec((block_total, k_rows, 2 * RADIX), lambda k: (0, 0, 0)),
            pl.BlockSpec((step_templates, 2, k_rows, RADIX), lambda k: (k, 0, 0, 0)),
            pl.BlockSpec((2 * RADIX, 2 * k_rows), fixed),
            pl.BlockSpec((2 * RADIX, 2 * k_rows), fixed),
            pl.BlockSpec((RADIX, RADIX), fixed),
            pl.BlockSpec((RADIX, RADIX), fixed),
            pl.BlockSpec((2 * RADIX, RADIX), fixed),
            pl.BlockSpec((2 * RADIX, RADIX), fixed),
        ],
        out_specs=pl.BlockSpec((step_templates, block_total, RADIX // 2), lambda k: (k, 0, 0)),
        compiler_params=pltpu.CompilerParams(dimension_semantics=("arbitrary",)),
        cost_estimate=pl.CostEstimate(
            flops=pair_flops * template_total * block_total,
            transcendentals=0,
            bytes_accessed=spectra.size * 4 + bank.size * 2 + template_total * block_total * RADIX * 2,
        ),
    )(spectra, bank, *tables)


def gathered_half(template_bank):
    seg_total = lax.axis_size("seg")
    me = lax.axis_index("seg")
    core = me % 2
    template_total, parts, local_bins = template_bank.shape
    half = template_total // 2
    mine = lax.dynamic_slice_in_dim(template_bank, core * half, half, axis=0)
    theirs = lax.dynamic_slice_in_dim(template_bank, (1 - core) * half, half, axis=0)
    arrived = lax.ppermute(theirs[None], "seg", [(i, i ^ 1) for i in range(seg_total)])
    upper = core != 0
    held = jnp.stack([jnp.where(upper, arrived, mine[None]), jnp.where(upper, mine[None], arrived)], axis=0)
    order = [1]
    distance = seg_total // 2
    while distance > 1:
        pairs = [(i, i ^ distance) for i in range(seg_total)]
        arrived = lax.ppermute(held, "seg", pairs)
        upper = (me & distance) != 0
        held = jnp.stack([jnp.where(upper, arrived, held), jnp.where(upper, held, arrived)], axis=0)
        order.append(distance)
        distance //= 2
    steps = len(order)
    held = held.reshape((2,) * steps + (half, parts, local_bins // RADIX, RADIX))
    axis_distance = list(reversed(order))
    bit_axes = tuple(sorted(range(steps), key=lambda axis: -axis_distance[axis]))
    held = jnp.transpose(held, (steps, steps + 1) + bit_axes + (steps + 2, steps + 3))
    return held.reshape(half, parts, seg_total * local_bins // RADIX, RADIX)


def local(strain, gate_mask, template_bank):
    seg_total = lax.axis_size("seg")
    core = lax.axis_index("seg") % 2
    bank = gathered_half(template_bank)
    gated = strain * gate_mask.astype(jnp.float32)
    local_blocks = gated.reshape(-1, BLOCK)
    block_total = local_blocks.shape[0]
    earlier = passed_along(local_blocks[block_total - 1], "seg", 1)
    mine = jnp.concatenate([earlier[None], local_blocks], axis=0)
    other = lax.ppermute(mine, "seg", [(i, i ^ 1) for i in range(seg_total)])
    chip_blocks = jnp.where(
        core == 0,
        jnp.concatenate([mine, other[1:]], axis=0),
        jnp.concatenate([other, mine[1:]], axis=0),
    )
    windows = jnp.concatenate([chip_blocks[:-1], chip_blocks[1:]], axis=1)
    spectra = forward(windows)
    tables = inverse_tables(spectra.shape[1])
    partner_spectra = lax.dynamic_slice_in_dim(spectra, (1 - core) * block_total, block_total, axis=0)
    own_spectra = lax.dynamic_slice_in_dim(spectra, core * block_total, block_total, axis=0)
    half = bank.shape[0]
    partner_peaks = window_peaks(partner_spectra, bank, tables).reshape(half, block_total * (RADIX // 2))
    returned = lax.ppermute(partner_peaks, "seg", [(i, i ^ 1) for i in range(seg_total)])
    own_peaks = window_peaks(own_spectra, bank, tables).reshape(half, block_total * (RADIX // 2))
    return jnp.where(
        core == 0,
        jnp.concatenate([own_peaks, returned], axis=0),
        jnp.concatenate([returned, own_peaks], axis=0),
    )


def solution(mesh):
    in_specs = (P(("grp", "seg")), P(("grp", "seg")), P("grp", None, "seg"))
    out_specs = P(None, ("grp", "seg"))
    return jax.shard_map(local, mesh=mesh, in_specs=in_specs, out_specs=out_specs, check_vma=False)
```

```python
import math

import jax
import jax.numpy as jnp
from jax import lax
from jax.experimental import pallas as pl
from jax.experimental.pallas import tpu as pltpu
from jax.sharding import PartitionSpec as P

RADIX = 256
BLOCK = 32768
SUBBANK = 8
SUBHALF = 4
STEP_TEMPLATES = 2


PRECISE = lax.Precision.HIGH
EPSILON = 1e-06


def passed_along(value, axis, by):
    count = lax.axis_size(axis)
    pairs = [(i, i + by) for i in range(count) if 0 <= i + by < count]
    return lax.ppermute(value, axis, pairs)


def angle_table(row_count, col_count, period):
    row_index = lax.broadcasted_iota(jnp.int32, (row_count, col_count), 0)
    col_index = lax.broadcasted_iota(jnp.int32, (row_count, col_count), 1)
    phase_step = row_index * col_index % period
    angle_value = phase_step.astype(jnp.float32) * (2.0 * math.pi / period)
    return (jnp.cos(angle_value), jnp.sin(angle_value))


def forward(windows):
    half_radix = RADIX // 2
    window_total = windows.shape[0]
    rows = windows.shape[1] // RADIX
    block_grid = windows.reshape(window_total, rows, RADIX)
    cos_first, sin_first = angle_table(rows, RADIX, RADIX)
    first_table = jnp.concatenate([cos_first, -sin_first], axis=1)
    first_section = jnp.einsum("bnm,nf->bmf", block_grid, first_table, precision=PRECISE)
    cos_twist, sin_twist = angle_table(RADIX, RADIX, RADIX * RADIX)
    real_part = first_section[..., :RADIX]
    imag_part = first_section[..., RADIX:]
    turned = jnp.concatenate(
        [
            real_part * cos_twist + imag_part * sin_twist,
            imag_part * cos_twist - real_part * sin_twist,
        ],
        axis=-1,
    )
    cos_second, sin_second = angle_table(RADIX, half_radix, RADIX)
    cosine_part = jnp.einsum("bnf,nk->bkf", turned, cos_second, precision=PRECISE)
    sine_part = jnp.einsum("bnf,nk->bkf", turned, sin_second, precision=PRECISE)
    return jnp.concatenate(
        [
            cosine_part[..., :RADIX] + sine_part[..., RADIX:],
            cosine_part[..., RADIX:] - sine_part[..., :RADIX],
        ],
        axis=-1,
    )


def split_pair(value):
    high = value.astype(jnp.bfloat16)
    low = (value - high.astype(jnp.float32)).astype(jnp.bfloat16)
    return high, low


def table_pair(value):
    high = lax.reduce_precision(value, exponent_bits=8, mantissa_bits=7)
    return high.astype(jnp.bfloat16), (value - high).astype(jnp.bfloat16)


def triple_dot(left_high, left_low, right_high, right_low):
    total = jnp.dot(left_high, right_high, preferred_element_type=jnp.float32)
    total = total + jnp.dot(left_high, right_low, preferred_element_type=jnp.float32)
    return total + jnp.dot(left_low, right_high, preferred_element_type=jnp.float32)


def inverse_tables(k_rows):
    half_radix = RADIX // 2
    cos_first, sin_first = angle_table(RADIX, k_rows, RADIX)
    first = jnp.concatenate(
        [
            jnp.concatenate([cos_first, -sin_first], axis=1),
            jnp.concatenate([sin_first, cos_first], axis=1),
        ],
        axis=0,
    )
    cos_twist, sin_twist = angle_table(RADIX, RADIX, RADIX * RADIX)
    cos_out, sin_out = angle_table(RADIX, RADIX, RADIX)
    real_cols = jnp.concatenate([cos_out, -sin_out], axis=0)
    imag_cols = jnp.concatenate([sin_out, cos_out], axis=0)
    second = jnp.concatenate([real_cols[:, half_radix:], imag_cols[:, half_radix:]], axis=1)
    first_high, first_low = table_pair(first)
    second_high, second_low = table_pair(second)
    return first_high, first_low, cos_twist, sin_twist, second_high, second_low


def peaks_kernel(spec_ref, bank_ref, fh_ref, fl_ref, tc_ref, ts_ref, sh_ref, sl_ref, out_ref):
    half_radix = RADIX // 2
    block_total = spec_ref.shape[0]
    step_templates = bank_ref.shape[0]
    pair_total = step_templates * block_total
    products = []
    scales = []
    for template in range(step_templates):
        wave_real = bank_ref[template, 0].astype(jnp.float32)
        wave_imag = bank_ref[template, 1].astype(jnp.float32)
        power_sum = jnp.sum(wave_real * wave_real + wave_imag * wave_imag, keepdims=True)
        norm_scale = 1.0 / jnp.sqrt(BLOCK * power_sum + EPSILON)
        scales.append(norm_scale * norm_scale)
        for block in range(block_total):
            spec_real = spec_ref[block, :, :RADIX]
            spec_imag = spec_ref[block, :, RADIX:]
            prod_real = spec_real * wave_real + spec_imag * wave_imag
            prod_imag = spec_imag * wave_real - spec_real * wave_imag
            products.append(jnp.concatenate([prod_real, prod_imag], axis=0))
    stacked = jnp.concatenate(products, axis=1)
    stacked_high, stacked_low = split_pair(stacked)
    first = triple_dot(fh_ref[...], fl_ref[...], stacked_high, stacked_low)
    cos_twist = tc_ref[...]
    sin_twist = ts_ref[...]
    turned_rows = []
    for pair in range(pair_total):
        real_part = first[:RADIX, pair * RADIX : (pair + 1) * RADIX]
        imag_part = first[RADIX:, pair * RADIX : (pair + 1) * RADIX]
        turned_rows.append(
            jnp.concatenate(
                [
                    real_part * cos_twist - imag_part * sin_twist,
                    real_part * sin_twist + imag_part * cos_twist,
                ],
                axis=1,
            )
        )
    turned = jnp.concatenate(turned_rows, axis=0)
    turned_high, turned_low = split_pair(turned)
    series = triple_dot(turned_high, turned_low, sh_ref[...], sl_ref[...])
    power_series = (
        series[:, :half_radix] * series[:, :half_radix]
        + series[:, half_radix:] * series[:, half_radix:]
    )
    peaks = jnp.max(power_series.reshape(pair_total, RADIX, half_radix), axis=1)
    for template in range(step_templates):
        rows = peaks[template * block_total : (template + 1) * block_total]
        out_ref[template] = rows * scales[template]


def window_peaks(spectra, bank, tables):
    block_total, k_rows, _ = spectra.shape
    template_total = bank.shape[0]
    step_templates = STEP_TEMPLATES if template_total % STEP_TEMPLATES == 0 else 1
    fixed = lambda k: (0, 0)
    pair_flops = 6 * (2 * RADIX) * (2 * k_rows) * RADIX + 6 * RADIX * (2 * RADIX) * RADIX
    return pl.pallas_call(
        peaks_kernel,
        out_shape=jax.ShapeDtypeStruct((template_total, block_total, RADIX // 2), jnp.float32),
        grid=(template_total // step_templates,),
        in_specs=[
            pl.BlockSpec((block_total, k_rows, 2 * RADIX), lambda k: (0, 0, 0)),
            pl.BlockSpec((step_templates, 2, k_rows, RADIX), lambda k: (k, 0, 0, 0)),
            pl.BlockSpec((2 * RADIX, 2 * k_rows), fixed),
            pl.BlockSpec((2 * RADIX, 2 * k_rows), fixed),
            pl.BlockSpec((RADIX, RADIX), fixed),
            pl.BlockSpec((RADIX, RADIX), fixed),
            pl.BlockSpec((2 * RADIX, RADIX), fixed),
            pl.BlockSpec((2 * RADIX, RADIX), fixed),
        ],
        out_specs=pl.BlockSpec((step_templates, block_total, RADIX // 2), lambda k: (k, 0, 0)),
        compiler_params=pltpu.CompilerParams(dimension_semantics=("arbitrary",)),
        cost_estimate=pl.CostEstimate(
            flops=pair_flops * template_total * block_total,
            transcendentals=0,
            bytes_accessed=spectra.size * 4 + bank.size * 2 + template_total * block_total * RADIX * 2,
        ),
    )(spectra, bank, *tables)


def gathered_half(template_bank, start, count):
    seg_total = lax.axis_size("seg")
    me = lax.axis_index("seg")
    core = me % 2
    template_total, parts, local_bins = template_bank.shape
    half = template_total // 2
    mine = lax.dynamic_slice_in_dim(template_bank, core * half + start, count, axis=0)
    theirs = lax.dynamic_slice_in_dim(template_bank, (1 - core) * half + start, count, axis=0)
    arrived = lax.ppermute(theirs[None], "seg", [(i, i ^ 1) for i in range(seg_total)])
    upper = core != 0
    held = jnp.stack([jnp.where(upper, arrived, mine[None]), jnp.where(upper, mine[None], arrived)], axis=0)
    order = [1]
    distance = seg_total // 2
    while distance > 1:
        pairs = [(i, i ^ distance) for i in range(seg_total)]
        arrived = lax.ppermute(held, "seg", pairs)
        upper = (me & distance) != 0
        held = jnp.stack([jnp.where(upper, arrived, held), jnp.where(upper, held, arrived)], axis=0)
        order.append(distance)
        distance //= 2
    steps = len(order)
    held = held.reshape((2,) * steps + (count, parts, local_bins // RADIX, RADIX))
    axis_distance = list(reversed(order))
    bit_axes = tuple(sorted(range(steps), key=lambda axis: -axis_distance[axis]))
    held = jnp.transpose(held, (steps, steps + 1) + bit_axes + (steps + 2, steps + 3))
    return held.reshape(count, parts, seg_total * local_bins // RADIX, RADIX)


def local(strain, gate_mask, template_bank):
    seg_total = lax.axis_size("seg")
    core = lax.axis_index("seg") % 2
    half = template_bank.shape[0] // 2
    banks = [gathered_half(template_bank, start, SUBHALF) for start in range(0, half, SUBHALF)]
    gated = strain * gate_mask.astype(jnp.float32)
    local_blocks = gated.reshape(-1, BLOCK)
    block_total = local_blocks.shape[0]
    earlier = passed_along(local_blocks[block_total - 1], "seg", 1)
    mine = jnp.concatenate([earlier[None], local_blocks], axis=0)
    other = lax.ppermute(mine, "seg", [(i, i ^ 1) for i in range(seg_total)])
    chip_blocks = jnp.where(
        core == 0,
        jnp.concatenate([mine, other[1:]], axis=0),
        jnp.concatenate([other, mine[1:]], axis=0),
    )
    windows = jnp.concatenate([chip_blocks[:-1], chip_blocks[1:]], axis=1)
    spectra = forward(windows)
    tables = inverse_tables(spectra.shape[1])
    partner_spectra = lax.dynamic_slice_in_dim(spectra, (1 - core) * block_total, block_total, axis=0)
    own_spectra = lax.dynamic_slice_in_dim(spectra, core * block_total, block_total, axis=0)
    own_parts = []
    returned_parts = []
    for bank in banks:
        partner_peaks = window_peaks(partner_spectra, bank, tables).reshape(SUBHALF, block_total * (RADIX // 2))
        returned_parts.append(lax.ppermute(partner_peaks, "seg", [(i, i ^ 1) for i in range(seg_total)]))
        own_parts.append(window_peaks(own_spectra, bank, tables).reshape(SUBHALF, block_total * (RADIX // 2)))
    own_peaks = jnp.concatenate(own_parts, axis=0)
    returned = jnp.concatenate(returned_parts, axis=0)
    return jnp.where(
        core == 0,
        jnp.concatenate([own_peaks, returned], axis=0),
        jnp.concatenate([returned, own_peaks], axis=0),
    )


def solution(mesh):
    in_specs = (P(("grp", "seg")), P(("grp", "seg")), P("grp", None, "seg"))
    out_specs = P(None, ("grp", "seg"))
    return jax.shard_map(local, mesh=mesh, in_specs=in_specs, out_specs=out_specs, check_vma=False)
```

```python
import math

import jax
import jax.numpy as jnp
from jax import lax
from jax.experimental import pallas as pl
from jax.experimental.pallas import tpu as pltpu
from jax.sharding import PartitionSpec as P

RADIX = 256
BLOCK = 32768
SUBBANK = 8
STEP_TEMPLATES = 2


PRECISE = lax.Precision.HIGH
EPSILON = 1e-06


def passed_along(value, axis, by):
    count = lax.axis_size(axis)
    pairs = [(i, i + by) for i in range(count) if 0 <= i + by < count]
    return lax.ppermute(value, axis, pairs)


def angle_table(row_count, col_count, period):
    row_index = lax.broadcasted_iota(jnp.int32, (row_count, col_count), 0)
    col_index = lax.broadcasted_iota(jnp.int32, (row_count, col_count), 1)
    phase_step = row_index * col_index % period
    angle_value = phase_step.astype(jnp.float32) * (2.0 * math.pi / period)
    return (jnp.cos(angle_value), jnp.sin(angle_value))


def forward(windows):
    half_radix = RADIX // 2
    window_total = windows.shape[0]
    rows = windows.shape[1] // RADIX
    block_grid = windows.reshape(window_total, rows, RADIX)
    cos_first, sin_first = angle_table(rows, RADIX, RADIX)
    first_table = jnp.concatenate([cos_first, -sin_first], axis=1)
    first_section = jnp.einsum("bnm,nf->bmf", block_grid, first_table, precision=PRECISE)
    cos_twist, sin_twist = angle_table(RADIX, RADIX, RADIX * RADIX)
    real_part = first_section[..., :RADIX]
    imag_part = first_section[..., RADIX:]
    turned = jnp.concatenate(
        [
            real_part * cos_twist + imag_part * sin_twist,
            imag_part * cos_twist - real_part * sin_twist,
        ],
        axis=-1,
    )
    cos_second, sin_second = angle_table(RADIX, half_radix, RADIX)
    cosine_part = jnp.einsum("bnf,nk->bkf", turned, cos_second, precision=PRECISE)
    sine_part = jnp.einsum("bnf,nk->bkf", turned, sin_second, precision=PRECISE)
    return jnp.concatenate(
        [
            cosine_part[..., :RADIX] + sine_part[..., RADIX:],
            cosine_part[..., RADIX:] - sine_part[..., :RADIX],
        ],
        axis=-1,
    )


def split_pair(value):
    high = value.astype(jnp.bfloat16)
    low = (value - high.astype(jnp.float32)).astype(jnp.bfloat16)
    return high, low


def table_pair(value):
    high = lax.reduce_precision(value, exponent_bits=8, mantissa_bits=7)
    return high.astype(jnp.bfloat16), (value - high).astype(jnp.bfloat16)


def triple_dot(left_high, left_low, right_high, right_low):
    total = jnp.dot(left_high, right_high, preferred_element_type=jnp.float32)
    total = total + jnp.dot(left_high, right_low, preferred_element_type=jnp.float32)
    return total + jnp.dot(left_low, right_high, preferred_element_type=jnp.float32)


def inverse_tables(k_rows):
    half_radix = RADIX // 2
    cos_first, sin_first = angle_table(RADIX, k_rows, RADIX)
    first = jnp.concatenate(
        [
            jnp.concatenate([cos_first, -sin_first], axis=1),
            jnp.concatenate([sin_first, cos_first], axis=1),
        ],
        axis=0,
    )
    cos_twist, sin_twist = angle_table(RADIX, RADIX, RADIX * RADIX)
    cos_out, sin_out = angle_table(RADIX, RADIX, RADIX)
    real_cols = jnp.concatenate([cos_out, -sin_out], axis=0)
    imag_cols = jnp.concatenate([sin_out, cos_out], axis=0)
    second = jnp.concatenate([real_cols[:, half_radix:], imag_cols[:, half_radix:]], axis=1)
    first_high, first_low = table_pair(first)
    second_high, second_low = table_pair(second)
    return first_high, first_low, cos_twist, sin_twist, second_high, second_low


def peaks_kernel(spec_ref, bank_ref, fh_ref, fl_ref, tc_ref, ts_ref, sh_ref, sl_ref, out_ref):
    half_radix = RADIX // 2
    block_total = spec_ref.shape[0]
    step_templates = bank_ref.shape[0]
    pair_total = step_templates * block_total
    products = []
    scales = []
    for template in range(step_templates):
        wave_real = bank_ref[template, 0].astype(jnp.float32)
        wave_imag = bank_ref[template, 1].astype(jnp.float32)
        power_sum = jnp.sum(wave_real * wave_real + wave_imag * wave_imag, keepdims=True)
        norm_scale = 1.0 / jnp.sqrt(BLOCK * power_sum + EPSILON)
        scales.append(norm_scale * norm_scale)
        for block in range(block_total):
            spec_real = spec_ref[block, :, :RADIX]
            spec_imag = spec_ref[block, :, RADIX:]
            prod_real = spec_real * wave_real + spec_imag * wave_imag
            prod_imag = spec_imag * wave_real - spec_real * wave_imag
            products.append(jnp.concatenate([prod_real, prod_imag], axis=0))
    stacked = jnp.concatenate(products, axis=1)
    stacked_high, stacked_low = split_pair(stacked)
    first = triple_dot(fh_ref[...], fl_ref[...], stacked_high, stacked_low)
    cos_twist = tc_ref[...]
    sin_twist = ts_ref[...]
    turned_rows = []
    for pair in range(pair_total):
        real_part = first[:RADIX, pair * RADIX : (pair + 1) * RADIX]
        imag_part = first[RADIX:, pair * RADIX : (pair + 1) * RADIX]
        turned_rows.append(
            jnp.concatenate(
                [
                    real_part * cos_twist - imag_part * sin_twist,
                    real_part * sin_twist + imag_part * cos_twist,
                ],
                axis=1,
            )
        )
    turned = jnp.concatenate(turned_rows, axis=0)
    turned_high, turned_low = split_pair(turned)
    series = triple_dot(turned_high, turned_low, sh_ref[...], sl_ref[...])
    power_series = (
        series[:, :half_radix] * series[:, :half_radix]
        + series[:, half_radix:] * series[:, half_radix:]
    )
    peaks = jnp.max(power_series.reshape(pair_total, RADIX, half_radix), axis=1)
    for template in range(step_templates):
        rows = peaks[template * block_total : (template + 1) * block_total]
        out_ref[template] = rows * scales[template]


def window_peaks(spectra, bank, tables):
    block_total, k_rows, _ = spectra.shape
    template_total = bank.shape[0]
    step_templates = STEP_TEMPLATES if template_total % STEP_TEMPLATES == 0 else 1
    fixed = lambda k: (0, 0)
    pair_flops = 6 * (2 * RADIX) * (2 * k_rows) * RADIX + 6 * RADIX * (2 * RADIX) * RADIX
    return pl.pallas_call(
        peaks_kernel,
        out_shape=jax.ShapeDtypeStruct((template_total, block_total, RADIX // 2), jnp.float32),
        grid=(template_total // step_templates,),
        in_specs=[
            pl.BlockSpec((block_total, k_rows, 2 * RADIX), lambda k: (0, 0, 0)),
            pl.BlockSpec((step_templates, 2, k_rows, RADIX), lambda k: (k, 0, 0, 0)),
            pl.BlockSpec((2 * RADIX, 2 * k_rows), fixed),
            pl.BlockSpec((2 * RADIX, 2 * k_rows), fixed),
            pl.BlockSpec((RADIX, RADIX), fixed),
            pl.BlockSpec((RADIX, RADIX), fixed),
            pl.BlockSpec((2 * RADIX, RADIX), fixed),
            pl.BlockSpec((2 * RADIX, RADIX), fixed),
        ],
        out_specs=pl.BlockSpec((step_templates, block_total, RADIX // 2), lambda k: (k, 0, 0)),
        compiler_params=pltpu.CompilerParams(dimension_semantics=("arbitrary",)),
        cost_estimate=pl.CostEstimate(
            flops=pair_flops * template_total * block_total,
            transcendentals=0,
            bytes_accessed=spectra.size * 4 + bank.size * 2 + template_total * block_total * RADIX * 2,
        ),
    )(spectra, bank, *tables)


def gathered_half(template_bank):
    seg_total = lax.axis_size("seg")
    me = lax.axis_index("seg")
    core = me % 2
    template_total, parts, local_bins = template_bank.shape
    half = template_total // 2
    mine = lax.dynamic_slice_in_dim(template_bank, core * half, half, axis=0)
    theirs = lax.dynamic_slice_in_dim(template_bank, (1 - core) * half, half, axis=0)
    arrived = lax.ppermute(theirs[None], "seg", [(i, i ^ 1) for i in range(seg_total)])
    upper = core != 0
    held = jnp.stack([jnp.where(upper, arrived, mine[None]), jnp.where(upper, mine[None], arrived)], axis=0)
    odd_order = []
    distance = seg_total // 2
    while distance > 1:
        odd_order.append(distance)
        distance //= 2
    even_order = odd_order[:-2] + odd_order[-2:][::-1]
    for even_distance, odd_distance in zip(even_order, odd_order):
        pairs = [(i, i ^ (even_distance if i % 2 == 0 else odd_distance)) for i in range(seg_total)]
        arrived = lax.ppermute(held, "seg", pairs)
        upper = (me & jnp.where(core == 0, even_distance, odd_distance)) != 0
        held = jnp.stack([jnp.where(upper, arrived, held), jnp.where(upper, held, arrived)], axis=0)
    steps = len(odd_order) + 1
    held = held.reshape((2,) * steps + (half, parts, local_bins // RADIX, RADIX))

    def in_bin_order(order):
        axis_distance = list(reversed([1] + order))
        bit_axes = tuple(sorted(range(steps), key=lambda axis: -axis_distance[axis]))
        return jnp.transpose(held, (steps, steps + 1) + bit_axes + (steps + 2, steps + 3))

    held = jnp.where(core == 0, in_bin_order(even_order), in_bin_order(odd_order))
    return held.reshape(half, parts, seg_total * local_bins // RADIX, RADIX)


def local(strain, gate_mask, template_bank):
    seg_total = lax.axis_size("seg")
    core = lax.axis_index("seg") % 2
    bank = gathered_half(template_bank)
    gated = strain * gate_mask.astype(jnp.float32)
    local_blocks = gated.reshape(-1, BLOCK)
    block_total = local_blocks.shape[0]
    earlier = passed_along(local_blocks[block_total - 1], "seg", 1)
    mine = jnp.concatenate([earlier[None], local_blocks], axis=0)
    other = lax.ppermute(mine, "seg", [(i, i ^ 1) for i in range(seg_total)])
    chip_blocks = jnp.where(
        core == 0,
        jnp.concatenate([mine, other[1:]], axis=0),
        jnp.concatenate([other, mine[1:]], axis=0),
    )
    windows = jnp.concatenate([chip_blocks[:-1], chip_blocks[1:]], axis=1)
    spectra = forward(windows)
    tables = inverse_tables(spectra.shape[1])
    partner_spectra = lax.dynamic_slice_in_dim(spectra, (1 - core) * block_total, block_total, axis=0)
    own_spectra = lax.dynamic_slice_in_dim(spectra, core * block_total, block_total, axis=0)
    half = bank.shape[0]
    partner_peaks = window_peaks(partner_spectra, bank, tables).reshape(half, block_total * (RADIX // 2))
    returned = lax.ppermute(partner_peaks, "seg", [(i, i ^ 1) for i in range(seg_total)])
    own_peaks = window_peaks(own_spectra, bank, tables).reshape(half, block_total * (RADIX // 2))
    return jnp.where(
        core == 0,
        jnp.concatenate([own_peaks, returned], axis=0),
        jnp.concatenate([returned, own_peaks], axis=0),
    )


def solution(mesh):
    in_specs = (P(("grp", "seg")), P(("grp", "seg")), P("grp", None, "seg"))
    out_specs = P(None, ("grp", "seg"))
    return jax.shard_map(local, mesh=mesh, in_specs=in_specs, out_specs=out_specs, check_vma=False)
```

```python
import math

import jax
import jax.numpy as jnp
from jax import lax
from jax.experimental import pallas as pl
from jax.experimental.pallas import tpu as pltpu
from jax.sharding import PartitionSpec as P

RADIX = 256
BLOCK = 32768
SUBBANK = 8
STEP_TEMPLATES = 2


PRECISE = lax.Precision.HIGH
EPSILON = 1e-06


def passed_along(value, axis, by):
    count = lax.axis_size(axis)
    pairs = [(i, i + by) for i in range(count) if 0 <= i + by < count]
    return lax.ppermute(value, axis, pairs)


def angle_table(row_count, col_count, period):
    row_index = lax.broadcasted_iota(jnp.int32, (row_count, col_count), 0)
    col_index = lax.broadcasted_iota(jnp.int32, (row_count, col_count), 1)
    phase_step = row_index * col_index % period
    angle_value = phase_step.astype(jnp.float32) * (2.0 * math.pi / period)
    return (jnp.cos(angle_value), jnp.sin(angle_value))


def forward(windows):
    half_radix = RADIX // 2
    window_total = windows.shape[0]
    rows = windows.shape[1] // RADIX
    block_grid = windows.reshape(window_total, rows, RADIX)
    cos_first, sin_first = angle_table(rows, RADIX, RADIX)
    first_table = jnp.concatenate([cos_first, -sin_first], axis=1)
    first_section = jnp.einsum("bnm,nf->bmf", block_grid, first_table, precision=PRECISE)
    cos_twist, sin_twist = angle_table(RADIX, RADIX, RADIX * RADIX)
    real_part = first_section[..., :RADIX]
    imag_part = first_section[..., RADIX:]
    turned = jnp.concatenate(
        [
            real_part * cos_twist + imag_part * sin_twist,
            imag_part * cos_twist - real_part * sin_twist,
        ],
        axis=-1,
    )
    cos_second, sin_second = angle_table(RADIX, half_radix, RADIX)
    cosine_part = jnp.einsum("bnf,nk->bkf", turned, cos_second, precision=PRECISE)
    sine_part = jnp.einsum("bnf,nk->bkf", turned, sin_second, precision=PRECISE)
    return jnp.concatenate(
        [
            cosine_part[..., :RADIX] + sine_part[..., RADIX:],
            cosine_part[..., RADIX:] - sine_part[..., :RADIX],
        ],
        axis=-1,
    )


def split_pair(value):
    high = value.astype(jnp.bfloat16)
    low = (value - high.astype(jnp.float32)).astype(jnp.bfloat16)
    return high, low


def table_pair(value):
    high = lax.reduce_precision(value, exponent_bits=8, mantissa_bits=7)
    return high.astype(jnp.bfloat16), (value - high).astype(jnp.bfloat16)


def triple_dot(left_high, left_low, right_high, right_low):
    total = jnp.dot(left_high, right_high, preferred_element_type=jnp.float32)
    total = total + jnp.dot(left_high, right_low, preferred_element_type=jnp.float32)
    return total + jnp.dot(left_low, right_high, preferred_element_type=jnp.float32)


def inverse_tables(k_rows):
    half_radix = RADIX // 2
    cos_first, sin_first = angle_table(RADIX, k_rows, RADIX)
    first = jnp.concatenate(
        [
            jnp.concatenate([cos_first, -sin_first], axis=1),
            jnp.concatenate([sin_first, cos_first], axis=1),
        ],
        axis=0,
    )
    cos_twist, sin_twist = angle_table(RADIX, RADIX, RADIX * RADIX)
    cos_out, sin_out = angle_table(RADIX, RADIX, RADIX)
    real_cols = jnp.concatenate([cos_out, -sin_out], axis=0)
    imag_cols = jnp.concatenate([sin_out, cos_out], axis=0)
    second = jnp.concatenate([real_cols[:, half_radix:], imag_cols[:, half_radix:]], axis=1)
    first_high, first_low = table_pair(first)
    second_high, second_low = table_pair(second)
    return first_high, first_low, cos_twist, sin_twist, second_high, second_low


def peaks_kernel(spec_ref, bank_ref, fh_ref, fl_ref, tc_ref, ts_ref, sh_ref, sl_ref, out_ref):
    half_radix = RADIX // 2
    block_total = spec_ref.shape[0]
    step_templates = bank_ref.shape[0]
    pair_total = step_templates * block_total
    products = []
    scales = []
    for template in range(step_templates):
        wave_real = bank_ref[template, 0].astype(jnp.float32)
        wave_imag = bank_ref[template, 1].astype(jnp.float32)
        power_sum = jnp.sum(wave_real * wave_real + wave_imag * wave_imag, keepdims=True)
        norm_scale = 1.0 / jnp.sqrt(BLOCK * power_sum + EPSILON)
        scales.append(norm_scale * norm_scale)
        for block in range(block_total):
            spec_real = spec_ref[block, :, :RADIX]
            spec_imag = spec_ref[block, :, RADIX:]
            prod_real = spec_real * wave_real + spec_imag * wave_imag
            prod_imag = spec_imag * wave_real - spec_real * wave_imag
            products.append(jnp.concatenate([prod_real, prod_imag], axis=0))
    stacked = jnp.concatenate(products, axis=1)
    stacked_high, stacked_low = split_pair(stacked)
    first = triple_dot(fh_ref[...], fl_ref[...], stacked_high, stacked_low)
    cos_twist = tc_ref[...]
    sin_twist = ts_ref[...]
    turned_rows = []
    for pair in range(pair_total):
        real_part = first[:RADIX, pair * RADIX : (pair + 1) * RADIX]
        imag_part = first[RADIX:, pair * RADIX : (pair + 1) * RADIX]
        turned_rows.append(
            jnp.concatenate(
                [
                    real_part * cos_twist - imag_part * sin_twist,
                    real_part * sin_twist + imag_part * cos_twist,
                ],
                axis=1,
            )
        )
    turned = jnp.concatenate(turned_rows, axis=0)
    turned_high, turned_low = split_pair(turned)
    series = triple_dot(turned_high, turned_low, sh_ref[...], sl_ref[...])
    power_series = (
        series[:, :half_radix] * series[:, :half_radix]
        + series[:, half_radix:] * series[:, half_radix:]
    )
    peaks = jnp.max(power_series.reshape(pair_total, RADIX, half_radix), axis=1)
    for template in range(step_templates):
        rows = peaks[template * block_total : (template + 1) * block_total]
        out_ref[template] = rows * scales[template]


def window_peaks(spectra, bank, tables):
    block_total, k_rows, _ = spectra.shape
    template_total = bank.shape[0]
    step_templates = STEP_TEMPLATES if template_total % STEP_TEMPLATES == 0 else 1
    fixed = lambda k: (0, 0)
    pair_flops = 6 * (2 * RADIX) * (2 * k_rows) * RADIX + 6 * RADIX * (2 * RADIX) * RADIX
    return pl.pallas_call(
        peaks_kernel,
        out_shape=jax.ShapeDtypeStruct((template_total, block_total, RADIX // 2), jnp.float32),
        grid=(template_total // step_templates,),
        in_specs=[
            pl.BlockSpec((block_total, k_rows, 2 * RADIX), lambda k: (0, 0, 0)),
            pl.BlockSpec((step_templates, 2, k_rows, RADIX), lambda k: (k, 0, 0, 0)),
            pl.BlockSpec((2 * RADIX, 2 * k_rows), fixed),
            pl.BlockSpec((2 * RADIX, 2 * k_rows), fixed),
            pl.BlockSpec((RADIX, RADIX), fixed),
            pl.BlockSpec((RADIX, RADIX), fixed),
            pl.BlockSpec((2 * RADIX, RADIX), fixed),
            pl.BlockSpec((2 * RADIX, RADIX), fixed),
        ],
        out_specs=pl.BlockSpec((step_templates, block_total, RADIX // 2), lambda k: (k, 0, 0)),
        compiler_params=pltpu.CompilerParams(dimension_semantics=("arbitrary",)),
        cost_estimate=pl.CostEstimate(
            flops=pair_flops * template_total * block_total,
            transcendentals=0,
            bytes_accessed=spectra.size * 4 + bank.size * 2 + template_total * block_total * RADIX * 2,
        ),
    )(spectra, bank, *tables)


def gathered_half(template_bank):
    seg_total = lax.axis_size("seg")
    me = lax.axis_index("seg")
    core = me % 2
    template_total, parts, local_bins = template_bank.shape
    half = template_total // 2
    held = template_bank[None]
    odd_order = []
    distance = seg_total // 2
    while distance > 1:
        odd_order.append(distance)
        distance //= 2
    even_order = odd_order[:-2] + odd_order[-2:][::-1]
    for even_distance, odd_distance in zip(even_order, odd_order):
        pairs = [(i, i ^ (even_distance if i % 2 == 0 else odd_distance)) for i in range(seg_total)]
        arrived = lax.ppermute(held, "seg", pairs)
        upper = (me & jnp.where(core == 0, even_distance, odd_distance)) != 0
        held = jnp.stack([jnp.where(upper, arrived, held), jnp.where(upper, held, arrived)], axis=0)
    template_axis = len(odd_order) + 1
    mine = lax.dynamic_slice_in_dim(held, core * half, half, axis=template_axis)
    theirs = lax.dynamic_slice_in_dim(held, (1 - core) * half, half, axis=template_axis)
    arrived = lax.ppermute(theirs, "seg", [(i, i ^ 1) for i in range(seg_total)])
    arrived = jnp.swapaxes(arrived, 0, 1)
    upper = core != 0
    held = jnp.stack([jnp.where(upper, arrived, mine), jnp.where(upper, mine, arrived)], axis=0)
    steps = len(odd_order) + 1
    held = held.reshape((2,) * steps + (half, parts, local_bins // RADIX, RADIX))

    def in_bin_order(order):
        axis_distance = list(reversed(order + [1]))
        bit_axes = tuple(sorted(range(steps), key=lambda axis: -axis_distance[axis]))
        return jnp.transpose(held, (steps, steps + 1) + bit_axes + (steps + 2, steps + 3))

    held = jnp.where(core == 0, in_bin_order(even_order), in_bin_order(odd_order))
    return held.reshape(half, parts, seg_total * local_bins // RADIX, RADIX)


def local(strain, gate_mask, template_bank):
    seg_total = lax.axis_size("seg")
    core = lax.axis_index("seg") % 2
    bank = gathered_half(template_bank)
    gated = strain * gate_mask.astype(jnp.float32)
    local_blocks = gated.reshape(-1, BLOCK)
    block_total = local_blocks.shape[0]
    earlier = passed_along(local_blocks[block_total - 1], "seg", 1)
    mine = jnp.concatenate([earlier[None], local_blocks], axis=0)
    other = lax.ppermute(mine, "seg", [(i, i ^ 1) for i in range(seg_total)])
    chip_blocks = jnp.where(
        core == 0,
        jnp.concatenate([mine, other[1:]], axis=0),
        jnp.concatenate([other, mine[1:]], axis=0),
    )
    windows = jnp.concatenate([chip_blocks[:-1], chip_blocks[1:]], axis=1)
    spectra = forward(windows)
    tables = inverse_tables(spectra.shape[1])
    partner_spectra = lax.dynamic_slice_in_dim(spectra, (1 - core) * block_total, block_total, axis=0)
    own_spectra = lax.dynamic_slice_in_dim(spectra, core * block_total, block_total, axis=0)
    half = bank.shape[0]
    partner_peaks = window_peaks(partner_spectra, bank, tables).reshape(half, block_total * (RADIX // 2))
    returned = lax.ppermute(partner_peaks, "seg", [(i, i ^ 1) for i in range(seg_total)])
    own_peaks = window_peaks(own_spectra, bank, tables).reshape(half, block_total * (RADIX // 2))
    return jnp.where(
        core == 0,
        jnp.concatenate([own_peaks, returned], axis=0),
        jnp.concatenate([returned, own_peaks], axis=0),
    )


def solution(mesh):
    in_specs = (P(("grp", "seg")), P(("grp", "seg")), P("grp", None, "seg"))
    out_specs = P(None, ("grp", "seg"))
    return jax.shard_map(local, mesh=mesh, in_specs=in_specs, out_specs=out_specs, check_vma=False)
```

```python
import math

import jax
import jax.numpy as jnp
from jax import lax
from jax.experimental import pallas as pl
from jax.experimental.pallas import tpu as pltpu
from jax.sharding import PartitionSpec as P

RADIX = 256
BLOCK = 32768
SUBBANK = 8
STEP_TEMPLATES = 2


PRECISE = lax.Precision.HIGH
EPSILON = 1e-06


def passed_along(value, axis, by):
    count = lax.axis_size(axis)
    pairs = [(i, i + by) for i in range(count) if 0 <= i + by < count]
    return lax.ppermute(value, axis, pairs)


def angle_table(row_count, col_count, period):
    row_index = lax.broadcasted_iota(jnp.int32, (row_count, col_count), 0)
    col_index = lax.broadcasted_iota(jnp.int32, (row_count, col_count), 1)
    phase_step = row_index * col_index % period
    angle_value = phase_step.astype(jnp.float32) * (2.0 * math.pi / period)
    return (jnp.cos(angle_value), jnp.sin(angle_value))


def forward(windows):
    half_radix = RADIX // 2
    window_total = windows.shape[0]
    rows = windows.shape[1] // RADIX
    block_grid = windows.reshape(window_total, rows, RADIX)
    cos_first, sin_first = angle_table(rows, RADIX, RADIX)
    first_table = jnp.concatenate([cos_first, -sin_first], axis=1)
    first_section = jnp.einsum("bnm,nf->bmf", block_grid, first_table, precision=PRECISE)
    cos_twist, sin_twist = angle_table(RADIX, RADIX, RADIX * RADIX)
    real_part = first_section[..., :RADIX]
    imag_part = first_section[..., RADIX:]
    turned = jnp.concatenate(
        [
            real_part * cos_twist + imag_part * sin_twist,
            imag_part * cos_twist - real_part * sin_twist,
        ],
        axis=-1,
    )
    cos_second, sin_second = angle_table(RADIX, half_radix, RADIX)
    cosine_part = jnp.einsum("bnf,nk->bkf", turned, cos_second, precision=PRECISE)
    sine_part = jnp.einsum("bnf,nk->bkf", turned, sin_second, precision=PRECISE)
    return jnp.concatenate(
        [
            cosine_part[..., :RADIX] + sine_part[..., RADIX:],
            cosine_part[..., RADIX:] - sine_part[..., :RADIX],
        ],
        axis=-1,
    )


def split_pair(value):
    high = value.astype(jnp.bfloat16)
    low = (value - high.astype(jnp.float32)).astype(jnp.bfloat16)
    return high, low


def table_pair(value):
    high = lax.reduce_precision(value, exponent_bits=8, mantissa_bits=7)
    return high.astype(jnp.bfloat16), (value - high).astype(jnp.bfloat16)


def triple_dot(left_high, left_low, right_high, right_low):
    total = jnp.dot(left_high, right_high, preferred_element_type=jnp.float32)
    total = total + jnp.dot(left_high, right_low, preferred_element_type=jnp.float32)
    return total + jnp.dot(left_low, right_high, preferred_element_type=jnp.float32)


def inverse_tables(k_rows):
    half_radix = RADIX // 2
    cos_first, sin_first = angle_table(RADIX, k_rows, RADIX)
    first = jnp.concatenate(
        [
            jnp.concatenate([cos_first, -sin_first], axis=1),
            jnp.concatenate([sin_first, cos_first], axis=1),
        ],
        axis=0,
    )
    cos_twist, sin_twist = angle_table(RADIX, RADIX, RADIX * RADIX)
    cos_out, sin_out = angle_table(RADIX, RADIX, RADIX)
    real_cols = jnp.concatenate([cos_out, -sin_out], axis=0)
    imag_cols = jnp.concatenate([sin_out, cos_out], axis=0)
    second = jnp.concatenate([real_cols[:, half_radix:], imag_cols[:, half_radix:]], axis=1)
    first_high, first_low = table_pair(first)
    second_high, second_low = table_pair(second)
    return first_high, first_low, cos_twist, sin_twist, second_high, second_low


def peaks_kernel(spec_ref, bank_ref, fh_ref, fl_ref, tc_ref, ts_ref, sh_ref, sl_ref, out_ref):
    half_radix = RADIX // 2
    block_total = spec_ref.shape[0]
    step_templates = bank_ref.shape[0]
    pair_total = step_templates * block_total
    products = []
    scales = []
    for template in range(step_templates):
        wave_real = bank_ref[template, 0].astype(jnp.float32)
        wave_imag = bank_ref[template, 1].astype(jnp.float32)
        power_sum = jnp.sum(wave_real * wave_real + wave_imag * wave_imag, keepdims=True)
        norm_scale = 1.0 / jnp.sqrt(BLOCK * power_sum + EPSILON)
        scales.append(norm_scale * norm_scale)
        for block in range(block_total):
            spec_real = spec_ref[block, :, :RADIX]
            spec_imag = spec_ref[block, :, RADIX:]
            prod_real = spec_real * wave_real + spec_imag * wave_imag
            prod_imag = spec_imag * wave_real - spec_real * wave_imag
            products.append(jnp.concatenate([prod_real, prod_imag], axis=0))
    stacked = jnp.concatenate(products, axis=1)
    stacked_high, stacked_low = split_pair(stacked)
    first = triple_dot(fh_ref[...], fl_ref[...], stacked_high, stacked_low)
    cos_twist = tc_ref[...]
    sin_twist = ts_ref[...]
    turned_rows = []
    for pair in range(pair_total):
        real_part = first[:RADIX, pair * RADIX : (pair + 1) * RADIX]
        imag_part = first[RADIX:, pair * RADIX : (pair + 1) * RADIX]
        turned_rows.append(
            jnp.concatenate(
                [
                    real_part * cos_twist - imag_part * sin_twist,
                    real_part * sin_twist + imag_part * cos_twist,
                ],
                axis=1,
            )
        )
    turned = jnp.concatenate(turned_rows, axis=0)
    turned_high, turned_low = split_pair(turned)
    series = triple_dot(turned_high, turned_low, sh_ref[...], sl_ref[...])
    power_series = (
        series[:, :half_radix] * series[:, :half_radix]
        + series[:, half_radix:] * series[:, half_radix:]
    )
    peaks = jnp.max(power_series.reshape(pair_total, RADIX, half_radix), axis=1)
    for template in range(step_templates):
        rows = peaks[template * block_total : (template + 1) * block_total]
        out_ref[template] = rows * scales[template]


def window_peaks(spectra, bank, tables):
    block_total, k_rows, _ = spectra.shape
    template_total = bank.shape[0]
    step_templates = STEP_TEMPLATES if template_total % STEP_TEMPLATES == 0 else 1
    fixed = lambda k: (0, 0)
    pair_flops = 6 * (2 * RADIX) * (2 * k_rows) * RADIX + 6 * RADIX * (2 * RADIX) * RADIX
    return pl.pallas_call(
        peaks_kernel,
        out_shape=jax.ShapeDtypeStruct((template_total, block_total, RADIX // 2), jnp.float32),
        grid=(template_total // step_templates,),
        in_specs=[
            pl.BlockSpec((block_total, k_rows, 2 * RADIX), lambda k: (0, 0, 0)),
            pl.BlockSpec((step_templates, 2, k_rows, RADIX), lambda k: (k, 0, 0, 0)),
            pl.BlockSpec((2 * RADIX, 2 * k_rows), fixed),
            pl.BlockSpec((2 * RADIX, 2 * k_rows), fixed),
            pl.BlockSpec((RADIX, RADIX), fixed),
            pl.BlockSpec((RADIX, RADIX), fixed),
            pl.BlockSpec((2 * RADIX, RADIX), fixed),
            pl.BlockSpec((2 * RADIX, RADIX), fixed),
        ],
        out_specs=pl.BlockSpec((step_templates, block_total, RADIX // 2), lambda k: (k, 0, 0)),
        compiler_params=pltpu.CompilerParams(dimension_semantics=("arbitrary",)),
        cost_estimate=pl.CostEstimate(
            flops=pair_flops * template_total * block_total,
            transcendentals=0,
            bytes_accessed=spectra.size * 4 + bank.size * 2 + template_total * block_total * RADIX * 2,
        ),
    )(spectra, bank, *tables)


def gathered_half(template_bank):
    seg_total = lax.axis_size("seg")
    me = lax.axis_index("seg")
    core = me % 2
    template_total, parts, local_bins = template_bank.shape
    half = template_total // 2
    mine = lax.dynamic_slice_in_dim(template_bank, core * half, half, axis=0)
    theirs = lax.dynamic_slice_in_dim(template_bank, (1 - core) * half, half, axis=0)
    arrived = lax.ppermute(theirs[None], "seg", [(i, i ^ 1) for i in range(seg_total)])
    upper = core != 0
    held = jnp.stack([jnp.where(upper, arrived, mine[None]), jnp.where(upper, mine[None], arrived)], axis=0)
    odd_order = []
    distance = seg_total // 2
    while distance > 1:
        odd_order.append(distance)
        distance //= 2
    even_order = odd_order[:-2] + odd_order[-2:][::-1]
    for even_distance, odd_distance in zip(even_order, odd_order):
        pairs = [(i, i ^ (even_distance if i % 2 == 0 else odd_distance)) for i in range(seg_total)]
        arrived = lax.ppermute(held, "seg", pairs)
        upper = (me & jnp.where(core == 0, even_distance, odd_distance)) != 0
        held = jnp.stack([jnp.where(upper, arrived, held), jnp.where(upper, held, arrived)], axis=0)
    steps = len(odd_order) + 1
    held = held.reshape((2,) * steps + (half, parts, local_bins // RADIX, RADIX))

    def in_bin_order(order):
        axis_distance = list(reversed([1] + order))
        bit_axes = tuple(sorted(range(steps), key=lambda axis: -axis_distance[axis]))
        return jnp.transpose(held, (steps, steps + 1) + bit_axes + (steps + 2, steps + 3))

    held = jnp.where(core == 0, in_bin_order(even_order), in_bin_order(odd_order))
    return held.reshape(half, parts, seg_total * local_bins // RADIX, RADIX)


def local(strain, gate_mask, template_bank):
    seg_total = lax.axis_size("seg")
    core = lax.axis_index("seg") % 2
    bank = gathered_half(template_bank)
    gated = strain * gate_mask.astype(jnp.float32)
    local_blocks = gated.reshape(-1, BLOCK)
    block_total = local_blocks.shape[0]
    earlier = passed_along(local_blocks[block_total - 1], "seg", 1)
    mine = jnp.concatenate([earlier[None], local_blocks], axis=0)
    other = lax.ppermute(mine, "seg", [(i, i ^ 1) for i in range(seg_total)])
    chip_blocks = jnp.where(
        core == 0,
        jnp.concatenate([mine, other[1:]], axis=0),
        jnp.concatenate([other, mine[1:]], axis=0),
    )
    windows = jnp.concatenate([chip_blocks[:-1], chip_blocks[1:]], axis=1)
    spectra = forward(windows)
    tables = inverse_tables(spectra.shape[1])
    partner_spectra = lax.dynamic_slice_in_dim(spectra, (1 - core) * block_total, block_total, axis=0)
    own_spectra = lax.dynamic_slice_in_dim(spectra, core * block_total, block_total, axis=0)
    half = bank.shape[0]
    partner_peaks = window_peaks(partner_spectra, bank, tables)
    returned = lax.ppermute(partner_peaks, "seg", [(i, i ^ 1) for i in range(seg_total)])
    own_peaks = window_peaks(own_spectra, bank, tables)
    peaks = jnp.where(
        core == 0,
        jnp.concatenate([own_peaks, returned], axis=0),
        jnp.concatenate([returned, own_peaks], axis=0),
    )
    return peaks.reshape(2 * half, block_total * (RADIX // 2))


def solution(mesh):
    in_specs = (P(("grp", "seg")), P(("grp", "seg")), P("grp", None, "seg"))
    out_specs = P(None, ("grp", "seg"))
    return jax.shard_map(local, mesh=mesh, in_specs=in_specs, out_specs=out_specs, check_vma=False)
```

```python
import math

import jax
import jax.numpy as jnp
from jax import lax
from jax.experimental import pallas as pl
from jax.experimental.pallas import tpu as pltpu
from jax.sharding import PartitionSpec as P

RADIX = 256
BLOCK = 32768
SUBBANK = 8
STEP_TEMPLATES = 2


PRECISE = lax.Precision.HIGH
EPSILON = 1e-06


def passed_along(value, axis, by):
    count = lax.axis_size(axis)
    pairs = [(i, i + by) for i in range(count) if 0 <= i + by < count]
    return lax.ppermute(value, axis, pairs)


def angle_table(row_count, col_count, period):
    row_index = lax.broadcasted_iota(jnp.int32, (row_count, col_count), 0)
    col_index = lax.broadcasted_iota(jnp.int32, (row_count, col_count), 1)
    phase_step = row_index * col_index % period
    angle_value = phase_step.astype(jnp.float32) * (2.0 * math.pi / period)
    return (jnp.cos(angle_value), jnp.sin(angle_value))


def forward(windows):
    half_radix = RADIX // 2
    window_total = windows.shape[0]
    rows = windows.shape[1] // RADIX
    block_grid = windows.reshape(window_total, rows, RADIX)
    cos_first, sin_first = angle_table(rows, RADIX, RADIX)
    first_table = jnp.concatenate([cos_first, -sin_first], axis=1)
    first_section = jnp.einsum("bnm,nf->bmf", block_grid, first_table, precision=PRECISE)
    cos_twist, sin_twist = angle_table(RADIX, RADIX, RADIX * RADIX)
    real_part = first_section[..., :RADIX]
    imag_part = first_section[..., RADIX:]
    turned = jnp.concatenate(
        [
            real_part * cos_twist + imag_part * sin_twist,
            imag_part * cos_twist - real_part * sin_twist,
        ],
        axis=-1,
    )
    cos_second, sin_second = angle_table(RADIX, half_radix, RADIX)
    cosine_part = jnp.einsum("bnf,nk->bkf", turned, cos_second, precision=PRECISE)
    sine_part = jnp.einsum("bnf,nk->bkf", turned, sin_second, precision=PRECISE)
    return jnp.concatenate(
        [
            cosine_part[..., :RADIX] + sine_part[..., RADIX:],
            cosine_part[..., RADIX:] - sine_part[..., :RADIX],
        ],
        axis=-1,
    )


def split_pair(value):
    high = value.astype(jnp.bfloat16)
    low = (value - high.astype(jnp.float32)).astype(jnp.bfloat16)
    return high, low


def table_pair(value):
    high = lax.reduce_precision(value, exponent_bits=8, mantissa_bits=7)
    return high.astype(jnp.bfloat16), (value - high).astype(jnp.bfloat16)


def inverse_tables(k_rows):
    half_radix = RADIX // 2
    cos_first, sin_first = angle_table(RADIX, k_rows, RADIX)
    first = jnp.concatenate(
        [
            jnp.concatenate([cos_first, -sin_first], axis=1),
            jnp.concatenate([sin_first, cos_first], axis=1),
        ],
        axis=0,
    )
    cos_twist, sin_twist = angle_table(RADIX, RADIX, RADIX * RADIX)
    cos_out, sin_out = angle_table(RADIX, RADIX, RADIX)
    real_cols = jnp.concatenate([cos_out, -sin_out], axis=0)
    imag_cols = jnp.concatenate([sin_out, cos_out], axis=0)
    second = jnp.concatenate([real_cols[:, half_radix:], imag_cols[:, half_radix:]], axis=1)
    first_high, first_low = table_pair(first)
    second_high, second_low = table_pair(second)
    first_cat = jnp.concatenate([first_high, first_high, first_low], axis=1)
    second_cat = jnp.concatenate([second_high, second_low, second_high], axis=0)
    return first_cat, cos_twist, sin_twist, second_cat


def peaks_kernel(spec_ref, bank_ref, first_ref, tc_ref, ts_ref, second_ref, out_ref):
    half_radix = RADIX // 2
    block_total = spec_ref.shape[0]
    step_templates = bank_ref.shape[0]
    pair_total = step_templates * block_total
    products = []
    scales = []
    for template in range(step_templates):
        wave_real = bank_ref[template, 0].astype(jnp.float32)
        wave_imag = bank_ref[template, 1].astype(jnp.float32)
        power_sum = jnp.sum(wave_real * wave_real + wave_imag * wave_imag, keepdims=True)
        norm_scale = 1.0 / jnp.sqrt(BLOCK * power_sum + EPSILON)
        scales.append(norm_scale * norm_scale)
        for block in range(block_total):
            spec_real = spec_ref[block, :, :RADIX]
            spec_imag = spec_ref[block, :, RADIX:]
            prod_real = spec_real * wave_real + spec_imag * wave_imag
            prod_imag = spec_imag * wave_real - spec_real * wave_imag
            products.append(jnp.concatenate([prod_real, prod_imag], axis=0))
    stacked = jnp.concatenate(products, axis=1)
    stacked_high, stacked_low = split_pair(stacked)
    first = jnp.dot(
        first_ref[...],
        jnp.concatenate([stacked_high, stacked_low, stacked_high], axis=0),
        preferred_element_type=jnp.float32,
    )
    cos_twist = tc_ref[...]
    sin_twist = ts_ref[...]
    turned_rows = []
    for pair in range(pair_total):
        real_part = first[:RADIX, pair * RADIX : (pair + 1) * RADIX]
        imag_part = first[RADIX:, pair * RADIX : (pair + 1) * RADIX]
        turned_rows.append(
            jnp.concatenate(
                [
                    real_part * cos_twist - imag_part * sin_twist,
                    real_part * sin_twist + imag_part * cos_twist,
                ],
                axis=1,
            )
        )
    turned = jnp.concatenate(turned_rows, axis=0)
    turned_high, turned_low = split_pair(turned)
    series = jnp.dot(
        jnp.concatenate([turned_high, turned_high, turned_low], axis=1),
        second_ref[...],
        preferred_element_type=jnp.float32,
    )
    power_series = (
        series[:, :half_radix] * series[:, :half_radix]
        + series[:, half_radix:] * series[:, half_radix:]
    )
    peaks = jnp.max(power_series.reshape(pair_total, RADIX, half_radix), axis=1)
    for template in range(step_templates):
        rows = peaks[template * block_total : (template + 1) * block_total]
        out_ref[template] = rows * scales[template]


def window_peaks(spectra, bank, tables):
    block_total, k_rows, _ = spectra.shape
    template_total = bank.shape[0]
    step_templates = STEP_TEMPLATES if template_total % STEP_TEMPLATES == 0 else 1
    fixed = lambda k: (0, 0)
    pair_flops = 6 * (2 * RADIX) * (2 * k_rows) * RADIX + 6 * RADIX * (2 * RADIX) * RADIX
    return pl.pallas_call(
        peaks_kernel,
        out_shape=jax.ShapeDtypeStruct((template_total, block_total, RADIX // 2), jnp.float32),
        grid=(template_total // step_templates,),
        in_specs=[
            pl.BlockSpec((block_total, k_rows, 2 * RADIX), lambda k: (0, 0, 0)),
            pl.BlockSpec((step_templates, 2, k_rows, RADIX), lambda k: (k, 0, 0, 0)),
            pl.BlockSpec((2 * RADIX, 6 * k_rows), fixed),
            pl.BlockSpec((RADIX, RADIX), fixed),
            pl.BlockSpec((RADIX, RADIX), fixed),
            pl.BlockSpec((6 * RADIX, RADIX), fixed),
        ],
        out_specs=pl.BlockSpec((step_templates, block_total, RADIX // 2), lambda k: (k, 0, 0)),
        compiler_params=pltpu.CompilerParams(dimension_semantics=("arbitrary",)),
        cost_estimate=pl.CostEstimate(
            flops=pair_flops * template_total * block_total,
            transcendentals=0,
            bytes_accessed=spectra.size * 4 + bank.size * 2 + template_total * block_total * RADIX * 2,
        ),
    )(spectra, bank, *tables)


def gathered_half(template_bank):
    seg_total = lax.axis_size("seg")
    me = lax.axis_index("seg")
    core = me % 2
    template_total, parts, local_bins = template_bank.shape
    half = template_total // 2
    mine = lax.dynamic_slice_in_dim(template_bank, core * half, half, axis=0)
    theirs = lax.dynamic_slice_in_dim(template_bank, (1 - core) * half, half, axis=0)
    arrived = lax.ppermute(theirs[None], "seg", [(i, i ^ 1) for i in range(seg_total)])
    upper = core != 0
    held = jnp.stack([jnp.where(upper, arrived, mine[None]), jnp.where(upper, mine[None], arrived)], axis=0)
    odd_order = []
    distance = seg_total // 2
    while distance > 1:
        odd_order.append(distance)
        distance //= 2
    even_order = odd_order[:-2] + odd_order[-2:][::-1]
    for even_distance, odd_distance in zip(even_order, odd_order):
        pairs = [(i, i ^ (even_distance if i % 2 == 0 else odd_distance)) for i in range(seg_total)]
        arrived = lax.ppermute(held, "seg", pairs)
        upper = (me & jnp.where(core == 0, even_distance, odd_distance)) != 0
        held = jnp.stack([jnp.where(upper, arrived, held), jnp.where(upper, held, arrived)], axis=0)
    steps = len(odd_order) + 1
    held = held.reshape((2,) * steps + (half, parts, local_bins // RADIX, RADIX))

    def in_bin_order(order):
        axis_distance = list(reversed([1] + order))
        bit_axes = tuple(sorted(range(steps), key=lambda axis: -axis_distance[axis]))
        return jnp.transpose(held, (steps, steps + 1) + bit_axes + (steps + 2, steps + 3))

    held = jnp.where(core == 0, in_bin_order(even_order), in_bin_order(odd_order))
    return held.reshape(half, parts, seg_total * local_bins // RADIX, RADIX)


def local(strain, gate_mask, template_bank):
    seg_total = lax.axis_size("seg")
    core = lax.axis_index("seg") % 2
    bank = gathered_half(template_bank)
    gated = strain * gate_mask.astype(jnp.float32)
    local_blocks = gated.reshape(-1, BLOCK)
    block_total = local_blocks.shape[0]
    earlier = passed_along(local_blocks[block_total - 1], "seg", 1)
    mine = jnp.concatenate([earlier[None], local_blocks], axis=0)
    other = lax.ppermute(mine, "seg", [(i, i ^ 1) for i in range(seg_total)])
    chip_blocks = jnp.where(
        core == 0,
        jnp.concatenate([mine, other[1:]], axis=0),
        jnp.concatenate([other, mine[1:]], axis=0),
    )
    windows = jnp.concatenate([chip_blocks[:-1], chip_blocks[1:]], axis=1)
    spectra = forward(windows)
    tables = inverse_tables(spectra.shape[1])
    partner_spectra = lax.dynamic_slice_in_dim(spectra, (1 - core) * block_total, block_total, axis=0)
    own_spectra = lax.dynamic_slice_in_dim(spectra, core * block_total, block_total, axis=0)
    half = bank.shape[0]
    partner_peaks = window_peaks(partner_spectra, bank, tables)
    returned = lax.ppermute(partner_peaks, "seg", [(i, i ^ 1) for i in range(seg_total)])
    own_peaks = window_peaks(own_spectra, bank, tables)
    peaks = jnp.where(
        core == 0,
        jnp.concatenate([own_peaks, returned], axis=0),
        jnp.concatenate([returned, own_peaks], axis=0),
    )
    return peaks.reshape(2 * half, block_total * (RADIX // 2))


def solution(mesh):
    in_specs = (P(("grp", "seg")), P(("grp", "seg")), P("grp", None, "seg"))
    out_specs = P(None, ("grp", "seg"))
    return jax.shard_map(local, mesh=mesh, in_specs=in_specs, out_specs=out_specs, check_vma=False)
```

```python
import math

import jax
import jax.numpy as jnp
from jax import lax
from jax.experimental import pallas as pl
from jax.experimental.pallas import tpu as pltpu
from jax.sharding import PartitionSpec as P

RADIX = 256
BLOCK = 32768
SUBBANK = 8
STEP_TEMPLATES = 2


PRECISE = lax.Precision.HIGH
EPSILON = 1e-06


def passed_along(value, axis, by):
    count = lax.axis_size(axis)
    pairs = [(i, i + by) for i in range(count) if 0 <= i + by < count]
    return lax.ppermute(value, axis, pairs)


def angle_table(row_count, col_count, period):
    row_index = lax.broadcasted_iota(jnp.int32, (row_count, col_count), 0)
    col_index = lax.broadcasted_iota(jnp.int32, (row_count, col_count), 1)
    phase_step = row_index * col_index % period
    angle_value = phase_step.astype(jnp.float32) * (2.0 * math.pi / period)
    return (jnp.cos(angle_value), jnp.sin(angle_value))


def forward(windows):
    half_radix = RADIX // 2
    window_total = windows.shape[0]
    rows = windows.shape[1] // RADIX
    block_grid = windows.reshape(window_total, rows, RADIX)
    cos_first, sin_first = angle_table(rows, RADIX, RADIX)
    first_table = jnp.concatenate([cos_first, -sin_first], axis=1)
    first_section = jnp.einsum("bnm,nf->bmf", block_grid, first_table, precision=PRECISE)
    cos_twist, sin_twist = angle_table(RADIX, RADIX, RADIX * RADIX)
    real_part = first_section[..., :RADIX]
    imag_part = first_section[..., RADIX:]
    turned = jnp.concatenate(
        [
            real_part * cos_twist + imag_part * sin_twist,
            imag_part * cos_twist - real_part * sin_twist,
        ],
        axis=-1,
    )
    cos_second, sin_second = angle_table(RADIX, half_radix, RADIX)
    cosine_part = jnp.einsum("bnf,nk->bkf", turned, cos_second, precision=PRECISE)
    sine_part = jnp.einsum("bnf,nk->bkf", turned, sin_second, precision=PRECISE)
    return jnp.concatenate(
        [
            cosine_part[..., :RADIX] + sine_part[..., RADIX:],
            cosine_part[..., RADIX:] - sine_part[..., :RADIX],
        ],
        axis=-1,
    )


def split_pair(value):
    high = value.astype(jnp.bfloat16)
    low = (value - high.astype(jnp.float32)).astype(jnp.bfloat16)
    return high, low


def table_pair(value):
    high = lax.reduce_precision(value, exponent_bits=8, mantissa_bits=7)
    return high.astype(jnp.bfloat16), (value - high).astype(jnp.bfloat16)


def triple_dot(left_high, left_low, right_high, right_low):
    total = jnp.dot(left_high, right_high, preferred_element_type=jnp.float32)
    total = total + jnp.dot(left_high, right_low, preferred_element_type=jnp.float32)
    return total + jnp.dot(left_low, right_high, preferred_element_type=jnp.float32)


def inverse_tables(k_rows):
    half_radix = RADIX // 2
    cos_first, sin_first = angle_table(RADIX, k_rows, RADIX)
    first = jnp.concatenate(
        [
            jnp.concatenate([cos_first, -sin_first], axis=1),
            jnp.concatenate([sin_first, cos_first], axis=1),
        ],
        axis=0,
    )
    cos_twist, sin_twist = angle_table(RADIX, RADIX, RADIX * RADIX)
    cos_out, sin_out = angle_table(RADIX, RADIX, RADIX)
    real_cols = jnp.concatenate([cos_out, -sin_out], axis=0)
    imag_cols = jnp.concatenate([sin_out, cos_out], axis=0)
    second = jnp.concatenate([real_cols[:, half_radix:], imag_cols[:, half_radix:]], axis=1)
    first_high, first_low = table_pair(first)
    second_high, second_low = table_pair(second)
    return first_high, first_low, cos_twist, sin_twist, second_high, second_low


def peaks_kernel(spec_ref, bank_ref, fh_ref, fl_ref, tc_ref, ts_ref, sh_ref, sl_ref, out_ref):
    half_radix = RADIX // 2
    block_total = spec_ref.shape[0]
    step_templates = bank_ref.shape[0]
    pair_total = step_templates * block_total
    products = []
    scales = []
    for template in range(step_templates):
        wave_real = bank_ref[template, 0].astype(jnp.float32)
        wave_imag = bank_ref[template, 1].astype(jnp.float32)
        power_sum = jnp.sum(wave_real * wave_real + wave_imag * wave_imag, keepdims=True)
        norm_scale = 1.0 / jnp.sqrt(BLOCK * power_sum + EPSILON)
        scales.append(norm_scale * norm_scale)
        for block in range(block_total):
            spec_real = spec_ref[block, :, :RADIX]
            spec_imag = spec_ref[block, :, RADIX:]
            prod_real = spec_real * wave_real + spec_imag * wave_imag
            prod_imag = spec_imag * wave_real - spec_real * wave_imag
            products.append(jnp.concatenate([prod_real, prod_imag], axis=0))
    stacked = jnp.concatenate(products, axis=1)
    stacked_high, stacked_low = split_pair(stacked)
    first = triple_dot(fh_ref[...], fl_ref[...], stacked_high, stacked_low)
    cos_twist = tc_ref[...]
    sin_twist = ts_ref[...]
    turned_rows = []
    for pair in range(pair_total):
        real_part = first[:RADIX, pair * RADIX : (pair + 1) * RADIX]
        imag_part = first[RADIX:, pair * RADIX : (pair + 1) * RADIX]
        turned_rows.append(
            jnp.concatenate(
                [
                    real_part * cos_twist - imag_part * sin_twist,
                    real_part * sin_twist + imag_part * cos_twist,
                ],
                axis=1,
            )
        )
    turned = jnp.concatenate(turned_rows, axis=0)
    turned_high, turned_low = split_pair(turned)
    series = triple_dot(turned_high, turned_low, sh_ref[...], sl_ref[...])
    power_series = (
        series[:, :half_radix] * series[:, :half_radix]
        + series[:, half_radix:] * series[:, half_radix:]
    )
    peaks = jnp.max(power_series.reshape(pair_total, RADIX, half_radix), axis=1)
    for template in range(step_templates):
        rows = peaks[template * block_total : (template + 1) * block_total]
        out_ref[template] = rows * scales[template]


def window_peaks(spectra, bank, tables):
    block_total, k_rows, _ = spectra.shape
    template_total = bank.shape[0]
    step_templates = STEP_TEMPLATES if template_total % STEP_TEMPLATES == 0 else 1
    fixed = lambda k: (0, 0)
    pair_flops = 6 * (2 * RADIX) * (2 * k_rows) * RADIX + 6 * RADIX * (2 * RADIX) * RADIX
    return pl.pallas_call(
        peaks_kernel,
        out_shape=jax.ShapeDtypeStruct((template_total, block_total, RADIX // 2), jnp.float32),
        grid=(template_total // step_templates,),
        in_specs=[
            pl.BlockSpec((block_total, k_rows, 2 * RADIX), lambda k: (0, 0, 0)),
            pl.BlockSpec((step_templates, 2, k_rows, RADIX), lambda k: (k, 0, 0, 0)),
            pl.BlockSpec((2 * RADIX, 2 * k_rows), fixed),
            pl.BlockSpec((2 * RADIX, 2 * k_rows), fixed),
            pl.BlockSpec((RADIX, RADIX), fixed),
            pl.BlockSpec((RADIX, RADIX), fixed),
            pl.BlockSpec((2 * RADIX, RADIX), fixed),
            pl.BlockSpec((2 * RADIX, RADIX), fixed),
        ],
        out_specs=pl.BlockSpec((step_templates, block_total, RADIX // 2), lambda k: (k, 0, 0)),
        compiler_params=pltpu.CompilerParams(dimension_semantics=("arbitrary",)),
        cost_estimate=pl.CostEstimate(
            flops=pair_flops * template_total * block_total,
            transcendentals=0,
            bytes_accessed=spectra.size * 4 + bank.size * 2 + template_total * block_total * RADIX * 2,
        ),
    )(spectra, bank, *tables)


def gathered_half(template_bank):
    seg_total = lax.axis_size("seg")
    me = lax.axis_index("seg")
    core = me % 2
    template_total, parts, local_bins = template_bank.shape
    half = template_total // 2
    mine = lax.dynamic_slice_in_dim(template_bank, core * half, half, axis=0)
    theirs = lax.dynamic_slice_in_dim(template_bank, (1 - core) * half, half, axis=0)
    arrived = lax.ppermute(theirs[None], "seg", [(i, i ^ 1) for i in range(seg_total)])
    first_arrived = arrived
    upper = core != 0
    held = jnp.stack([jnp.where(upper, arrived, mine[None]), jnp.where(upper, mine[None], arrived)], axis=0)
    odd_order = []
    distance = seg_total // 2
    while distance > 1:
        odd_order.append(distance)
        distance //= 2
    even_order = odd_order[:-2] + odd_order[-2:][::-1]
    for even_distance, odd_distance in zip(even_order, odd_order):
        pairs = [(i, i ^ (even_distance if i % 2 == 0 else odd_distance)) for i in range(seg_total)]
        arrived = lax.ppermute(held, "seg", pairs)
        upper = (me & jnp.where(core == 0, even_distance, odd_distance)) != 0
        held = jnp.stack([jnp.where(upper, arrived, held), jnp.where(upper, held, arrived)], axis=0)
    steps = len(odd_order) + 1
    held = held.reshape((2,) * steps + (half, parts, local_bins // RADIX, RADIX))

    def in_bin_order(order):
        axis_distance = list(reversed([1] + order))
        bit_axes = tuple(sorted(range(steps), key=lambda axis: -axis_distance[axis]))
        return jnp.transpose(held, (steps, steps + 1) + bit_axes + (steps + 2, steps + 3))

    held = jnp.where(core == 0, in_bin_order(even_order), in_bin_order(odd_order))
    return held.reshape(half, parts, seg_total * local_bins // RADIX, RADIX), first_arrived


def local(strain, gate_mask, template_bank):
    seg_total = lax.axis_size("seg")
    core = lax.axis_index("seg") % 2
    bank, first_arrived = gathered_half(template_bank)
    gated = strain * gate_mask.astype(jnp.float32)
    local_blocks = gated.reshape(-1, BLOCK)
    block_total = local_blocks.shape[0]
    last_block, _ = lax.optimization_barrier((local_blocks[block_total - 1], first_arrived))
    earlier = passed_along(last_block, "seg", 1)
    mine = jnp.concatenate([earlier[None], local_blocks], axis=0)
    other = lax.ppermute(mine, "seg", [(i, i ^ 1) for i in range(seg_total)])
    chip_blocks = jnp.where(
        core == 0,
        jnp.concatenate([mine, other[1:]], axis=0),
        jnp.concatenate([other, mine[1:]], axis=0),
    )
    windows = jnp.concatenate([chip_blocks[:-1], chip_blocks[1:]], axis=1)
    spectra = forward(windows)
    tables = inverse_tables(spectra.shape[1])
    partner_spectra = lax.dynamic_slice_in_dim(spectra, (1 - core) * block_total, block_total, axis=0)
    own_spectra = lax.dynamic_slice_in_dim(spectra, core * block_total, block_total, axis=0)
    half = bank.shape[0]
    partner_peaks = window_peaks(partner_spectra, bank, tables)
    returned = lax.ppermute(partner_peaks, "seg", [(i, i ^ 1) for i in range(seg_total)])
    own_peaks = window_peaks(own_spectra, bank, tables)
    peaks = jnp.where(
        core == 0,
        jnp.concatenate([own_peaks, returned], axis=0),
        jnp.concatenate([returned, own_peaks], axis=0),
    )
    return peaks.reshape(2 * half, block_total * (RADIX // 2))


def solution(mesh):
    in_specs = (P(("grp", "seg")), P(("grp", "seg")), P("grp", None, "seg"))
    out_specs = P(None, ("grp", "seg"))
    return jax.shard_map(local, mesh=mesh, in_specs=in_specs, out_specs=out_specs, check_vma=False)
```

```python
import math

import jax
import jax.numpy as jnp
from jax import lax
from jax.experimental import pallas as pl
from jax.experimental.pallas import tpu as pltpu
from jax.sharding import PartitionSpec as P

RADIX = 256
BLOCK = 32768
SUBBANK = 8
STEP_TEMPLATES = 2


PRECISE = lax.Precision.HIGH
EPSILON = 1e-06


def passed_along(value, axis, by):
    count = lax.axis_size(axis)
    pairs = [(i, i + by) for i in range(count) if 0 <= i + by < count]
    return lax.ppermute(value, axis, pairs)


def angle_table(row_count, col_count, period):
    row_index = lax.broadcasted_iota(jnp.int32, (row_count, col_count), 0)
    col_index = lax.broadcasted_iota(jnp.int32, (row_count, col_count), 1)
    phase_step = row_index * col_index % period
    angle_value = phase_step.astype(jnp.float32) * (2.0 * math.pi / period)
    return (jnp.cos(angle_value), jnp.sin(angle_value))


def forward(windows):
    half_radix = RADIX // 2
    window_total = windows.shape[0]
    rows = windows.shape[1] // RADIX
    block_grid = windows.reshape(window_total, rows, RADIX)
    cos_first, sin_first = angle_table(rows, RADIX, RADIX)
    first_table = jnp.concatenate([cos_first, -sin_first], axis=1)
    first_section = jnp.einsum("bnm,nf->bmf", block_grid, first_table, precision=PRECISE)
    cos_twist, sin_twist = angle_table(RADIX, RADIX, RADIX * RADIX)
    real_part = first_section[..., :RADIX]
    imag_part = first_section[..., RADIX:]
    turned = jnp.concatenate(
        [
            real_part * cos_twist + imag_part * sin_twist,
            imag_part * cos_twist - real_part * sin_twist,
        ],
        axis=-1,
    )
    cos_second, sin_second = angle_table(RADIX, half_radix, RADIX)
    cosine_part = jnp.einsum("bnf,nk->bkf", turned, cos_second, precision=PRECISE)
    sine_part = jnp.einsum("bnf,nk->bkf", turned, sin_second, precision=PRECISE)
    return jnp.concatenate(
        [
            cosine_part[..., :RADIX] + sine_part[..., RADIX:],
            cosine_part[..., RADIX:] - sine_part[..., :RADIX],
        ],
        axis=-1,
    )


def split_pair(value):
    high = value.astype(jnp.bfloat16)
    low = (value - high.astype(jnp.float32)).astype(jnp.bfloat16)
    return high, low


def table_pair(value):
    high = lax.reduce_precision(value, exponent_bits=8, mantissa_bits=7)
    return high.astype(jnp.bfloat16), (value - high).astype(jnp.bfloat16)


def triple_dot(left_high, left_low, right_high, right_low):
    total = jnp.dot(left_high, right_high, preferred_element_type=jnp.float32)
    total = total + jnp.dot(left_high, right_low, preferred_element_type=jnp.float32)
    return total + jnp.dot(left_low, right_high, preferred_element_type=jnp.float32)


def inverse_tables(k_rows):
    half_radix = RADIX // 2
    cos_first, sin_first = angle_table(RADIX, k_rows, RADIX)
    first = jnp.concatenate(
        [
            jnp.concatenate([cos_first, -sin_first], axis=1),
            jnp.concatenate([sin_first, cos_first], axis=1),
        ],
        axis=0,
    )
    cos_twist, sin_twist = angle_table(RADIX, RADIX, RADIX * RADIX)
    cos_out, sin_out = angle_table(RADIX, RADIX, RADIX)
    real_cols = jnp.concatenate([cos_out, -sin_out], axis=0)
    imag_cols = jnp.concatenate([sin_out, cos_out], axis=0)
    second = jnp.concatenate([real_cols[:, half_radix:], imag_cols[:, half_radix:]], axis=1)
    first_high, first_low = table_pair(first)
    second_high, second_low = table_pair(second)
    return first_high, first_low, cos_twist, sin_twist, second_high, second_low


def peaks_kernel(spec_ref, bank_ref, fh_ref, fl_ref, tc_ref, ts_ref, sh_ref, sl_ref, out_ref):
    half_radix = RADIX // 2
    block_total = spec_ref.shape[0]
    step_templates = bank_ref.shape[0]
    pair_total = step_templates * block_total
    products = []
    scales = []
    for template in range(step_templates):
        wave_real = bank_ref[template, 0].astype(jnp.float32)
        wave_imag = bank_ref[template, 1].astype(jnp.float32)
        power_sum = jnp.sum(wave_real * wave_real + wave_imag * wave_imag, keepdims=True)
        norm_scale = 1.0 / jnp.sqrt(BLOCK * power_sum + EPSILON)
        scales.append(norm_scale * norm_scale)
        for block in range(block_total):
            spec_real = spec_ref[block, :, :RADIX]
            spec_imag = spec_ref[block, :, RADIX:]
            prod_real = spec_real * wave_real + spec_imag * wave_imag
            prod_imag = spec_imag * wave_real - spec_real * wave_imag
            products.append(jnp.concatenate([prod_real, prod_imag], axis=0))
    stacked = jnp.concatenate(products, axis=1)
    stacked_high, stacked_low = split_pair(stacked)
    first = triple_dot(fh_ref[...], fl_ref[...], stacked_high, stacked_low)
    cos_twist = tc_ref[...]
    sin_twist = ts_ref[...]
    turned_rows = []
    for pair in range(pair_total):
        real_part = first[:RADIX, pair * RADIX : (pair + 1) * RADIX]
        imag_part = first[RADIX:, pair * RADIX : (pair + 1) * RADIX]
        turned_rows.append(
            jnp.concatenate(
                [
                    real_part * cos_twist - imag_part * sin_twist,
                    real_part * sin_twist + imag_part * cos_twist,
                ],
                axis=1,
            )
        )
    turned = jnp.concatenate(turned_rows, axis=0)
    turned_high, turned_low = split_pair(turned)
    series = triple_dot(turned_high, turned_low, sh_ref[...], sl_ref[...])
    power_series = (
        series[:, :half_radix] * series[:, :half_radix]
        + series[:, half_radix:] * series[:, half_radix:]
    )
    peaks = jnp.max(power_series.reshape(pair_total, RADIX, half_radix), axis=1)
    for template in range(step_templates):
        rows = peaks[template * block_total : (template + 1) * block_total]
        out_ref[template] = rows * scales[template]


def window_peaks(spectra, bank, tables):
    block_total, k_rows, _ = spectra.shape
    template_total = bank.shape[0]
    step_templates = STEP_TEMPLATES if template_total % STEP_TEMPLATES == 0 else 1
    fixed = lambda k: (0, 0)
    pair_flops = 6 * (2 * RADIX) * (2 * k_rows) * RADIX + 6 * RADIX * (2 * RADIX) * RADIX
    return pl.pallas_call(
        peaks_kernel,
        out_shape=jax.ShapeDtypeStruct((template_total, block_total, RADIX // 2), jnp.float32),
        grid=(template_total // step_templates,),
        in_specs=[
            pl.BlockSpec((block_total, k_rows, 2 * RADIX), lambda k: (0, 0, 0)),
            pl.BlockSpec((step_templates, 2, k_rows, RADIX), lambda k: (k, 0, 0, 0)),
            pl.BlockSpec((2 * RADIX, 2 * k_rows), fixed),
            pl.BlockSpec((2 * RADIX, 2 * k_rows), fixed),
            pl.BlockSpec((RADIX, RADIX), fixed),
            pl.BlockSpec((RADIX, RADIX), fixed),
            pl.BlockSpec((2 * RADIX, RADIX), fixed),
            pl.BlockSpec((2 * RADIX, RADIX), fixed),
        ],
        out_specs=pl.BlockSpec((step_templates, block_total, RADIX // 2), lambda k: (k, 0, 0)),
        compiler_params=pltpu.CompilerParams(dimension_semantics=("arbitrary",)),
        cost_estimate=pl.CostEstimate(
            flops=pair_flops * template_total * block_total,
            transcendentals=0,
            bytes_accessed=spectra.size * 4 + bank.size * 2 + template_total * block_total * RADIX * 2,
        ),
    )(spectra, bank, *tables)


def gathered_half(template_bank):
    seg_total = lax.axis_size("seg")
    me = lax.axis_index("seg")
    core = me % 2
    template_total, parts, local_bins = template_bank.shape
    half = template_total // 2
    mine = lax.dynamic_slice_in_dim(template_bank, core * half, half, axis=0)
    theirs = lax.dynamic_slice_in_dim(template_bank, (1 - core) * half, half, axis=0)
    arrived = lax.ppermute(theirs[None], "seg", [(i, i ^ 1) for i in range(seg_total)])
    first_arrived = arrived
    upper = core != 0
    held = jnp.stack([jnp.where(upper, arrived, mine[None]), jnp.where(upper, mine[None], arrived)], axis=0)
    odd_order = []
    distance = seg_total // 2
    while distance > 1:
        odd_order.append(distance)
        distance //= 2
    even_order = odd_order[:-2] + odd_order[-2:][::-1]
    for even_distance, odd_distance in zip(even_order, odd_order):
        pairs = [(i, i ^ (even_distance if i % 2 == 0 else odd_distance)) for i in range(seg_total)]
        arrived = lax.ppermute(held, "seg", pairs)
        if even_distance == odd_distance:
            first_arrived = arrived
        upper = (me & jnp.where(core == 0, even_distance, odd_distance)) != 0
        held = jnp.stack([jnp.where(upper, arrived, held), jnp.where(upper, held, arrived)], axis=0)
    steps = len(odd_order) + 1
    held = held.reshape((2,) * steps + (half, parts, local_bins // RADIX, RADIX))

    def in_bin_order(order):
        axis_distance = list(reversed([1] + order))
        bit_axes = tuple(sorted(range(steps), key=lambda axis: -axis_distance[axis]))
        return jnp.transpose(held, (steps, steps + 1) + bit_axes + (steps + 2, steps + 3))

    held = jnp.where(core == 0, in_bin_order(even_order), in_bin_order(odd_order))
    return held.reshape(half, parts, seg_total * local_bins // RADIX, RADIX), first_arrived


def local(strain, gate_mask, template_bank):
    seg_total = lax.axis_size("seg")
    core = lax.axis_index("seg") % 2
    bank, first_arrived = gathered_half(template_bank)
    gated = strain * gate_mask.astype(jnp.float32)
    local_blocks = gated.reshape(-1, BLOCK)
    block_total = local_blocks.shape[0]
    last_block, _ = lax.optimization_barrier((local_blocks[block_total - 1], first_arrived))
    earlier = passed_along(last_block, "seg", 1)
    mine = jnp.concatenate([earlier[None], local_blocks], axis=0)
    other = lax.ppermute(mine, "seg", [(i, i ^ 1) for i in range(seg_total)])
    chip_blocks = jnp.where(
        core == 0,
        jnp.concatenate([mine, other[1:]], axis=0),
        jnp.concatenate([other, mine[1:]], axis=0),
    )
    windows = jnp.concatenate([chip_blocks[:-1], chip_blocks[1:]], axis=1)
    spectra = forward(windows)
    tables = inverse_tables(spectra.shape[1])
    partner_spectra = lax.dynamic_slice_in_dim(spectra, (1 - core) * block_total, block_total, axis=0)
    own_spectra = lax.dynamic_slice_in_dim(spectra, core * block_total, block_total, axis=0)
    half = bank.shape[0]
    partner_peaks = window_peaks(partner_spectra, bank, tables)
    returned = lax.ppermute(partner_peaks, "seg", [(i, i ^ 1) for i in range(seg_total)])
    own_peaks = window_peaks(own_spectra, bank, tables)
    peaks = jnp.where(
        core == 0,
        jnp.concatenate([own_peaks, returned], axis=0),
        jnp.concatenate([returned, own_peaks], axis=0),
    )
    return peaks.reshape(2 * half, block_total * (RADIX // 2))


def solution(mesh):
    in_specs = (P(("grp", "seg")), P(("grp", "seg")), P("grp", None, "seg"))
    out_specs = P(None, ("grp", "seg"))
    return jax.shard_map(local, mesh=mesh, in_specs=in_specs, out_specs=out_specs, check_vma=False)
```

```python
import math

import jax
import jax.numpy as jnp
from jax import lax
from jax.experimental import pallas as pl
from jax.experimental.pallas import tpu as pltpu
from jax.sharding import PartitionSpec as P

RADIX = 256
BLOCK = 32768
SUBBANK = 8
STEP_TEMPLATES = 4


PRECISE = lax.Precision.HIGH
EPSILON = 1e-06


def passed_along(value, axis, by):
    count = lax.axis_size(axis)
    pairs = [(i, i + by) for i in range(count) if 0 <= i + by < count]
    return lax.ppermute(value, axis, pairs)


def angle_table(row_count, col_count, period):
    row_index = lax.broadcasted_iota(jnp.int32, (row_count, col_count), 0)
    col_index = lax.broadcasted_iota(jnp.int32, (row_count, col_count), 1)
    phase_step = row_index * col_index % period
    angle_value = phase_step.astype(jnp.float32) * (2.0 * math.pi / period)
    return (jnp.cos(angle_value), jnp.sin(angle_value))


def forward(windows):
    half_radix = RADIX // 2
    window_total = windows.shape[0]
    rows = windows.shape[1] // RADIX
    block_grid = windows.reshape(window_total, rows, RADIX)
    cos_first, sin_first = angle_table(rows, RADIX, RADIX)
    first_table = jnp.concatenate([cos_first, -sin_first], axis=1)
    first_section = jnp.einsum("bnm,nf->bmf", block_grid, first_table, precision=PRECISE)
    cos_twist, sin_twist = angle_table(RADIX, RADIX, RADIX * RADIX)
    real_part = first_section[..., :RADIX]
    imag_part = first_section[..., RADIX:]
    turned = jnp.concatenate(
        [
            real_part * cos_twist + imag_part * sin_twist,
            imag_part * cos_twist - real_part * sin_twist,
        ],
        axis=-1,
    )
    cos_second, sin_second = angle_table(RADIX, half_radix, RADIX)
    cosine_part = jnp.einsum("bnf,nk->bkf", turned, cos_second, precision=PRECISE)
    sine_part = jnp.einsum("bnf,nk->bkf", turned, sin_second, precision=PRECISE)
    return jnp.concatenate(
        [
            cosine_part[..., :RADIX] + sine_part[..., RADIX:],
            cosine_part[..., RADIX:] - sine_part[..., :RADIX],
        ],
        axis=-1,
    )


def split_pair(value):
    high = value.astype(jnp.bfloat16)
    low = (value - high.astype(jnp.float32)).astype(jnp.bfloat16)
    return high, low


def table_pair(value):
    high = lax.reduce_precision(value, exponent_bits=8, mantissa_bits=7)
    return high.astype(jnp.bfloat16), (value - high).astype(jnp.bfloat16)


def triple_dot(left_high, left_low, right_high, right_low):
    total = jnp.dot(left_high, right_high, preferred_element_type=jnp.float32)
    total = total + jnp.dot(left_high, right_low, preferred_element_type=jnp.float32)
    return total + jnp.dot(left_low, right_high, preferred_element_type=jnp.float32)


def inverse_tables(k_rows):
    half_radix = RADIX // 2
    cos_first, sin_first = angle_table(RADIX, k_rows, RADIX)
    first = jnp.concatenate(
        [
            jnp.concatenate([cos_first, -sin_first], axis=1),
            jnp.concatenate([sin_first, cos_first], axis=1),
        ],
        axis=0,
    )
    cos_twist, sin_twist = angle_table(RADIX, RADIX, RADIX * RADIX)
    cos_out, sin_out = angle_table(RADIX, RADIX, RADIX)
    real_cols = jnp.concatenate([cos_out, -sin_out], axis=0)
    imag_cols = jnp.concatenate([sin_out, cos_out], axis=0)
    second = jnp.concatenate([real_cols[:, half_radix:], imag_cols[:, half_radix:]], axis=1)
    first_high, first_low = table_pair(first)
    second_high, second_low = table_pair(second)
    return first_high, first_low, cos_twist, sin_twist, second_high, second_low


def peaks_kernel(spec_ref, bank_ref, fh_ref, fl_ref, tc_ref, ts_ref, sh_ref, sl_ref, out_ref):
    half_radix = RADIX // 2
    block_total = spec_ref.shape[0]
    step_templates = bank_ref.shape[0]
    pair_total = step_templates * block_total
    products = []
    scales = []
    for template in range(step_templates):
        wave_real = bank_ref[template, 0].astype(jnp.float32)
        wave_imag = bank_ref[template, 1].astype(jnp.float32)
        power_sum = jnp.sum(wave_real * wave_real + wave_imag * wave_imag, keepdims=True)
        norm_scale = 1.0 / jnp.sqrt(BLOCK * power_sum + EPSILON)
        scales.append(norm_scale * norm_scale)
        for block in range(block_total):
            spec_real = spec_ref[block, :, :RADIX]
            spec_imag = spec_ref[block, :, RADIX:]
            prod_real = spec_real * wave_real + spec_imag * wave_imag
            prod_imag = spec_imag * wave_real - spec_real * wave_imag
            products.append(jnp.concatenate([prod_real, prod_imag], axis=0))
    stacked = jnp.concatenate(products, axis=1)
    stacked_high, stacked_low = split_pair(stacked)
    first = triple_dot(fh_ref[...], fl_ref[...], stacked_high, stacked_low)
    cos_twist = tc_ref[...]
    sin_twist = ts_ref[...]
    turned_rows = []
    for pair in range(pair_total):
        real_part = first[:RADIX, pair * RADIX : (pair + 1) * RADIX]
        imag_part = first[RADIX:, pair * RADIX : (pair + 1) * RADIX]
        turned_rows.append(
            jnp.concatenate(
                [
                    real_part * cos_twist - imag_part * sin_twist,
                    real_part * sin_twist + imag_part * cos_twist,
                ],
                axis=1,
            )
        )
    turned = jnp.concatenate(turned_rows, axis=0)
    turned_high, turned_low = split_pair(turned)
    series = triple_dot(turned_high, turned_low, sh_ref[...], sl_ref[...])
    power_series = (
        series[:, :half_radix] * series[:, :half_radix]
        + series[:, half_radix:] * series[:, half_radix:]
    )
    peaks = jnp.max(power_series.reshape(pair_total, RADIX, half_radix), axis=1)
    for template in range(step_templates):
        rows = peaks[template * block_total : (template + 1) * block_total]
        out_ref[template] = rows * scales[template]


def window_peaks(spectra, bank, tables):
    block_total, k_rows, _ = spectra.shape
    template_total = bank.shape[0]
    step_templates = STEP_TEMPLATES if template_total % STEP_TEMPLATES == 0 else 1
    fixed = lambda k: (0, 0)
    pair_flops = 6 * (2 * RADIX) * (2 * k_rows) * RADIX + 6 * RADIX * (2 * RADIX) * RADIX
    return pl.pallas_call(
        peaks_kernel,
        out_shape=jax.ShapeDtypeStruct((template_total, block_total, RADIX // 2), jnp.float32),
        grid=(template_total // step_templates,),
        in_specs=[
            pl.BlockSpec((block_total, k_rows, 2 * RADIX), lambda k: (0, 0, 0)),
            pl.BlockSpec((step_templates, 2, k_rows, RADIX), lambda k: (k, 0, 0, 0)),
            pl.BlockSpec((2 * RADIX, 2 * k_rows), fixed),
            pl.BlockSpec((2 * RADIX, 2 * k_rows), fixed),
            pl.BlockSpec((RADIX, RADIX), fixed),
            pl.BlockSpec((RADIX, RADIX), fixed),
            pl.BlockSpec((2 * RADIX, RADIX), fixed),
            pl.BlockSpec((2 * RADIX, RADIX), fixed),
        ],
        out_specs=pl.BlockSpec((step_templates, block_total, RADIX // 2), lambda k: (k, 0, 0)),
        compiler_params=pltpu.CompilerParams(dimension_semantics=("arbitrary",)),
        cost_estimate=pl.CostEstimate(
            flops=pair_flops * template_total * block_total,
            transcendentals=0,
            bytes_accessed=spectra.size * 4 + bank.size * 2 + template_total * block_total * RADIX * 2,
        ),
    )(spectra, bank, *tables)


def gathered_half(template_bank):
    seg_total = lax.axis_size("seg")
    me = lax.axis_index("seg")
    core = me % 2
    template_total, parts, local_bins = template_bank.shape
    half = template_total // 2
    mine = lax.dynamic_slice_in_dim(template_bank, core * half, half, axis=0)
    theirs = lax.dynamic_slice_in_dim(template_bank, (1 - core) * half, half, axis=0)
    arrived = lax.ppermute(theirs[None], "seg", [(i, i ^ 1) for i in range(seg_total)])
    first_arrived = arrived
    upper = core != 0
    held = jnp.stack([jnp.where(upper, arrived, mine[None]), jnp.where(upper, mine[None], arrived)], axis=0)
    odd_order = []
    distance = seg_total // 2
    while distance > 1:
        odd_order.append(distance)
        distance //= 2
    even_order = odd_order[:-2] + odd_order[-2:][::-1]
    for even_distance, odd_distance in zip(even_order, odd_order):
        pairs = [(i, i ^ (even_distance if i % 2 == 0 else odd_distance)) for i in range(seg_total)]
        arrived = lax.ppermute(held, "seg", pairs)
        upper = (me & jnp.where(core == 0, even_distance, odd_distance)) != 0
        held = jnp.stack([jnp.where(upper, arrived, held), jnp.where(upper, held, arrived)], axis=0)
    steps = len(odd_order) + 1
    held = held.reshape((2,) * steps + (half, parts, local_bins // RADIX, RADIX))

    def in_bin_order(order):
        axis_distance = list(reversed([1] + order))
        bit_axes = tuple(sorted(range(steps), key=lambda axis: -axis_distance[axis]))
        return jnp.transpose(held, (steps, steps + 1) + bit_axes + (steps + 2, steps + 3))

    held = jnp.where(core == 0, in_bin_order(even_order), in_bin_order(odd_order))
    return held.reshape(half, parts, seg_total * local_bins // RADIX, RADIX), first_arrived


def local(strain, gate_mask, template_bank):
    seg_total = lax.axis_size("seg")
    core = lax.axis_index("seg") % 2
    bank, first_arrived = gathered_half(template_bank)
    gated = strain * gate_mask.astype(jnp.float32)
    local_blocks = gated.reshape(-1, BLOCK)
    block_total = local_blocks.shape[0]
    last_block, _ = lax.optimization_barrier((local_blocks[block_total - 1], first_arrived))
    earlier = passed_along(last_block, "seg", 1)
    mine = jnp.concatenate([earlier[None], local_blocks], axis=0)
    other = lax.ppermute(mine, "seg", [(i, i ^ 1) for i in range(seg_total)])
    chip_blocks = jnp.where(
        core == 0,
        jnp.concatenate([mine, other[1:]], axis=0),
        jnp.concatenate([other, mine[1:]], axis=0),
    )
    windows = jnp.concatenate([chip_blocks[:-1], chip_blocks[1:]], axis=1)
    spectra = forward(windows)
    tables = inverse_tables(spectra.shape[1])
    partner_spectra = lax.dynamic_slice_in_dim(spectra, (1 - core) * block_total, block_total, axis=0)
    own_spectra = lax.dynamic_slice_in_dim(spectra, core * block_total, block_total, axis=0)
    half = bank.shape[0]
    partner_peaks = window_peaks(partner_spectra, bank, tables)
    returned = lax.ppermute(partner_peaks, "seg", [(i, i ^ 1) for i in range(seg_total)])
    own_peaks = window_peaks(own_spectra, bank, tables)
    peaks = jnp.where(
        core == 0,
        jnp.concatenate([own_peaks, returned], axis=0),
        jnp.concatenate([returned, own_peaks], axis=0),
    )
    return peaks.reshape(2 * half, block_total * (RADIX // 2))


def solution(mesh):
    in_specs = (P(("grp", "seg")), P(("grp", "seg")), P("grp", None, "seg"))
    out_specs = P(None, ("grp", "seg"))
    return jax.shard_map(local, mesh=mesh, in_specs=in_specs, out_specs=out_specs, check_vma=False)
```
